128 devices in a mesh: gy: 8 (over x, y_hi), gz: 16 (over z, y_lo, core).
Axes of the slice: x: 4, y: 4 (y_hi: 2, y_lo: 2; y = y_hi * 2 + y_lo), z: 4, core: 2. Of those that a mesh axis runs over, the one named last changes fastest.
Arguments:
- fixed_features: bfloat16 [1024, 131072], P('gy', 'gz'), may hold values from -14 to 14
- moving_features: bfloat16 [1024, 131072], P('gy', 'gz'), may hold values from -14 to 14
- cand_offsets: int32 [256, 16, 16], P('gy', 'gz'), may hold values from -32 to 32, as said below
- cand_lengths: int32 [256, 16], P('gy', 'gz'), may hold values from 6 to 16, as said below
- smooth_radii: int32 [3], replicated, may hold values from 1 to 4, as said below
Outputs:
- disp_init: float32 [1024, 8192], P('gy', 'gz')
- disp_final: float32 [1024, 8192], P('gy', 'gz')
The draws below stay inside these ranges and needn't reach their ends.
Inputs may be any that keep to these rules, and one draw needn't show every extreme that they name: Each offset is a multiple of 4 and moves its block inside the grid: 0 <= 4 b + cand_offsets[b, s, k] <= 1020 for every slot. `cand_lengths`: some list is full in every draw. `smooth_radii`: the radii of the iterations differ from one another; 1 and 4 both occur in every draw.
All inputs are finite; a program needn't handle non-finite values.
Results may differ from the reference program's by a relative error of at most 0.0003.
Values may be sent and summed in bfloat16 or wider, within the bound.
No kernel may reach another device: no remote copies, remote signals or barrier semaphores. Data moves between devices by JAX's collectives and lax.ppermute only.
A program may use at most 128 MiB of HBM per device.

```python
import jax
import jax.numpy as jnp
from jax import lax

CH = 16
XS = 8
CY = 128
CZ = 64
MAXC = 16
REACH = 32
RMAX = 4
ITERS = 3
Y = 1024
Z = 1024


def draw_features(key, salt_value):
    array_shape = (Y, Z * XS * CH)
    values = jnp.clip(jax.random.normal(jax.random.fold_in(key, salt_value), array_shape, jnp.float32), -4.0, 4.0)
    return values.astype(jnp.bfloat16)


def draw_fixed_features(key, part):
    return draw_features(key, 1)


def draw_moving_features(key, part):
    return draw_features(key, 2)


def draw_cand_offsets(key, part):
    blocks = Y // 4
    zshards = Z // CZ
    steps = 4 * jax.random.randint(jax.random.fold_in(key, 21), (blocks, zshards, MAXC), -(REACH // 4), REACH // 4 + 1)
    base_rows = 4 * jnp.arange(blocks, dtype=jnp.int32)
    targets = jnp.clip(base_rows[:, None, None] + steps, 0, Y - 4)
    upper = jnp.minimum(base_rows + REACH, Y - 4)
    lower = jnp.maximum(base_rows - REACH, 0)
    targets = targets.at[:, :, 0].set(jnp.broadcast_to(upper[:, None], (blocks, zshards)))
    targets = targets.at[:, :, 1].set(jnp.broadcast_to(lower[:, None], (blocks, zshards)))
    return (targets - base_rows[:, None, None]).astype(jnp.int32)


def draw_cand_lengths(key, part):
    groups_y = Y // CY
    zshards = Z // CZ
    per_group = CY // 4
    least = max(2, 3 * MAXC // 8)
    heavy_mask = jax.random.randint(jax.random.fold_in(key, 11), (groups_y, zshards), 0, 4) == 0
    forced = jax.random.randint(jax.random.fold_in(key, 12), (), 0, groups_y * zshards)
    heavy_mask = heavy_mask | (jnp.arange(groups_y * zshards).reshape(groups_y, zshards) == forced)
    heavy_rows = jnp.repeat(heavy_mask, per_group, axis=0)
    list_shape = (Y // 4, zshards)
    heavy_len = jax.random.randint(jax.random.fold_in(key, 13), list_shape, 3 * MAXC // 4, MAXC + 1)
    light_len = jax.random.randint(jax.random.fold_in(key, 14), list_shape, least, max(least, 3 * MAXC // 4) + 1)
    length_draw = jnp.where(heavy_rows, heavy_len, light_len)
    row_index = forced // zshards * per_group
    col_index = forced % zshards
    length_draw = length_draw.at[row_index, col_index].set(MAXC)
    return length_draw.astype(jnp.int32)


def draw_smooth_radii(key, part):
    middle_pool = jax.random.permutation(jax.random.fold_in(key, 32), jnp.arange(2, RMAX, dtype=jnp.int32))
    chosen = jnp.concatenate([jnp.array([1, RMAX], dtype=jnp.int32), middle_pool[:ITERS - 2].astype(jnp.int32)])
    order = jax.random.permutation(jax.random.fold_in(key, 33), jnp.arange(ITERS, dtype=jnp.int32))
    return chosen[order].astype(jnp.int32)


def setup_inputs(seed: int = 0) -> dict:
    arg_keys = jax.random.split(jax.random.key(seed), 6)
    fixed_features = draw_fixed_features(jax.random.fold_in(arg_keys[5], 71), 0)
    moving_features = draw_moving_features(jax.random.fold_in(arg_keys[5], 71), 0)
    cand_offsets = draw_cand_offsets(jax.random.fold_in(arg_keys[5], 71), 0)
    cand_lengths = draw_cand_lengths(jax.random.fold_in(arg_keys[5], 71), 0)
    smooth_radii = draw_smooth_radii(jax.random.fold_in(arg_keys[5], 71), 0)
    return dict(fixed_features=fixed_features, moving_features=moving_features, cand_offsets=cand_offsets, cand_lengths=cand_lengths, smooth_radii=smooth_radii)


softmin_temp = 2.0
smooth_weight = 2.0
adam_rate = 0.2
beta_first = 0.9
beta_second = 0.999
adam_floor = 0.05

def box_weights(radius):
    spread = jnp.arange(-RMAX, RMAX + 1).astype(jnp.int32)
    inside = jnp.abs(spread) <= radius
    return jnp.where(inside, 1.0, 0.0).astype(jnp.float32) / (2 * radius + 1).astype(jnp.float32)

def smooth_inner(padded, radius, margin):
    weights = box_weights(radius)
    height = padded.shape[0] - 2 * margin
    layers = padded.shape[1] - 2 * margin
    depth_cells = padded.shape[2]
    along_y = jnp.zeros((height, padded.shape[1], depth_cells), jnp.float32)
    for offset in range(-RMAX, RMAX + 1):
        along_y = along_y + weights[RMAX + offset] * padded[margin + offset:margin + offset + height]
    along_z = jnp.zeros((height, layers, depth_cells), jnp.float32)
    for offset in range(-RMAX, RMAX + 1):
        along_z = along_z + weights[RMAX + offset] * along_y[:, margin + offset:margin + offset + layers]
    x_padded = jnp.pad(along_z, ((0, 0), (0, 0), (RMAX, RMAX)))
    along_x = jnp.zeros((height, layers, depth_cells), jnp.float32)
    for offset in range(-RMAX, RMAX + 1):
        along_x = along_x + weights[RMAX + offset] * x_padded[:, :, RMAX + offset:RMAX + offset + depth_cells]
    return along_x

def adam_update(field, target_field, smoothed, first_moment, second_moment, iteration):
    gradient = field - target_field + smooth_weight * (field - smoothed)
    first_moment = beta_first * first_moment + (1.0 - beta_first) * gradient
    second_moment = beta_second * second_moment + (1.0 - beta_second) * gradient * gradient
    first_hat = first_moment / (1.0 - beta_first ** (iteration + 1))
    second_hat = second_moment / (1.0 - beta_second ** (iteration + 1))
    field = field - adam_rate * first_hat / (jnp.sqrt(second_hat) + adam_floor)
    return (field, first_moment, second_moment)

def reference(fixed_features, moving_features, cand_offsets, cand_lengths, smooth_radii):
    total_y = fixed_features.shape[0]
    blocks = total_y // 4
    shards = cand_offsets.shape[1]
    columns = fixed_features.shape[1] // CH
    per_shard = columns // shards
    fixed_split = fixed_features.reshape(total_y, shards, per_shard, CH)
    moving_split = moving_features.reshape(total_y, shards, per_shard, CH)
    quad_rows = jnp.arange(4).astype(jnp.int32)
    shard_ids = jnp.arange(shards).astype(jnp.int32)
    slot_ids = jnp.arange(MAXC).astype(jnp.int32)

    def per_block(block_index):
        base_row = (4 * block_index).astype(jnp.int32)
        fixed_rows = lax.dynamic_slice_in_dim(fixed_split, base_row, 4, 0).astype(jnp.float32)
        shifts = lax.dynamic_index_in_dim(cand_offsets, block_index, 0, keepdims=False)
        counts = lax.dynamic_index_in_dim(cand_lengths, block_index, 0, keepdims=False)
        targets = (base_row + shifts).astype(jnp.int32)
        row_ids = targets[:, :, None] + quad_rows
        moved_rows = moving_split[row_ids, shard_ids[:, None, None]].astype(jnp.float32)
        differences = jnp.transpose(fixed_rows, (1, 0, 2, 3))[:, None] - moved_rows
        cost_sum = lax.optimization_barrier(jnp.sum(differences * differences, axis=-1))
        scores = -cost_sum / softmin_temp
        valid_mask = (slot_ids[None, :] < counts[:, None])[:, :, None, None]
        scores = jnp.where(valid_mask, scores, -jnp.inf)
        peak_score = lax.optimization_barrier(jnp.max(scores, axis=1, keepdims=True))
        weights = jnp.where(valid_mask, jnp.exp(scores - peak_score), 0.0)
        shift_norm = (2.0 * shifts.astype(jnp.float32) / total_y)[:, :, None, None]
        field = lax.optimization_barrier(jnp.sum(weights * shift_norm, axis=1)) / lax.optimization_barrier(jnp.sum(weights, axis=1))
        return jnp.transpose(field, (1, 0, 2))
    fields = lax.map(per_block, jnp.arange(blocks).astype(jnp.int32))
    disp_init = fields.reshape(total_y, shards * per_shard)
    target_field = disp_init.reshape(total_y, -1, XS)
    field = target_field
    first_moment = jnp.zeros_like(target_field)
    second_moment = jnp.zeros_like(target_field)
    for iteration in range(ITERS):
        padded = jnp.pad(field, ((RMAX, RMAX), (RMAX, RMAX), (0, 0)))
        smoothed = smooth_inner(padded, smooth_radii[iteration], RMAX)
        field, first_moment, second_moment = adam_update(field, target_field, smoothed, first_moment, second_moment, iteration)
    return (disp_init, field.reshape(total_y, -1))
```

```python
import jax
import jax.numpy as jnp
from jax import lax
from jax.experimental import pallas as pl
from jax.experimental.pallas import tpu as pltpu
from jax.sharding import PartitionSpec as P

CH = 16
XS = 8
REACH = 32
RMAX = 4
ITERS = 3
NOFF = 2 * (REACH // 4) + 1


softmin_temp = 2.0
smooth_weight = 2.0
adam_rate = 0.2
beta_first = 0.9
beta_second = 0.999
adam_floor = 0.05


def with_halo(cells, sides, width):
    for axis, dim in sides:
        count = lax.axis_size(axis)
        ends = count - 1
        head = lax.slice_in_dim(cells, 0, width, axis=dim)
        tail = lax.slice_in_dim(cells, cells.shape[dim] - width, cells.shape[dim], axis=dim)
        cells = jnp.concatenate(
            [
                lax.ppermute(tail, axis, [(i, (i + 1) % count) for i in range(ends)]),
                cells,
                lax.ppermute(head, axis, [((i + 1) % count, i) for i in range(ends)]),
            ],
            axis=dim,
        )
    return cells


def box_weights(radius):
    spread = jnp.arange(-RMAX, RMAX + 1)
    inside = jnp.abs(spread) <= radius
    return jnp.where(inside, 1.0, 0.0).astype(jnp.float32) / (2 * radius + 1).astype(jnp.float32)


def smooth_inner(padded, radius, margin):
    weights = box_weights(radius)
    height = padded.shape[0] - 2 * margin
    layers = padded.shape[1] - 2 * margin
    depth_cells = padded.shape[2]
    along_y = jnp.zeros((height, padded.shape[1], depth_cells), jnp.float32)
    for offset in range(-RMAX, RMAX + 1):
        along_y = (
            along_y + weights[RMAX + offset] * padded[margin + offset : margin + offset + height]
        )
    along_z = jnp.zeros((height, layers, depth_cells), jnp.float32)
    for offset in range(-RMAX, RMAX + 1):
        along_z = (
            along_z
            + weights[RMAX + offset] * along_y[:, margin + offset : margin + offset + layers]
        )
    x_padded = jnp.pad(along_z, ((0, 0), (0, 0), (RMAX, RMAX)))
    along_x = jnp.zeros((height, layers, depth_cells), jnp.float32)
    for offset in range(-RMAX, RMAX + 1):
        along_x = (
            along_x
            + weights[RMAX + offset] * x_padded[:, :, RMAX + offset : RMAX + offset + depth_cells]
        )
    return along_x


def adam_update(field, target_field, smoothed, first_moment, second_moment, iteration):
    gradient = field - target_field + smooth_weight * (field - smoothed)
    first_moment = beta_first * first_moment + (1.0 - beta_first) * gradient
    second_moment = beta_second * second_moment + (1.0 - beta_second) * gradient * gradient
    first_hat = first_moment / (1.0 - beta_first ** (iteration + 1))
    second_hat = second_moment / (1.0 - beta_second ** (iteration + 1))
    field = field - adam_rate * first_hat / (jnp.sqrt(second_hat) + adam_floor)
    return (field, first_moment, second_moment)


def softmin_kernel(total_y, f_ref, m0_ref, m4_ref, n_ref, o_ref):
    height = f_ref.shape[1]
    lanes_total = f_ref.shape[2]

    def body(t, carry):
        r0 = pl.multiple_of(t * 8, 8)
        for j in range(lanes_total // 128):
            lanes = pl.ds(128 * j, 128)
            fixed = [f_ref[c, pl.ds(r0, 8), lanes] for c in range(CH)]
            scores = []
            counts = []
            for o in range(NOFF):
                shift = 4 * o
                if shift % 8 == 0:
                    src, base = m0_ref, shift
                else:
                    src, base = m4_ref, shift - 4
                acc = None
                for c in range(CH):
                    d = fixed[c] - src[c, pl.ds(r0 + base, 8), lanes]
                    acc = d * d if acc is None else acc + d * d
                n_o = n_ref[o, pl.ds(r0, 8), :]
                counts.append(n_o)
                scores.append(jnp.where(n_o > 0.0, -acc / softmin_temp, -jnp.inf))
            peak = scores[0]
            for s in scores[1:]:
                peak = jnp.maximum(peak, s)
            den = None
            num = None
            for o in range(NOFF):
                w = counts[o] * jnp.exp(scores[o] - peak)
                shift_norm = 2.0 * float(4 * o - REACH) / total_y
                den = w if den is None else den + w
                num = w * shift_norm if num is None else num + w * shift_norm
            o_ref[pl.ds(r0, 8), lanes] = num / den
        return carry

    lax.fori_loop(0, height // 8, body, 0)


def per_device(fixed_features, moving_features, cand_offsets, cand_lengths, smooth_radii):
    height = fixed_features.shape[0]
    columns_dev = fixed_features.shape[1] // CH
    blocks = height // 4
    total_y = height * lax.axis_size("gy")
    shifts = cand_offsets[:, 0, :]
    counts = cand_lengths[:, 0]
    live = jnp.arange(shifts.shape[1], dtype=jnp.int32)[None, :] < counts[:, None]
    offset_values = 4 * jnp.arange(NOFF, dtype=jnp.int32) - REACH
    hits = (shifts[:, :, None] == offset_values[None, None, :]) & live[:, :, None]
    mult = jnp.sum(hits.astype(jnp.float32), axis=1)
    mult_rows = jnp.repeat(mult.T, 4, axis=1)
    mult_rows = jnp.broadcast_to(mult_rows[:, :, None], (NOFF, height, 128))

    fixed_t = fixed_features.reshape(height, columns_dev, CH).transpose(2, 0, 1)
    moving_t = moving_features.reshape(height, columns_dev, CH).transpose(2, 0, 1)
    moving_h = with_halo(moving_t, (("gy", 1),), REACH).astype(jnp.float32)
    moving_h = jnp.pad(moving_h, ((0, 0), (0, 4), (0, 0)))
    rows = height + 2 * REACH
    m0 = moving_h[:, :rows]
    m4 = moving_h[:, 4 : rows + 4]
    disp_init = pl.pallas_call(
        lambda *refs: softmin_kernel(total_y, *refs),
        out_shape=jax.ShapeDtypeStruct((height, columns_dev), jnp.float32),
        compiler_params=pltpu.CompilerParams(vmem_limit_bytes=60 * 1024 * 1024),
    )(fixed_t.astype(jnp.float32), m0, m4, mult_rows)

    target_field = disp_init.reshape(height, -1, XS)
    field = target_field
    first_moment = jnp.zeros_like(target_field)
    second_moment = jnp.zeros_like(target_field)
    for iteration in range(ITERS):
        padded = with_halo(field, (("gy", 0), ("gz", 1)), RMAX)
        smoothed = smooth_inner(padded, smooth_radii[iteration], RMAX)
        field, first_moment, second_moment = adam_update(
            field, target_field, smoothed, first_moment, second_moment, iteration
        )
    return (disp_init, field.reshape(height, columns_dev))


def solution(mesh):
    in_specs = (P("gy", "gz"), P("gy", "gz"), P("gy", "gz", None), P("gy", "gz"), P())
    out_specs = (P("gy", "gz"), P("gy", "gz"))
    return jax.shard_map(
        per_device, mesh=mesh, in_specs=in_specs, out_specs=out_specs, check_vma=False
    )
```

```python
import jax
import jax.numpy as jnp
from jax import lax
from jax.experimental import pallas as pl
from jax.experimental.pallas import tpu as pltpu
from jax.sharding import PartitionSpec as P

CH = 16
XS = 8
REACH = 32
RMAX = 4
ITERS = 3
NOFF = 2 * (REACH // 4) + 1


softmin_temp = 2.0
smooth_weight = 2.0
adam_rate = 0.2
beta_first = 0.9
beta_second = 0.999
adam_floor = 0.05


def with_halo(cells, sides, width):
    for axis, dim in sides:
        count = lax.axis_size(axis)
        ends = count - 1
        head = lax.slice_in_dim(cells, 0, width, axis=dim)
        tail = lax.slice_in_dim(cells, cells.shape[dim] - width, cells.shape[dim], axis=dim)
        cells = jnp.concatenate(
            [
                lax.ppermute(tail, axis, [(i, (i + 1) % count) for i in range(ends)]),
                cells,
                lax.ppermute(head, axis, [((i + 1) % count, i) for i in range(ends)]),
            ],
            axis=dim,
        )
    return cells


def box_weights(radius):
    spread = jnp.arange(-RMAX, RMAX + 1)
    inside = jnp.abs(spread) <= radius
    return jnp.where(inside, 1.0, 0.0).astype(jnp.float32) / (2 * radius + 1).astype(jnp.float32)


def smooth_inner(padded, radius, margin):
    weights = box_weights(radius)
    height = padded.shape[0] - 2 * margin
    layers = padded.shape[1] - 2 * margin
    depth_cells = padded.shape[2]
    along_y = jnp.zeros((height, padded.shape[1], depth_cells), jnp.float32)
    for offset in range(-RMAX, RMAX + 1):
        along_y = (
            along_y + weights[RMAX + offset] * padded[margin + offset : margin + offset + height]
        )
    along_z = jnp.zeros((height, layers, depth_cells), jnp.float32)
    for offset in range(-RMAX, RMAX + 1):
        along_z = (
            along_z
            + weights[RMAX + offset] * along_y[:, margin + offset : margin + offset + layers]
        )
    x_padded = jnp.pad(along_z, ((0, 0), (0, 0), (RMAX, RMAX)))
    along_x = jnp.zeros((height, layers, depth_cells), jnp.float32)
    for offset in range(-RMAX, RMAX + 1):
        along_x = (
            along_x
            + weights[RMAX + offset] * x_padded[:, :, RMAX + offset : RMAX + offset + depth_cells]
        )
    return along_x


def adam_update(field, target_field, smoothed, first_moment, second_moment, iteration):
    gradient = field - target_field + smooth_weight * (field - smoothed)
    first_moment = beta_first * first_moment + (1.0 - beta_first) * gradient
    second_moment = beta_second * second_moment + (1.0 - beta_second) * gradient * gradient
    first_hat = first_moment / (1.0 - beta_first ** (iteration + 1))
    second_hat = second_moment / (1.0 - beta_second ** (iteration + 1))
    field = field - adam_rate * first_hat / (jnp.sqrt(second_hat) + adam_floor)
    return (field, first_moment, second_moment)


HALO_Y = 16
HALO_Z = 128


def exchange_halo(cells, wy, wz):
    ny = lax.axis_size("gy")
    nz = lax.axis_size("gz")

    def send(piece, dy, dz):
        pairs = []
        for a in range(ny):
            for b in range(nz):
                if 0 <= a + dy < ny and 0 <= b + dz < nz:
                    pairs.append((a * nz + b, (a + dy) * nz + b + dz))
        return lax.ppermute(piece, ("gy", "gz"), pairs)

    top_rows = cells[-wy:]
    bottom_rows = cells[:wy]
    top = send(top_rows, 1, 0)
    bottom = send(bottom_rows, -1, 0)
    left = send(cells[:, -wz:], 0, 1)
    right = send(cells[:, :wz], 0, -1)
    top_left = send(top_rows[:, -wz:], 1, 1)
    top_right = send(top_rows[:, :wz], 1, -1)
    bottom_left = send(bottom_rows[:, -wz:], -1, 1)
    bottom_right = send(bottom_rows[:, :wz], -1, -1)
    return jnp.concatenate(
        [
            jnp.concatenate([top_left, top, top_right], axis=1),
            jnp.concatenate([left, cells, right], axis=1),
            jnp.concatenate([bottom_left, bottom, bottom_right], axis=1),
        ],
        axis=0,
    )


def shifted(a, offset, axis):
    if offset == 0:
        return a
    return pltpu.roll(a, (-offset) % a.shape[axis], axis)


def box_smooth(u, radius, lane_x):
    scale = 1.0 / float(2 * radius + 1)
    along_y = u
    for o in range(1, radius + 1):
        along_y = along_y + shifted(u, -o, 0) + shifted(u, o, 0)
    along_y = along_y * scale
    along_z = along_y
    for o in range(1, radius + 1):
        along_z = along_z + shifted(along_y, -XS * o, 1) + shifted(along_y, XS * o, 1)
    along_z = along_z * scale
    along_x = along_z
    for o in range(1, radius + 1):
        along_x = (
            along_x
            + jnp.where(lane_x >= o, shifted(along_z, -o, 1), 0.0)
            + jnp.where(lane_x < XS - o, shifted(along_z, o, 1), 0.0)
        )
    return along_x * scale


def adam_kernel(radii_ref, d_ref, mask_ref, o_ref):
    target = d_ref[...]
    inside = mask_ref[...] > 0.0
    lane_x = lax.broadcasted_iota(jnp.int32, target.shape, 1) % XS
    field = jnp.where(inside, target, 0.0)
    first_moment = jnp.zeros_like(target)
    second_moment = jnp.zeros_like(target)
    for iteration in range(ITERS):
        radius = radii_ref[iteration]
        smoothed = lax.switch(
            jnp.clip(radius - 1, 0, RMAX - 1),
            [lambda u, r=r: box_smooth(u, r, lane_x) for r in range(1, RMAX + 1)],
            field,
        )
        field, first_moment, second_moment = adam_update(
            field, target, smoothed, first_moment, second_moment, iteration
        )
        field = jnp.where(inside, field, 0.0)
    height = o_ref.shape[0]
    width = o_ref.shape[1]
    o_ref[...] = field[HALO_Y : HALO_Y + height, HALO_Z : HALO_Z + width]


def softmin_kernel(total_y, f_ref, m0_ref, m4_ref, n_ref, o_ref):
    height = f_ref.shape[1]
    lanes_total = f_ref.shape[2]

    def body(t, carry):
        r0 = pl.multiple_of(t * 8, 8)
        for j in range(lanes_total // 128):
            lanes = pl.ds(128 * j, 128)
            fixed = [f_ref[c, pl.ds(r0, 8), lanes] for c in range(CH)]
            scores = []
            counts = []
            for o in range(NOFF):
                shift = 4 * o
                if shift % 8 == 0:
                    src, base = m0_ref, shift
                else:
                    src, base = m4_ref, shift - 4
                acc = None
                for c in range(CH):
                    d = fixed[c] - src[c, pl.ds(r0 + base, 8), lanes]
                    acc = d * d if acc is None else acc + d * d
                n_o = n_ref[o, pl.ds(r0, 8), :]
                counts.append(n_o)
                scores.append(jnp.where(n_o > 0.0, -acc / softmin_temp, -jnp.inf))
            peak = scores[0]
            for s in scores[1:]:
                peak = jnp.maximum(peak, s)
            den = None
            num = None
            for o in range(NOFF):
                w = counts[o] * jnp.exp(scores[o] - peak)
                shift_norm = 2.0 * float(4 * o - REACH) / total_y
                den = w if den is None else den + w
                num = w * shift_norm if num is None else num + w * shift_norm
            o_ref[pl.ds(r0, 8), lanes] = num / den
        return carry

    lax.fori_loop(0, height // 8, body, 0)


def per_device(fixed_features, moving_features, cand_offsets, cand_lengths, smooth_radii):
    height = fixed_features.shape[0]
    columns_dev = fixed_features.shape[1] // CH
    blocks = height // 4
    total_y = height * lax.axis_size("gy")
    shifts = cand_offsets[:, 0, :]
    counts = cand_lengths[:, 0]
    live = jnp.arange(shifts.shape[1], dtype=jnp.int32)[None, :] < counts[:, None]
    offset_values = 4 * jnp.arange(NOFF, dtype=jnp.int32) - REACH
    hits = (shifts[:, :, None] == offset_values[None, None, :]) & live[:, :, None]
    mult = jnp.sum(hits.astype(jnp.float32), axis=1)
    mult_rows = jnp.repeat(mult.T, 4, axis=1)
    mult_rows = jnp.broadcast_to(mult_rows[:, :, None], (NOFF, height, 128))

    fixed_t = fixed_features.reshape(height, columns_dev, CH).transpose(2, 0, 1)
    moving_t = moving_features.reshape(height, columns_dev, CH).transpose(2, 0, 1)
    moving_h = with_halo(moving_t, (("gy", 1),), REACH).astype(jnp.float32)
    moving_h = jnp.pad(moving_h, ((0, 0), (0, 4), (0, 0)))
    rows = height + 2 * REACH
    m0 = moving_h[:, :rows]
    m4 = moving_h[:, 4 : rows + 4]
    disp_init = pl.pallas_call(
        lambda *refs: softmin_kernel(total_y, *refs),
        out_shape=jax.ShapeDtypeStruct((height, columns_dev), jnp.float32),
        compiler_params=pltpu.CompilerParams(vmem_limit_bytes=60 * 1024 * 1024),
    )(fixed_t.astype(jnp.float32), m0, m4, mult_rows)

    ext = exchange_halo(disp_init, HALO_Y, HALO_Z)
    rows_ext, lanes_ext = ext.shape
    row_global = lax.axis_index("gy") * height - HALO_Y + lax.broadcasted_iota(
        jnp.int32, (rows_ext, lanes_ext), 0
    )
    lane_global = lax.axis_index("gz") * columns_dev - HALO_Z + lax.broadcasted_iota(
        jnp.int32, (rows_ext, lanes_ext), 1
    )
    inside = (
        (row_global >= 0)
        & (row_global < total_y)
        & (lane_global >= 0)
        & (lane_global < columns_dev * lax.axis_size("gz"))
    )
    grid_mask = inside.astype(jnp.float32)
    final_ext = pl.pallas_call(
        adam_kernel,
        out_shape=jax.ShapeDtypeStruct((height, columns_dev), jnp.float32),
        in_specs=[
            pl.BlockSpec(memory_space=pltpu.SMEM),
            pl.BlockSpec(memory_space=pltpu.VMEM),
            pl.BlockSpec(memory_space=pltpu.VMEM),
        ],
        compiler_params=pltpu.CompilerParams(vmem_limit_bytes=32 * 1024 * 1024),
    )(smooth_radii.astype(jnp.int32), ext, grid_mask)
    return (disp_init, final_ext)


def solution(mesh):
    in_specs = (P("gy", "gz"), P("gy", "gz"), P("gy", "gz", None), P("gy", "gz"), P())
    out_specs = (P("gy", "gz"), P("gy", "gz"))
    return jax.shard_map(
        per_device, mesh=mesh, in_specs=in_specs, out_specs=out_specs, check_vma=False
    )
```

```python
import jax
import jax.numpy as jnp
from jax import lax
from jax.experimental import pallas as pl
from jax.experimental.pallas import tpu as pltpu
from jax.sharding import PartitionSpec as P

CH = 16
XS = 8
REACH = 32
RMAX = 4
ITERS = 3
NOFF = 2 * (REACH // 4) + 1


softmin_temp = 2.0
smooth_weight = 2.0
adam_rate = 0.2
beta_first = 0.9
beta_second = 0.999
adam_floor = 0.05


def with_halo(cells, sides, width):
    for axis, dim in sides:
        count = lax.axis_size(axis)
        ends = count - 1
        head = lax.slice_in_dim(cells, 0, width, axis=dim)
        tail = lax.slice_in_dim(cells, cells.shape[dim] - width, cells.shape[dim], axis=dim)
        cells = jnp.concatenate(
            [
                lax.ppermute(tail, axis, [(i, (i + 1) % count) for i in range(ends)]),
                cells,
                lax.ppermute(head, axis, [((i + 1) % count, i) for i in range(ends)]),
            ],
            axis=dim,
        )
    return cells


def box_weights(radius):
    spread = jnp.arange(-RMAX, RMAX + 1)
    inside = jnp.abs(spread) <= radius
    return jnp.where(inside, 1.0, 0.0).astype(jnp.float32) / (2 * radius + 1).astype(jnp.float32)


def smooth_inner(padded, radius, margin):
    weights = box_weights(radius)
    height = padded.shape[0] - 2 * margin
    layers = padded.shape[1] - 2 * margin
    depth_cells = padded.shape[2]
    along_y = jnp.zeros((height, padded.shape[1], depth_cells), jnp.float32)
    for offset in range(-RMAX, RMAX + 1):
        along_y = (
            along_y + weights[RMAX + offset] * padded[margin + offset : margin + offset + height]
        )
    along_z = jnp.zeros((height, layers, depth_cells), jnp.float32)
    for offset in range(-RMAX, RMAX + 1):
        along_z = (
            along_z
            + weights[RMAX + offset] * along_y[:, margin + offset : margin + offset + layers]
        )
    x_padded = jnp.pad(along_z, ((0, 0), (0, 0), (RMAX, RMAX)))
    along_x = jnp.zeros((height, layers, depth_cells), jnp.float32)
    for offset in range(-RMAX, RMAX + 1):
        along_x = (
            along_x
            + weights[RMAX + offset] * x_padded[:, :, RMAX + offset : RMAX + offset + depth_cells]
        )
    return along_x


def adam_update(field, target_field, smoothed, first_moment, second_moment, iteration):
    gradient = field - target_field + smooth_weight * (field - smoothed)
    first_moment = beta_first * first_moment + (1.0 - beta_first) * gradient
    second_moment = beta_second * second_moment + (1.0 - beta_second) * gradient * gradient
    first_hat = first_moment / (1.0 - beta_first ** (iteration + 1))
    second_hat = second_moment / (1.0 - beta_second ** (iteration + 1))
    field = field - adam_rate * first_hat / (jnp.sqrt(second_hat) + adam_floor)
    return (field, first_moment, second_moment)


HALO_Y = 16
HALO_Z = 128
SEND_Y = 8
SEND_Z = 8 * XS


def exchange_halo(cells, wy, wz, send_y, send_z):
    ny = lax.axis_size("gy")
    nz = lax.axis_size("gz")
    top = lax.ppermute(cells[-send_y:], "gy", [(i, i + 1) for i in range(ny - 1)])
    bottom = lax.ppermute(cells[:send_y], "gy", [(i + 1, i) for i in range(ny - 1)])
    cells = jnp.concatenate([top, cells, bottom], axis=0)
    left = lax.ppermute(cells[:, -send_z:], "gz", [(i, i + 1) for i in range(nz - 1)])
    right = lax.ppermute(cells[:, :send_z], "gz", [(i + 1, i) for i in range(nz - 1)])
    cells = jnp.concatenate([left, cells, right], axis=1)
    return jnp.pad(cells, ((wy - send_y, wy - send_y), (wz - send_z, wz - send_z)))


def shifted(a, offset, axis):
    if offset == 0:
        return a
    return pltpu.roll(a, (-offset) % a.shape[axis], axis)


def box_smooth(u, radius, lane_x):
    scale = 1.0 / float(2 * radius + 1)
    along_y = u
    for o in range(1, radius + 1):
        along_y = along_y + shifted(u, -o, 0) + shifted(u, o, 0)
    along_y = along_y * scale
    along_z = along_y
    for o in range(1, radius + 1):
        along_z = along_z + shifted(along_y, -XS * o, 1) + shifted(along_y, XS * o, 1)
    along_z = along_z * scale
    along_x = along_z
    for o in range(1, radius + 1):
        along_x = (
            along_x
            + jnp.where(lane_x >= o, shifted(along_z, -o, 1), 0.0)
            + jnp.where(lane_x < XS - o, shifted(along_z, o, 1), 0.0)
        )
    return along_x * scale


def adam_kernel(radii_ref, d_ref, mask_ref, o_ref):
    target = d_ref[...]
    inside = mask_ref[...] > 0.0
    lane_x = lax.broadcasted_iota(jnp.int32, target.shape, 1) % XS
    field = jnp.where(inside, target, 0.0)
    first_moment = jnp.zeros_like(target)
    second_moment = jnp.zeros_like(target)
    for iteration in range(ITERS):
        radius = radii_ref[iteration]
        smoothed = lax.switch(
            jnp.clip(radius - 1, 0, RMAX - 1),
            [lambda u, r=r: box_smooth(u, r, lane_x) for r in range(1, RMAX + 1)],
            field,
        )
        field, first_moment, second_moment = adam_update(
            field, target, smoothed, first_moment, second_moment, iteration
        )
        field = jnp.where(inside, field, 0.0)
    height = o_ref.shape[0]
    width = o_ref.shape[1]
    o_ref[...] = field[HALO_Y : HALO_Y + height, HALO_Z : HALO_Z + width]


def softmin_kernel(total_y, ft_ref, mt_ref, top_ref, bot_ref, n_ref, o_ref, f_ref, m0_ref, m4_ref):
    height = ft_ref.shape[1]
    lanes_total = ft_ref.shape[2]
    rows = height + 2 * REACH

    def build(c, carry):
        f_ref[c] = ft_ref[c].astype(jnp.float32)
        m0_ref[c, pl.ds(0, REACH), :] = top_ref[c].astype(jnp.float32)
        m0_ref[c, pl.ds(REACH, height), :] = mt_ref[c].astype(jnp.float32)
        m0_ref[c, pl.ds(REACH + height, REACH), :] = bot_ref[c].astype(jnp.float32)
        return carry

    lax.fori_loop(0, CH, build, 0)

    def build_shifted(c, carry):
        m4_ref[c, pl.ds(0, rows - 8), :] = m0_ref[c, pl.ds(4, rows - 8), :]
        m4_ref[c, pl.ds(rows - 8, 8), :] = jnp.zeros((8, lanes_total), jnp.float32)
        return carry

    lax.fori_loop(0, CH, build_shifted, 0)

    def body(t, carry):
        r0 = pl.multiple_of(t * 8, 8)
        for j in range(lanes_total // 128):
            lanes = pl.ds(128 * j, 128)
            fixed = [f_ref[c, pl.ds(r0, 8), lanes] for c in range(CH)]
            scores = []
            counts = []
            for o in range(NOFF):
                shift = 4 * o
                if shift % 8 == 0:
                    src, base = m0_ref, shift
                else:
                    src, base = m4_ref, shift - 4
                acc = None
                for c in range(CH):
                    d = fixed[c] - src[c, pl.ds(r0 + base, 8), lanes]
                    acc = d * d if acc is None else acc + d * d
                n_o = n_ref[o, pl.ds(r0, 8), :]
                counts.append(n_o)
                scores.append(jnp.where(n_o > 0.0, -acc / softmin_temp, -jnp.inf))
            peak = scores[0]
            for s in scores[1:]:
                peak = jnp.maximum(peak, s)
            den = None
            num = None
            for o in range(NOFF):
                w = counts[o] * jnp.exp(scores[o] - peak)
                shift_norm = 2.0 * float(4 * o - REACH) / total_y
                den = w if den is None else den + w
                num = w * shift_norm if num is None else num + w * shift_norm
            o_ref[pl.ds(r0, 8), lanes] = num / den
        return carry

    lax.fori_loop(0, height // 8, body, 0)


def per_device(fixed_features, moving_features, cand_offsets, cand_lengths, smooth_radii):
    height = fixed_features.shape[0]
    columns_dev = fixed_features.shape[1] // CH
    blocks = height // 4
    total_y = height * lax.axis_size("gy")
    shifts = cand_offsets[:, 0, :]
    counts = cand_lengths[:, 0]
    live = jnp.arange(shifts.shape[1], dtype=jnp.int32)[None, :] < counts[:, None]
    offset_values = 4 * jnp.arange(NOFF, dtype=jnp.int32) - REACH
    hits = (shifts[:, :, None] == offset_values[None, None, :]) & live[:, :, None]
    mult = jnp.sum(hits.astype(jnp.float32), axis=1)
    mult_rows = jnp.repeat(mult.T, 4, axis=1)
    mult_rows = jnp.broadcast_to(mult_rows[:, :, None], (NOFF, height, 128))

    gy_count = lax.axis_size("gy")
    top_rows = lax.ppermute(
        moving_features[height - REACH :], "gy", [(i, i + 1) for i in range(gy_count - 1)]
    )
    bottom_rows = lax.ppermute(
        moving_features[:REACH], "gy", [(i + 1, i) for i in range(gy_count - 1)]
    )

    def channel_major(a):
        return a.reshape(a.shape[0], columns_dev, CH).transpose(2, 0, 1)

    rows = height + 2 * REACH
    disp_init = pl.pallas_call(
        lambda *refs: softmin_kernel(total_y, *refs),
        out_shape=jax.ShapeDtypeStruct((height, columns_dev), jnp.float32),
        scratch_shapes=[
            pltpu.VMEM((CH, height, columns_dev), jnp.float32),
            pltpu.VMEM((CH, rows, columns_dev), jnp.float32),
            pltpu.VMEM((CH, rows, columns_dev), jnp.float32),
        ],
        compiler_params=pltpu.CompilerParams(vmem_limit_bytes=60 * 1024 * 1024),
    )(
        channel_major(fixed_features),
        channel_major(moving_features),
        channel_major(top_rows),
        channel_major(bottom_rows),
        mult_rows,
    )

    ext = exchange_halo(disp_init, HALO_Y, HALO_Z, SEND_Y, SEND_Z)
    rows_ext, lanes_ext = ext.shape
    row_global = lax.axis_index("gy") * height - HALO_Y + lax.broadcasted_iota(
        jnp.int32, (rows_ext, lanes_ext), 0
    )
    lane_global = lax.axis_index("gz") * columns_dev - HALO_Z + lax.broadcasted_iota(
        jnp.int32, (rows_ext, lanes_ext), 1
    )
    inside = (
        (row_global >= 0)
        & (row_global < total_y)
        & (lane_global >= 0)
        & (lane_global < columns_dev * lax.axis_size("gz"))
    )
    grid_mask = inside.astype(jnp.float32)
    final_ext = pl.pallas_call(
        adam_kernel,
        out_shape=jax.ShapeDtypeStruct((height, columns_dev), jnp.float32),
        in_specs=[
            pl.BlockSpec(memory_space=pltpu.SMEM),
            pl.BlockSpec(memory_space=pltpu.VMEM),
            pl.BlockSpec(memory_space=pltpu.VMEM),
        ],
        compiler_params=pltpu.CompilerParams(vmem_limit_bytes=32 * 1024 * 1024),
    )(smooth_radii.astype(jnp.int32), ext, grid_mask)
    return (disp_init, final_ext)


def solution(mesh):
    in_specs = (P("gy", "gz"), P("gy", "gz"), P("gy", "gz", None), P("gy", "gz"), P())
    out_specs = (P("gy", "gz"), P("gy", "gz"))
    return jax.shard_map(
        per_device, mesh=mesh, in_specs=in_specs, out_specs=out_specs, check_vma=False
    )
```

```python
import jax
import jax.numpy as jnp
from jax import lax
from jax.experimental import pallas as pl
from jax.experimental.pallas import tpu as pltpu
from jax.sharding import PartitionSpec as P

CH = 16
XS = 8
REACH = 32
RMAX = 4
ITERS = 3
NOFF = 2 * (REACH // 4) + 1


softmin_temp = 2.0
smooth_weight = 2.0
adam_rate = 0.2
beta_first = 0.9
beta_second = 0.999
adam_floor = 0.05


def with_halo(cells, sides, width):
    for axis, dim in sides:
        count = lax.axis_size(axis)
        ends = count - 1
        head = lax.slice_in_dim(cells, 0, width, axis=dim)
        tail = lax.slice_in_dim(cells, cells.shape[dim] - width, cells.shape[dim], axis=dim)
        cells = jnp.concatenate(
            [
                lax.ppermute(tail, axis, [(i, (i + 1) % count) for i in range(ends)]),
                cells,
                lax.ppermute(head, axis, [((i + 1) % count, i) for i in range(ends)]),
            ],
            axis=dim,
        )
    return cells


def box_weights(radius):
    spread = jnp.arange(-RMAX, RMAX + 1)
    inside = jnp.abs(spread) <= radius
    return jnp.where(inside, 1.0, 0.0).astype(jnp.float32) / (2 * radius + 1).astype(jnp.float32)


def smooth_inner(padded, radius, margin):
    weights = box_weights(radius)
    height = padded.shape[0] - 2 * margin
    layers = padded.shape[1] - 2 * margin
    depth_cells = padded.shape[2]
    along_y = jnp.zeros((height, padded.shape[1], depth_cells), jnp.float32)
    for offset in range(-RMAX, RMAX + 1):
        along_y = (
            along_y + weights[RMAX + offset] * padded[margin + offset : margin + offset + height]
        )
    along_z = jnp.zeros((height, layers, depth_cells), jnp.float32)
    for offset in range(-RMAX, RMAX + 1):
        along_z = (
            along_z
            + weights[RMAX + offset] * along_y[:, margin + offset : margin + offset + layers]
        )
    x_padded = jnp.pad(along_z, ((0, 0), (0, 0), (RMAX, RMAX)))
    along_x = jnp.zeros((height, layers, depth_cells), jnp.float32)
    for offset in range(-RMAX, RMAX + 1):
        along_x = (
            along_x
            + weights[RMAX + offset] * x_padded[:, :, RMAX + offset : RMAX + offset + depth_cells]
        )
    return along_x


def adam_update(field, target_field, smoothed, first_moment, second_moment, iteration):
    gradient = field - target_field + smooth_weight * (field - smoothed)
    first_moment = beta_first * first_moment + (1.0 - beta_first) * gradient
    second_moment = beta_second * second_moment + (1.0 - beta_second) * gradient * gradient
    first_hat = first_moment / (1.0 - beta_first ** (iteration + 1))
    second_hat = second_moment / (1.0 - beta_second ** (iteration + 1))
    field = field - adam_rate * first_hat / (jnp.sqrt(second_hat) + adam_floor)
    return (field, first_moment, second_moment)


HALO_Y = 8
HALO_Z = 8 * XS
SEND_Y = 8
SEND_Z = 8 * XS


def exchange_halo(cells, wy, wz, send_y, send_z):
    ny = lax.axis_size("gy")
    nz = lax.axis_size("gz")
    top = lax.ppermute(cells[-send_y:], "gy", [(i, i + 1) for i in range(ny - 1)])
    bottom = lax.ppermute(cells[:send_y], "gy", [(i + 1, i) for i in range(ny - 1)])
    cells = jnp.concatenate([top, cells, bottom], axis=0)
    left = lax.ppermute(cells[:, -send_z:], "gz", [(i, i + 1) for i in range(nz - 1)])
    right = lax.ppermute(cells[:, :send_z], "gz", [(i + 1, i) for i in range(nz - 1)])
    cells = jnp.concatenate([left, cells, right], axis=1)
    return jnp.pad(cells, ((wy - send_y, wy - send_y), (wz - send_z, wz - send_z)))


def shifted(a, offset, axis):
    if offset == 0:
        return a
    return pltpu.roll(a, (-offset) % a.shape[axis], axis)


def box_smooth(u, radius, lane_x):
    scale = 1.0 / float(2 * radius + 1)
    along_y = u
    for o in range(1, radius + 1):
        along_y = along_y + shifted(u, -o, 0) + shifted(u, o, 0)
    along_y = along_y * scale
    along_z = along_y
    for o in range(1, radius + 1):
        along_z = along_z + shifted(along_y, -XS * o, 1) + shifted(along_y, XS * o, 1)
    along_z = along_z * scale
    along_x = along_z
    for o in range(1, radius + 1):
        along_x = (
            along_x
            + jnp.where(lane_x >= o, shifted(along_z, -o, 1), 0.0)
            + jnp.where(lane_x < XS - o, shifted(along_z, o, 1), 0.0)
        )
    return along_x * scale


def adam_kernel(radii_ref, d_ref, mask_ref, o_ref):
    target = d_ref[...]
    inside = mask_ref[...] > 0.0
    lane_x = lax.broadcasted_iota(jnp.int32, target.shape, 1) % XS
    field = jnp.where(inside, target, 0.0)
    first_moment = jnp.zeros_like(target)
    second_moment = jnp.zeros_like(target)
    for iteration in range(ITERS):
        radius = radii_ref[iteration]
        smoothed = lax.switch(
            jnp.clip(radius - 1, 0, RMAX - 1),
            [lambda u, r=r: box_smooth(u, r, lane_x) for r in range(1, RMAX + 1)],
            field,
        )
        field, first_moment, second_moment = adam_update(
            field, target, smoothed, first_moment, second_moment, iteration
        )
        field = jnp.where(inside, field, 0.0)
    height = o_ref.shape[0]
    width = o_ref.shape[1]
    o_ref[...] = field[HALO_Y : HALO_Y + height, HALO_Z : HALO_Z + width]


def softmin_kernel(total_y, tile_ranges, with_rows_beyond, *refs):
    if with_rows_beyond:
        ft_ref, mt_ref, top_ref, bot_ref, n_ref, done_ref, o_ref, f_ref, m0_ref, m4_ref = refs
    else:
        ft_ref, mt_ref, n_ref, o_ref, f_ref, m0_ref, m4_ref = refs
    height = ft_ref.shape[1]
    lanes_total = ft_ref.shape[2]
    rows = height + 2 * REACH

    def build(c, carry):
        f_ref[c] = ft_ref[c].astype(jnp.float32)
        m0_ref[c, pl.ds(REACH, height), :] = mt_ref[c].astype(jnp.float32)
        if with_rows_beyond:
            m0_ref[c, pl.ds(0, REACH), :] = top_ref[c].astype(jnp.float32)
            m0_ref[c, pl.ds(REACH + height, REACH), :] = bot_ref[c].astype(jnp.float32)
        else:
            m0_ref[c, pl.ds(0, REACH), :] = jnp.zeros((REACH, lanes_total), jnp.float32)
            m0_ref[c, pl.ds(REACH + height, REACH), :] = jnp.zeros((REACH, lanes_total), jnp.float32)
        return carry

    lax.fori_loop(0, CH, build, 0)

    def build_shifted(c, carry):
        m4_ref[c, pl.ds(0, rows - 8), :] = m0_ref[c, pl.ds(4, rows - 8), :]
        m4_ref[c, pl.ds(rows - 8, 8), :] = jnp.zeros((8, lanes_total), jnp.float32)
        return carry

    lax.fori_loop(0, CH, build_shifted, 0)

    def body(i, carry):
        t = i
        for lo, hi in tile_ranges[1:]:
            t = jnp.where(t >= tile_ranges[0][1], t - tile_ranges[0][1] + lo, t)
        t = t + tile_ranges[0][0]
        r0 = pl.multiple_of(t * 8, 8)
        for j in range(lanes_total // 128):
            lanes = pl.ds(128 * j, 128)
            fixed = [f_ref[c, pl.ds(r0, 8), lanes] for c in range(CH)]
            scores = []
            counts = []
            for o in range(NOFF):
                shift = 4 * o
                if shift % 8 == 0:
                    src, base = m0_ref, shift
                else:
                    src, base = m4_ref, shift - 4
                acc = None
                for c in range(CH):
                    d = fixed[c] - src[c, pl.ds(r0 + base, 8), lanes]
                    acc = d * d if acc is None else acc + d * d
                n_o = n_ref[o, pl.ds(r0, 8), :]
                counts.append(n_o)
                scores.append(jnp.where(n_o > 0.0, -acc / softmin_temp, -jnp.inf))
            peak = scores[0]
            for s in scores[1:]:
                peak = jnp.maximum(peak, s)
            den = None
            num = None
            for o in range(NOFF):
                w = counts[o] * jnp.exp(scores[o] - peak)
                shift_norm = 2.0 * float(4 * o - REACH) / total_y
                den = w if den is None else den + w
                num = w * shift_norm if num is None else num + w * shift_norm
            o_ref[pl.ds(r0, 8), lanes] = num / den
        return carry

    lax.fori_loop(0, sum(hi - lo for lo, hi in tile_ranges), body, 0)
    if with_rows_beyond:
        lo = tile_ranges[0][1] * 8
        hi = tile_ranges[1][0] * 8
        o_ref[pl.ds(lo, hi - lo), :] = done_ref[pl.ds(lo, hi - lo), :]


def per_device(fixed_features, moving_features, cand_offsets, cand_lengths, smooth_radii):
    height = fixed_features.shape[0]
    columns_dev = fixed_features.shape[1] // CH
    blocks = height // 4
    total_y = height * lax.axis_size("gy")
    shifts = cand_offsets[:, 0, :]
    counts = cand_lengths[:, 0]
    live = jnp.arange(shifts.shape[1], dtype=jnp.int32)[None, :] < counts[:, None]
    offset_values = 4 * jnp.arange(NOFF, dtype=jnp.int32) - REACH
    hits = (shifts[:, :, None] == offset_values[None, None, :]) & live[:, :, None]
    mult = jnp.sum(hits.astype(jnp.float32), axis=1)
    mult_rows = jnp.repeat(mult.T, 4, axis=1)
    mult_rows = jnp.broadcast_to(mult_rows[:, :, None], (NOFF, height, 128))

    gy_count = lax.axis_size("gy")
    top_rows = lax.ppermute(
        moving_features[height - REACH :], "gy", [(i, i + 1) for i in range(gy_count - 1)]
    )
    bottom_rows = lax.ppermute(
        moving_features[:REACH], "gy", [(i + 1, i) for i in range(gy_count - 1)]
    )

    def channel_major(a):
        return a.reshape(a.shape[0], columns_dev, CH).transpose(2, 0, 1)

    rows = height + 2 * REACH
    tiles = height // 8
    reach_tiles = REACH // 8
    scratch = [
        pltpu.VMEM((CH, height, columns_dev), jnp.float32),
        pltpu.VMEM((CH, rows, columns_dev), jnp.float32),
        pltpu.VMEM((CH, rows, columns_dev), jnp.float32),
    ]
    params = pltpu.CompilerParams(vmem_limit_bytes=60 * 1024 * 1024)
    out_shape = jax.ShapeDtypeStruct((height, columns_dev), jnp.float32)
    fixed_c = channel_major(fixed_features)
    moving_c = channel_major(moving_features)
    middle = pl.pallas_call(
        lambda *refs: softmin_kernel(total_y, [(reach_tiles, tiles - reach_tiles)], False, *refs),
        out_shape=out_shape,
        scratch_shapes=scratch,
        compiler_params=params,
    )(fixed_c, moving_c, mult_rows)
    disp_init = pl.pallas_call(
        lambda *refs: softmin_kernel(
            total_y, [(0, reach_tiles), (tiles - reach_tiles, tiles)], True, *refs
        ),
        out_shape=out_shape,
        scratch_shapes=scratch,
        compiler_params=params,
    )(
        fixed_c,
        moving_c,
        channel_major(top_rows),
        channel_major(bottom_rows),
        mult_rows,
        middle,
    )

    ext = exchange_halo(disp_init, HALO_Y, HALO_Z, SEND_Y, SEND_Z)
    rows_ext, lanes_ext = ext.shape
    row_global = lax.axis_index("gy") * height - HALO_Y + lax.broadcasted_iota(
        jnp.int32, (rows_ext, lanes_ext), 0
    )
    lane_global = lax.axis_index("gz") * columns_dev - HALO_Z + lax.broadcasted_iota(
        jnp.int32, (rows_ext, lanes_ext), 1
    )
    inside = (
        (row_global >= 0)
        & (row_global < total_y)
        & (lane_global >= 0)
        & (lane_global < columns_dev * lax.axis_size("gz"))
    )
    grid_mask = inside.astype(jnp.float32)
    final_ext = pl.pallas_call(
        adam_kernel,
        out_shape=jax.ShapeDtypeStruct((height, columns_dev), jnp.float32),
        in_specs=[
            pl.BlockSpec(memory_space=pltpu.SMEM),
            pl.BlockSpec(memory_space=pltpu.VMEM),
            pl.BlockSpec(memory_space=pltpu.VMEM),
        ],
        compiler_params=pltpu.CompilerParams(vmem_limit_bytes=32 * 1024 * 1024),
    )(smooth_radii.astype(jnp.int32), ext, grid_mask)
    return (disp_init, final_ext)


def solution(mesh):
    in_specs = (P("gy", "gz"), P("gy", "gz"), P("gy", "gz", None), P("gy", "gz"), P())
    out_specs = (P("gy", "gz"), P("gy", "gz"))
    return jax.shard_map(
        per_device, mesh=mesh, in_specs=in_specs, out_specs=out_specs, check_vma=False
    )
```

```python
import jax
import jax.numpy as jnp
from jax import lax
from jax.experimental import pallas as pl
from jax.experimental.pallas import tpu as pltpu
from jax.sharding import PartitionSpec as P

CH = 16
XS = 8
REACH = 32
RMAX = 4
ITERS = 3
NOFF = 2 * (REACH // 4) + 1


softmin_temp = 2.0
smooth_weight = 2.0
adam_rate = 0.2
beta_first = 0.9
beta_second = 0.999
adam_floor = 0.05


def with_halo(cells, sides, width):
    for axis, dim in sides:
        count = lax.axis_size(axis)
        ends = count - 1
        head = lax.slice_in_dim(cells, 0, width, axis=dim)
        tail = lax.slice_in_dim(cells, cells.shape[dim] - width, cells.shape[dim], axis=dim)
        cells = jnp.concatenate(
            [
                lax.ppermute(tail, axis, [(i, (i + 1) % count) for i in range(ends)]),
                cells,
                lax.ppermute(head, axis, [((i + 1) % count, i) for i in range(ends)]),
            ],
            axis=dim,
        )
    return cells


def box_weights(radius):
    spread = jnp.arange(-RMAX, RMAX + 1)
    inside = jnp.abs(spread) <= radius
    return jnp.where(inside, 1.0, 0.0).astype(jnp.float32) / (2 * radius + 1).astype(jnp.float32)


def smooth_inner(padded, radius, margin):
    weights = box_weights(radius)
    height = padded.shape[0] - 2 * margin
    layers = padded.shape[1] - 2 * margin
    depth_cells = padded.shape[2]
    along_y = jnp.zeros((height, padded.shape[1], depth_cells), jnp.float32)
    for offset in range(-RMAX, RMAX + 1):
        along_y = (
            along_y + weights[RMAX + offset] * padded[margin + offset : margin + offset + height]
        )
    along_z = jnp.zeros((height, layers, depth_cells), jnp.float32)
    for offset in range(-RMAX, RMAX + 1):
        along_z = (
            along_z
            + weights[RMAX + offset] * along_y[:, margin + offset : margin + offset + layers]
        )
    x_padded = jnp.pad(along_z, ((0, 0), (0, 0), (RMAX, RMAX)))
    along_x = jnp.zeros((height, layers, depth_cells), jnp.float32)
    for offset in range(-RMAX, RMAX + 1):
        along_x = (
            along_x
            + weights[RMAX + offset] * x_padded[:, :, RMAX + offset : RMAX + offset + depth_cells]
        )
    return along_x


def adam_update(field, target_field, smoothed, first_moment, second_moment, iteration):
    gradient = field - target_field + smooth_weight * (field - smoothed)
    first_moment = beta_first * first_moment + (1.0 - beta_first) * gradient
    second_moment = beta_second * second_moment + (1.0 - beta_second) * gradient * gradient
    first_hat = first_moment / (1.0 - beta_first ** (iteration + 1))
    second_hat = second_moment / (1.0 - beta_second ** (iteration + 1))
    field = field - adam_rate * first_hat / (jnp.sqrt(second_hat) + adam_floor)
    return (field, first_moment, second_moment)


HALO_Y = 8
HALO_Z = 8 * XS
SEND_Y = 8
SEND_Z = 8 * XS


def exchange_halo(cells, wy, wz, send_y, send_z):
    ny = lax.axis_size("gy")
    nz = lax.axis_size("gz")
    top = lax.ppermute(cells[-send_y:], "gy", [(i, i + 1) for i in range(ny - 1)])
    bottom = lax.ppermute(cells[:send_y], "gy", [(i + 1, i) for i in range(ny - 1)])
    cells = jnp.concatenate([top, cells, bottom], axis=0)
    left = lax.ppermute(cells[:, -send_z:], "gz", [(i, i + 1) for i in range(nz - 1)])
    right = lax.ppermute(cells[:, :send_z], "gz", [(i + 1, i) for i in range(nz - 1)])
    cells = jnp.concatenate([left, cells, right], axis=1)
    return jnp.pad(cells, ((wy - send_y, wy - send_y), (wz - send_z, wz - send_z)))


def shifted(a, offset, axis):
    if offset == 0:
        return a
    return pltpu.roll(a, (-offset) % a.shape[axis], axis)


def box_smooth(u, radius, lane_x):
    scale = 1.0 / float(2 * radius + 1)
    along_y = u
    for o in range(1, radius + 1):
        along_y = along_y + shifted(u, -o, 0) + shifted(u, o, 0)
    along_y = along_y * scale
    along_z = along_y
    for o in range(1, radius + 1):
        along_z = along_z + shifted(along_y, -XS * o, 1) + shifted(along_y, XS * o, 1)
    along_z = along_z * scale
    along_x = along_z
    for o in range(1, radius + 1):
        along_x = (
            along_x
            + jnp.where(lane_x >= o, shifted(along_z, -o, 1), 0.0)
            + jnp.where(lane_x < XS - o, shifted(along_z, o, 1), 0.0)
        )
    return along_x * scale


def adam_kernel(radii_ref, d_ref, mask_ref, o_ref):
    target = d_ref[...]
    inside = mask_ref[...] > 0.0
    lane_x = lax.broadcasted_iota(jnp.int32, target.shape, 1) % XS
    field = jnp.where(inside, target, 0.0)
    first_moment = jnp.zeros_like(target)
    second_moment = jnp.zeros_like(target)
    for iteration in range(ITERS):
        radius = radii_ref[iteration]
        smoothed = lax.switch(
            jnp.clip(radius - 1, 0, RMAX - 1),
            [lambda u, r=r: box_smooth(u, r, lane_x) for r in range(1, RMAX + 1)],
            field,
        )
        field, first_moment, second_moment = adam_update(
            field, target, smoothed, first_moment, second_moment, iteration
        )
        field = jnp.where(inside, field, 0.0)
    height = o_ref.shape[0]
    width = o_ref.shape[1]
    o_ref[...] = field[HALO_Y : HALO_Y + height, HALO_Z : HALO_Z + width]


def transpose_kernel(x_ref, o_ref, s_ref):
    chunk = 128 * CH
    for j in range(x_ref.shape[1] // chunk):
        s_ref[...] = x_ref[:, pl.ds(chunk * j, chunk)].astype(jnp.float32).T
        for c in range(CH):
            cols = s_ref[pl.ds(c, 128, stride=CH), :]
            o_ref[c, :, pl.ds(128 * j, 128)] = cols.T.astype(o_ref.dtype)


def channel_major(x):
    rows, lanes = x.shape
    return pl.pallas_call(
        transpose_kernel,
        out_shape=jax.ShapeDtypeStruct((CH, rows, lanes // CH), x.dtype),
        scratch_shapes=[pltpu.VMEM((128 * CH, rows), jnp.float32)],
    )(x)


def softmin_kernel(total_y, tile_ranges, with_rows_beyond, *refs):
    if with_rows_beyond:
        ft_ref, mt_ref, top_ref, bot_ref, n_ref, done_ref, o_ref, f_ref, m0_ref, m4_ref = refs
    else:
        ft_ref, mt_ref, n_ref, o_ref, f_ref, m0_ref, m4_ref = refs
    height = ft_ref.shape[1]
    lanes_total = ft_ref.shape[2]
    rows = height + 2 * REACH

    def build(c, carry):
        f_ref[c] = ft_ref[c].astype(jnp.float32)
        m0_ref[c, pl.ds(REACH, height), :] = mt_ref[c].astype(jnp.float32)
        if with_rows_beyond:
            m0_ref[c, pl.ds(0, REACH), :] = top_ref[c].astype(jnp.float32)
            m0_ref[c, pl.ds(REACH + height, REACH), :] = bot_ref[c].astype(jnp.float32)
        else:
            m0_ref[c, pl.ds(0, REACH), :] = jnp.zeros((REACH, lanes_total), jnp.float32)
            m0_ref[c, pl.ds(REACH + height, REACH), :] = jnp.zeros((REACH, lanes_total), jnp.float32)
        return carry

    lax.fori_loop(0, CH, build, 0)

    def build_shifted(c, carry):
        m4_ref[c, pl.ds(0, rows - 8), :] = m0_ref[c, pl.ds(4, rows - 8), :]
        m4_ref[c, pl.ds(rows - 8, 8), :] = jnp.zeros((8, lanes_total), jnp.float32)
        return carry

    lax.fori_loop(0, CH, build_shifted, 0)

    def body(i, carry):
        t = i
        for lo, hi in tile_ranges[1:]:
            t = jnp.where(t >= tile_ranges[0][1], t - tile_ranges[0][1] + lo, t)
        t = t + tile_ranges[0][0]
        r0 = pl.multiple_of(t * 8, 8)
        for j in range(lanes_total // 128):
            lanes = pl.ds(128 * j, 128)
            fixed = [f_ref[c, pl.ds(r0, 8), lanes] for c in range(CH)]
            scores = []
            counts = []
            for o in range(NOFF):
                shift = 4 * o
                if shift % 8 == 0:
                    src, base = m0_ref, shift
                else:
                    src, base = m4_ref, shift - 4
                acc = None
                for c in range(CH):
                    d = fixed[c] - src[c, pl.ds(r0 + base, 8), lanes]
                    acc = d * d if acc is None else acc + d * d
                n_o = n_ref[o, pl.ds(r0, 8), :]
                counts.append(n_o)
                scores.append(jnp.where(n_o > 0.0, -acc / softmin_temp, -jnp.inf))
            peak = scores[0]
            for s in scores[1:]:
                peak = jnp.maximum(peak, s)
            den = None
            num = None
            for o in range(NOFF):
                w = counts[o] * jnp.exp(scores[o] - peak)
                shift_norm = 2.0 * float(4 * o - REACH) / total_y
                den = w if den is None else den + w
                num = w * shift_norm if num is None else num + w * shift_norm
            o_ref[pl.ds(r0, 8), lanes] = num / den
        return carry

    lax.fori_loop(0, sum(hi - lo for lo, hi in tile_ranges), body, 0)
    if with_rows_beyond:
        lo = tile_ranges[0][1] * 8
        hi = tile_ranges[1][0] * 8
        o_ref[pl.ds(lo, hi - lo), :] = done_ref[pl.ds(lo, hi - lo), :]


def per_device(fixed_features, moving_features, cand_offsets, cand_lengths, smooth_radii):
    height = fixed_features.shape[0]
    columns_dev = fixed_features.shape[1] // CH
    blocks = height // 4
    total_y = height * lax.axis_size("gy")
    shifts = cand_offsets[:, 0, :]
    counts = cand_lengths[:, 0]
    live = jnp.arange(shifts.shape[1], dtype=jnp.int32)[None, :] < counts[:, None]
    offset_values = 4 * jnp.arange(NOFF, dtype=jnp.int32) - REACH
    hits = (shifts[:, :, None] == offset_values[None, None, :]) & live[:, :, None]
    mult = jnp.sum(hits.astype(jnp.float32), axis=1)
    mult_rows = jnp.repeat(mult.T, 4, axis=1)
    mult_rows = jnp.broadcast_to(mult_rows[:, :, None], (NOFF, height, 128))

    gy_count = lax.axis_size("gy")
    fixed_c = channel_major(fixed_features)
    moving_c = channel_major(moving_features)
    top_rows = lax.ppermute(
        moving_c[:, height - REACH :], "gy", [(i, i + 1) for i in range(gy_count - 1)]
    )
    bottom_rows = lax.ppermute(
        moving_c[:, :REACH], "gy", [(i + 1, i) for i in range(gy_count - 1)]
    )

    rows = height + 2 * REACH
    tiles = height // 8
    reach_tiles = REACH // 8
    scratch = [
        pltpu.VMEM((CH, height, columns_dev), jnp.float32),
        pltpu.VMEM((CH, rows, columns_dev), jnp.float32),
        pltpu.VMEM((CH, rows, columns_dev), jnp.float32),
    ]
    params = pltpu.CompilerParams(vmem_limit_bytes=60 * 1024 * 1024)
    out_shape = jax.ShapeDtypeStruct((height, columns_dev), jnp.float32)
    middle = pl.pallas_call(
        lambda *refs: softmin_kernel(total_y, [(reach_tiles, tiles - reach_tiles)], False, *refs),
        out_shape=out_shape,
        scratch_shapes=scratch,
        compiler_params=params,
    )(fixed_c, moving_c, mult_rows)
    disp_init = pl.pallas_call(
        lambda *refs: softmin_kernel(
            total_y, [(0, reach_tiles), (tiles - reach_tiles, tiles)], True, *refs
        ),
        out_shape=out_shape,
        scratch_shapes=scratch,
        compiler_params=params,
    )(
        fixed_c,
        moving_c,
        top_rows,
        bottom_rows,
        mult_rows,
        middle,
    )

    ext = exchange_halo(disp_init, HALO_Y, HALO_Z, SEND_Y, SEND_Z)
    rows_ext, lanes_ext = ext.shape
    row_global = lax.axis_index("gy") * height - HALO_Y + lax.broadcasted_iota(
        jnp.int32, (rows_ext, lanes_ext), 0
    )
    lane_global = lax.axis_index("gz") * columns_dev - HALO_Z + lax.broadcasted_iota(
        jnp.int32, (rows_ext, lanes_ext), 1
    )
    inside = (
        (row_global >= 0)
        & (row_global < total_y)
        & (lane_global >= 0)
        & (lane_global < columns_dev * lax.axis_size("gz"))
    )
    grid_mask = inside.astype(jnp.float32)
    final_ext = pl.pallas_call(
        adam_kernel,
        out_shape=jax.ShapeDtypeStruct((height, columns_dev), jnp.float32),
        in_specs=[
            pl.BlockSpec(memory_space=pltpu.SMEM),
            pl.BlockSpec(memory_space=pltpu.VMEM),
            pl.BlockSpec(memory_space=pltpu.VMEM),
        ],
        compiler_params=pltpu.CompilerParams(vmem_limit_bytes=32 * 1024 * 1024),
    )(smooth_radii.astype(jnp.int32), ext, grid_mask)
    return (disp_init, final_ext)


def solution(mesh):
    in_specs = (P("gy", "gz"), P("gy", "gz"), P("gy", "gz", None), P("gy", "gz"), P())
    out_specs = (P("gy", "gz"), P("gy", "gz"))
    return jax.shard_map(
        per_device, mesh=mesh, in_specs=in_specs, out_specs=out_specs, check_vma=False
    )
```

```python
import jax
import jax.numpy as jnp
from jax import lax
from jax.experimental import pallas as pl
from jax.experimental.pallas import tpu as pltpu
from jax.sharding import PartitionSpec as P

CH = 16
XS = 8
REACH = 32
RMAX = 4
ITERS = 3
NOFF = 2 * (REACH // 4) + 1


softmin_temp = 2.0
smooth_weight = 2.0
adam_rate = 0.2
beta_first = 0.9
beta_second = 0.999
adam_floor = 0.05


def with_halo(cells, sides, width):
    for axis, dim in sides:
        count = lax.axis_size(axis)
        ends = count - 1
        head = lax.slice_in_dim(cells, 0, width, axis=dim)
        tail = lax.slice_in_dim(cells, cells.shape[dim] - width, cells.shape[dim], axis=dim)
        cells = jnp.concatenate(
            [
                lax.ppermute(tail, axis, [(i, (i + 1) % count) for i in range(ends)]),
                cells,
                lax.ppermute(head, axis, [((i + 1) % count, i) for i in range(ends)]),
            ],
            axis=dim,
        )
    return cells


def box_weights(radius):
    spread = jnp.arange(-RMAX, RMAX + 1)
    inside = jnp.abs(spread) <= radius
    return jnp.where(inside, 1.0, 0.0).astype(jnp.float32) / (2 * radius + 1).astype(jnp.float32)


def smooth_inner(padded, radius, margin):
    weights = box_weights(radius)
    height = padded.shape[0] - 2 * margin
    layers = padded.shape[1] - 2 * margin
    depth_cells = padded.shape[2]
    along_y = jnp.zeros((height, padded.shape[1], depth_cells), jnp.float32)
    for offset in range(-RMAX, RMAX + 1):
        along_y = (
            along_y + weights[RMAX + offset] * padded[margin + offset : margin + offset + height]
        )
    along_z = jnp.zeros((height, layers, depth_cells), jnp.float32)
    for offset in range(-RMAX, RMAX + 1):
        along_z = (
            along_z
            + weights[RMAX + offset] * along_y[:, margin + offset : margin + offset + layers]
        )
    x_padded = jnp.pad(along_z, ((0, 0), (0, 0), (RMAX, RMAX)))
    along_x = jnp.zeros((height, layers, depth_cells), jnp.float32)
    for offset in range(-RMAX, RMAX + 1):
        along_x = (
            along_x
            + weights[RMAX + offset] * x_padded[:, :, RMAX + offset : RMAX + offset + depth_cells]
        )
    return along_x


def adam_update(field, target_field, smoothed, first_moment, second_moment, iteration):
    gradient = field - target_field + smooth_weight * (field - smoothed)
    first_moment = beta_first * first_moment + (1.0 - beta_first) * gradient
    second_moment = beta_second * second_moment + (1.0 - beta_second) * gradient * gradient
    first_hat = first_moment / (1.0 - beta_first ** (iteration + 1))
    second_hat = second_moment / (1.0 - beta_second ** (iteration + 1))
    field = field - adam_rate * first_hat / (jnp.sqrt(second_hat) + adam_floor)
    return (field, first_moment, second_moment)


HALO_Y = 8
HALO_Z = 8 * XS
EXT_ROWS = HALO_Y
SEND_Y = 8
SEND_Z = 8 * XS


def exchange_halo(cells, wy, wz, send_y, send_z):
    ny = lax.axis_size("gy")
    nz = lax.axis_size("gz")
    top = lax.ppermute(cells[-send_y:], "gy", [(i, i + 1) for i in range(ny - 1)])
    bottom = lax.ppermute(cells[:send_y], "gy", [(i + 1, i) for i in range(ny - 1)])
    cells = jnp.concatenate([top, cells, bottom], axis=0)
    left = lax.ppermute(cells[:, -send_z:], "gz", [(i, i + 1) for i in range(nz - 1)])
    right = lax.ppermute(cells[:, :send_z], "gz", [(i + 1, i) for i in range(nz - 1)])
    cells = jnp.concatenate([left, cells, right], axis=1)
    return jnp.pad(cells, ((wy - send_y, wy - send_y), (wz - send_z, wz - send_z)))


def shifted(a, offset, axis):
    if offset == 0:
        return a
    return pltpu.roll(a, (-offset) % a.shape[axis], axis)


def box_smooth(u, radius, lane_x):
    scale = 1.0 / float(2 * radius + 1)
    along_y = u
    for o in range(1, radius + 1):
        along_y = along_y + shifted(u, -o, 0) + shifted(u, o, 0)
    along_y = along_y * scale
    along_z = along_y
    for o in range(1, radius + 1):
        along_z = along_z + shifted(along_y, -XS * o, 1) + shifted(along_y, XS * o, 1)
    along_z = along_z * scale
    along_x = along_z
    for o in range(1, radius + 1):
        along_x = (
            along_x
            + jnp.where(lane_x >= o, shifted(along_z, -o, 1), 0.0)
            + jnp.where(lane_x < XS - o, shifted(along_z, o, 1), 0.0)
        )
    return along_x * scale


def adam_kernel(radii_ref, d_ref, mask_ref, o_ref):
    target = d_ref[...]
    inside = mask_ref[...] > 0.0
    lane_x = lax.broadcasted_iota(jnp.int32, target.shape, 1) % XS
    field = jnp.where(inside, target, 0.0)
    first_moment = jnp.zeros_like(target)
    second_moment = jnp.zeros_like(target)
    for iteration in range(ITERS):
        radius = radii_ref[iteration]
        smoothed = lax.switch(
            jnp.clip(radius - 1, 0, RMAX - 1),
            [lambda u, r=r: box_smooth(u, r, lane_x) for r in range(1, RMAX + 1)],
            field,
        )
        field, first_moment, second_moment = adam_update(
            field, target, smoothed, first_moment, second_moment, iteration
        )
        field = jnp.where(inside, field, 0.0)
    height = o_ref.shape[0]
    width = o_ref.shape[1]
    o_ref[...] = field[HALO_Y : HALO_Y + height, HALO_Z : HALO_Z + width]


def transpose_kernel(x_ref, o_ref, s_ref):
    chunk = 128 * CH
    for j in range(x_ref.shape[1] // chunk):
        s_ref[...] = x_ref[:, pl.ds(chunk * j, chunk)].astype(jnp.float32).T
        for c in range(CH):
            cols = s_ref[pl.ds(c, 128, stride=CH), :]
            o_ref[c, :, pl.ds(128 * j, 128)] = cols.T.astype(o_ref.dtype)


def channel_major(x):
    rows, lanes = x.shape
    return pl.pallas_call(
        transpose_kernel,
        out_shape=jax.ShapeDtypeStruct((CH, rows, lanes // CH), x.dtype),
        scratch_shapes=[pltpu.VMEM((128 * CH, rows), jnp.float32)],
    )(x)


def softmin_tiles(total_y, f_ref, m0_ref, m4_ref, n_ref, o_ref, tile_ranges):
    lanes_total = f_ref.shape[2]

    def body(i, carry):
        t = i
        for lo, hi in tile_ranges[1:]:
            t = jnp.where(t >= tile_ranges[0][1], t - tile_ranges[0][1] + lo, t)
        t = t + tile_ranges[0][0]
        r0 = pl.multiple_of(t * 8, 8)
        for j in range(lanes_total // 128):
            lanes = pl.ds(128 * j, 128)
            fixed = [f_ref[c, pl.ds(r0, 8), lanes] for c in range(CH)]
            scores = []
            counts = []
            for o in range(NOFF):
                shift = 4 * o
                if shift % 8 == 0:
                    src, base = m0_ref, shift
                else:
                    src, base = m4_ref, shift - 4
                acc = None
                for c in range(CH):
                    d = fixed[c] - src[c, pl.ds(r0 + base, 8), lanes]
                    acc = d * d if acc is None else acc + d * d
                n_o = n_ref[o, pl.ds(r0, 8), :]
                counts.append(n_o)
                scores.append(jnp.where(n_o > 0.0, -acc / softmin_temp, -jnp.inf))
            peak = scores[0]
            for s in scores[1:]:
                peak = jnp.maximum(peak, s)
            den = None
            num = None
            for o in range(NOFF):
                w = counts[o] * jnp.exp(scores[o] - peak)
                shift_norm = 2.0 * float(4 * o - REACH) / total_y
                den = w if den is None else den + w
                num = w * shift_norm if num is None else num + w * shift_norm
            o_ref[pl.ds(r0, 8), lanes] = jnp.where(den > 0.0, num / den, 0.0)
        return carry

    lax.fori_loop(0, sum(hi - lo for lo, hi in tile_ranges), body, 0)


def build_shifted(m0_ref, m4_ref):
    rows = m0_ref.shape[1]

    def step(c, carry):
        m4_ref[c, pl.ds(0, rows - 8), :] = m0_ref[c, pl.ds(4, rows - 8), :]
        m4_ref[c, pl.ds(rows - 8, 8), :] = jnp.zeros((8, m0_ref.shape[2]), jnp.float32)
        return carry

    lax.fori_loop(0, CH, step, 0)


def softmin_middle_kernel(total_y, ft_ref, mt_ref, n_ref, o_ref, f_ref, m0_ref, m4_ref):
    height = ft_ref.shape[1]
    lanes_total = ft_ref.shape[2]

    def build(c, carry):
        f_ref[c] = ft_ref[c].astype(jnp.float32)
        m0_ref[c, pl.ds(REACH, height), :] = mt_ref[c].astype(jnp.float32)
        m0_ref[c, pl.ds(0, REACH), :] = jnp.zeros((REACH, lanes_total), jnp.float32)
        m0_ref[c, pl.ds(REACH + height, REACH), :] = jnp.zeros((REACH, lanes_total), jnp.float32)
        return carry

    lax.fori_loop(0, CH, build, 0)
    build_shifted(m0_ref, m4_ref)
    tiles = height // 8
    softmin_tiles(
        total_y, f_ref, m0_ref, m4_ref, n_ref, o_ref, [(REACH // 8, tiles - REACH // 8)]
    )


def softmin_edge_kernel(
    total_y, ft_ref, mt_ref, top_ref, bot_ref, n_ref, done_ref, ext_ref, o_ref, f_ref, m0_ref, m4_ref
):
    height = ft_ref.shape[1]
    reach_rows = REACH + EXT_ROWS

    def build(c, carry):
        top = top_ref[c].astype(jnp.float32)
        bot = bot_ref[c].astype(jnp.float32)
        f_ref[c, pl.ds(0, EXT_ROWS), :] = top[reach_rows : reach_rows + EXT_ROWS]
        f_ref[c, pl.ds(EXT_ROWS, height), :] = ft_ref[c].astype(jnp.float32)
        f_ref[c, pl.ds(EXT_ROWS + height, EXT_ROWS), :] = bot[reach_rows : reach_rows + EXT_ROWS]
        m0_ref[c, pl.ds(0, reach_rows), :] = top[:reach_rows]
        m0_ref[c, pl.ds(reach_rows, height), :] = mt_ref[c].astype(jnp.float32)
        m0_ref[c, pl.ds(reach_rows + height, reach_rows), :] = bot[:reach_rows]
        return carry

    lax.fori_loop(0, CH, build, 0)
    build_shifted(m0_ref, m4_ref)
    tiles = (height + 2 * EXT_ROWS) // 8
    edge = reach_rows // 8
    softmin_tiles(total_y, f_ref, m0_ref, m4_ref, n_ref, ext_ref, [(0, edge), (tiles - edge, tiles)])
    ext_ref[pl.ds(reach_rows, height - 2 * REACH), :] = done_ref[pl.ds(REACH, height - 2 * REACH), :]
    o_ref[...] = ext_ref[pl.ds(EXT_ROWS, height), :]


def per_device(fixed_features, moving_features, cand_offsets, cand_lengths, smooth_radii):
    height = fixed_features.shape[0]
    columns_dev = fixed_features.shape[1] // CH
    blocks = height // 4
    total_y = height * lax.axis_size("gy")
    shifts = cand_offsets[:, 0, :]
    counts = cand_lengths[:, 0]
    live = jnp.arange(shifts.shape[1], dtype=jnp.int32)[None, :] < counts[:, None]
    offset_values = 4 * jnp.arange(NOFF, dtype=jnp.int32) - REACH
    hits = (shifts[:, :, None] == offset_values[None, None, :]) & live[:, :, None]
    mult = jnp.sum(hits.astype(jnp.float32), axis=1)
    mult_rows = jnp.repeat(mult.T, 4, axis=1)
    lanes_n = 128

    gy_count = lax.axis_size("gy")
    fixed_c = channel_major(fixed_features)
    moving_c = channel_major(moving_features)
    reach_rows = REACH + EXT_ROWS

    def payload(moving_part, fixed_part, mult_part):
        counts_part = jnp.pad(mult_part.T, ((0, 0), (0, columns_dev - NOFF)))
        counts_part = jnp.zeros((CH, EXT_ROWS, columns_dev), jnp.float32).at[0].set(counts_part)
        return jnp.concatenate(
            [moving_part, fixed_part, counts_part.astype(moving_part.dtype)], axis=1
        )

    down = payload(
        moving_c[:, height - reach_rows :],
        fixed_c[:, height - EXT_ROWS :],
        mult_rows[:, height - EXT_ROWS :],
    )
    up = payload(moving_c[:, :reach_rows], fixed_c[:, :EXT_ROWS], mult_rows[:, :EXT_ROWS])
    top = lax.ppermute(down, "gy", [(i, i + 1) for i in range(gy_count - 1)])
    bottom = lax.ppermute(up, "gy", [(i + 1, i) for i in range(gy_count - 1)])

    rows = height + 2 * REACH
    scratch = [
        pltpu.VMEM((CH, height, columns_dev), jnp.float32),
        pltpu.VMEM((CH, rows, columns_dev), jnp.float32),
        pltpu.VMEM((CH, rows, columns_dev), jnp.float32),
    ]
    params = pltpu.CompilerParams(vmem_limit_bytes=60 * 1024 * 1024)
    out_shape = jax.ShapeDtypeStruct((height, columns_dev), jnp.float32)
    middle = pl.pallas_call(
        lambda *refs: softmin_middle_kernel(total_y, *refs),
        out_shape=out_shape,
        scratch_shapes=scratch,
        compiler_params=params,
    )(fixed_c, moving_c, jnp.broadcast_to(mult_rows[:, :, None], (NOFF, height, lanes_n)))

    def counts_of(part):
        return part[0, reach_rows + EXT_ROWS :, :NOFF].astype(jnp.float32).T

    mult_ext = jnp.concatenate([counts_of(top), mult_rows, counts_of(bottom)], axis=1)
    frame = height + 2 * EXT_ROWS
    edge_scratch = [
        pltpu.VMEM((CH, frame, columns_dev), jnp.float32),
        pltpu.VMEM((CH, frame + 2 * REACH, columns_dev), jnp.float32),
        pltpu.VMEM((CH, frame + 2 * REACH, columns_dev), jnp.float32),
    ]
    ext_y, disp_init = pl.pallas_call(
        lambda *refs: softmin_edge_kernel(total_y, *refs),
        out_shape=(jax.ShapeDtypeStruct((frame, columns_dev), jnp.float32), out_shape),
        scratch_shapes=edge_scratch,
        compiler_params=params,
    )(
        fixed_c,
        moving_c,
        top,
        bottom,
        jnp.broadcast_to(mult_ext[:, :, None], (NOFF, frame, lanes_n)),
        middle,
    )

    gz_count = lax.axis_size("gz")
    left = lax.ppermute(ext_y[:, -HALO_Z:], "gz", [(i, i + 1) for i in range(gz_count - 1)])
    right = lax.ppermute(ext_y[:, :HALO_Z], "gz", [(i + 1, i) for i in range(gz_count - 1)])
    ext = jnp.concatenate([left, ext_y, right], axis=1)
    rows_ext, lanes_ext = ext.shape
    row_global = lax.axis_index("gy") * height - HALO_Y + lax.broadcasted_iota(
        jnp.int32, (rows_ext, lanes_ext), 0
    )
    lane_global = lax.axis_index("gz") * columns_dev - HALO_Z + lax.broadcasted_iota(
        jnp.int32, (rows_ext, lanes_ext), 1
    )
    inside = (
        (row_global >= 0)
        & (row_global < total_y)
        & (lane_global >= 0)
        & (lane_global < columns_dev * lax.axis_size("gz"))
    )
    grid_mask = inside.astype(jnp.float32)
    final_ext = pl.pallas_call(
        adam_kernel,
        out_shape=jax.ShapeDtypeStruct((height, columns_dev), jnp.float32),
        in_specs=[
            pl.BlockSpec(memory_space=pltpu.SMEM),
            pl.BlockSpec(memory_space=pltpu.VMEM),
            pl.BlockSpec(memory_space=pltpu.VMEM),
        ],
        compiler_params=pltpu.CompilerParams(vmem_limit_bytes=32 * 1024 * 1024),
    )(smooth_radii.astype(jnp.int32), ext, grid_mask)
    return (disp_init, final_ext)


def solution(mesh):
    in_specs = (P("gy", "gz"), P("gy", "gz"), P("gy", "gz", None), P("gy", "gz"), P())
    out_specs = (P("gy", "gz"), P("gy", "gz"))
    return jax.shard_map(
        per_device, mesh=mesh, in_specs=in_specs, out_specs=out_specs, check_vma=False
    )
```

```python
import jax
import jax.numpy as jnp
from jax import lax
from jax.experimental import pallas as pl
from jax.experimental.pallas import tpu as pltpu
from jax.sharding import PartitionSpec as P

CH = 16
XS = 8
REACH = 32
RMAX = 4
ITERS = 3
NOFF = 2 * (REACH // 4) + 1


softmin_temp = 2.0
smooth_weight = 2.0
adam_rate = 0.2
beta_first = 0.9
beta_second = 0.999
adam_floor = 0.05


def with_halo(cells, sides, width):
    for axis, dim in sides:
        count = lax.axis_size(axis)
        ends = count - 1
        head = lax.slice_in_dim(cells, 0, width, axis=dim)
        tail = lax.slice_in_dim(cells, cells.shape[dim] - width, cells.shape[dim], axis=dim)
        cells = jnp.concatenate(
            [
                lax.ppermute(tail, axis, [(i, (i + 1) % count) for i in range(ends)]),
                cells,
                lax.ppermute(head, axis, [((i + 1) % count, i) for i in range(ends)]),
            ],
            axis=dim,
        )
    return cells


def box_weights(radius):
    spread = jnp.arange(-RMAX, RMAX + 1)
    inside = jnp.abs(spread) <= radius
    return jnp.where(inside, 1.0, 0.0).astype(jnp.float32) / (2 * radius + 1).astype(jnp.float32)


def smooth_inner(padded, radius, margin):
    weights = box_weights(radius)
    height = padded.shape[0] - 2 * margin
    layers = padded.shape[1] - 2 * margin
    depth_cells = padded.shape[2]
    along_y = jnp.zeros((height, padded.shape[1], depth_cells), jnp.float32)
    for offset in range(-RMAX, RMAX + 1):
        along_y = (
            along_y + weights[RMAX + offset] * padded[margin + offset : margin + offset + height]
        )
    along_z = jnp.zeros((height, layers, depth_cells), jnp.float32)
    for offset in range(-RMAX, RMAX + 1):
        along_z = (
            along_z
            + weights[RMAX + offset] * along_y[:, margin + offset : margin + offset + layers]
        )
    x_padded = jnp.pad(along_z, ((0, 0), (0, 0), (RMAX, RMAX)))
    along_x = jnp.zeros((height, layers, depth_cells), jnp.float32)
    for offset in range(-RMAX, RMAX + 1):
        along_x = (
            along_x
            + weights[RMAX + offset] * x_padded[:, :, RMAX + offset : RMAX + offset + depth_cells]
        )
    return along_x


def adam_update(field, target_field, smoothed, first_moment, second_moment, iteration):
    gradient = field - target_field + smooth_weight * (field - smoothed)
    first_moment = beta_first * first_moment + (1.0 - beta_first) * gradient
    second_moment = beta_second * second_moment + (1.0 - beta_second) * gradient * gradient
    first_hat = first_moment / (1.0 - beta_first ** (iteration + 1))
    second_hat = second_moment / (1.0 - beta_second ** (iteration + 1))
    field = field - adam_rate * first_hat / (jnp.sqrt(second_hat) + adam_floor)
    return (field, first_moment, second_moment)


HALO_Y = 8
HALO_Z = 8 * XS
SEND_Y = 8
SEND_Z = 8 * XS


def exchange_halo(cells, wy, wz, send_y, send_z):
    ny = lax.axis_size("gy")
    nz = lax.axis_size("gz")
    top = lax.ppermute(cells[-send_y:], "gy", [(i, i + 1) for i in range(ny - 1)])
    bottom = lax.ppermute(cells[:send_y], "gy", [(i + 1, i) for i in range(ny - 1)])
    cells = jnp.concatenate([top, cells, bottom], axis=0)
    left = lax.ppermute(cells[:, -send_z:], "gz", [(i, i + 1) for i in range(nz - 1)])
    right = lax.ppermute(cells[:, :send_z], "gz", [(i + 1, i) for i in range(nz - 1)])
    cells = jnp.concatenate([left, cells, right], axis=1)
    return jnp.pad(cells, ((wy - send_y, wy - send_y), (wz - send_z, wz - send_z)))


def shifted(a, offset, axis):
    if offset == 0:
        return a
    return pltpu.roll(a, (-offset) % a.shape[axis], axis)


def box_smooth(u, radius, lane_x):
    scale = 1.0 / float(2 * radius + 1)
    along_y = u
    for o in range(1, radius + 1):
        along_y = along_y + shifted(u, -o, 0) + shifted(u, o, 0)
    along_y = along_y * scale
    along_z = along_y
    for o in range(1, radius + 1):
        along_z = along_z + shifted(along_y, -XS * o, 1) + shifted(along_y, XS * o, 1)
    along_z = along_z * scale
    along_x = along_z
    for o in range(1, radius + 1):
        along_x = (
            along_x
            + jnp.where(lane_x >= o, shifted(along_z, -o, 1), 0.0)
            + jnp.where(lane_x < XS - o, shifted(along_z, o, 1), 0.0)
        )
    return along_x * scale


def adam_kernel(radii_ref, d_ref, mask_ref, o_ref):
    target = d_ref[...]
    inside = mask_ref[...] > 0.0
    lane_x = lax.broadcasted_iota(jnp.int32, target.shape, 1) % XS
    field = jnp.where(inside, target, 0.0)
    first_moment = jnp.zeros_like(target)
    second_moment = jnp.zeros_like(target)
    for iteration in range(ITERS):
        radius = radii_ref[iteration]
        smoothed = lax.switch(
            jnp.clip(radius - 1, 0, RMAX - 1),
            [lambda u, r=r: box_smooth(u, r, lane_x) for r in range(1, RMAX + 1)],
            field,
        )
        field, first_moment, second_moment = adam_update(
            field, target, smoothed, first_moment, second_moment, iteration
        )
        field = jnp.where(inside, field, 0.0)
    height = o_ref.shape[0]
    width = o_ref.shape[1]
    o_ref[...] = field[HALO_Y : HALO_Y + height, HALO_Z : HALO_Z + width]


def transpose_kernel(x_ref, o_ref, s_ref):
    chunk = 128 * CH
    for j in range(x_ref.shape[1] // chunk):
        s_ref[...] = x_ref[:, pl.ds(chunk * j, chunk)].astype(jnp.float32).T
        for c in range(CH):
            cols = s_ref[pl.ds(c, 128, stride=CH), :]
            o_ref[c, :, pl.ds(128 * j, 128)] = cols.T.astype(o_ref.dtype)


def channel_major(x):
    rows, lanes = x.shape
    return pl.pallas_call(
        transpose_kernel,
        out_shape=jax.ShapeDtypeStruct((CH, rows, lanes // CH), x.dtype),
        scratch_shapes=[pltpu.VMEM((128 * CH, rows), jnp.float32)],
    )(x)


def softmin_tiles(total_y, f_ref, m0_ref, m4_ref, n_ref, o_ref, first, last):
    lanes_total = f_ref.shape[2]

    def body(t, carry):
        r0 = pl.multiple_of(t * 8, 8)
        for j in range(lanes_total // 128):
            peak, den, num = offset_partial(
                total_y, f_ref, m0_ref, m4_ref, n_ref, r0, range(NOFF), pl.ds(128 * j, 128)
            )
            o_ref[pl.ds(r0, 8), pl.ds(128 * j, 128)] = num / den
        return carry

    lax.fori_loop(first, last, body, 0)


def offset_partial(total_y, f_ref, m0_ref, m4_ref, n_ref, r0, offsets, lanes):
    fixed = [f_ref[c, pl.ds(r0, 8), lanes] for c in range(CH)]
    scores = []
    counts = []
    for o in offsets:
        shift = 4 * o
        if shift % 8 == 0:
            src, base = m0_ref, shift
        else:
            src, base = m4_ref, shift - 4
        acc = None
        for c in range(CH):
            d = fixed[c] - src[c, pl.ds(r0 + base, 8), lanes]
            acc = d * d if acc is None else acc + d * d
        n_o = n_ref[o, pl.ds(r0, 8), :]
        counts.append(n_o)
        scores.append(jnp.where(n_o > 0.0, -acc / softmin_temp, -jnp.inf))
    peak = scores[0]
    for s in scores[1:]:
        peak = jnp.maximum(peak, s)
    base_score = jnp.where(peak == -jnp.inf, 0.0, peak)
    den = None
    num = None
    for o, s, n_o in zip(offsets, scores, counts):
        w = n_o * jnp.exp(s - base_score)
        shift_norm = 2.0 * float(4 * o - REACH) / total_y
        den = w if den is None else den + w
        num = w * shift_norm if num is None else num + w * shift_norm
    return peak, den, num


def edge_tiles(height):
    reach_tiles = REACH // 8
    return list(range(reach_tiles)) + list(range(height // 8 - reach_tiles, height // 8))


def halo_offsets(t, height):
    return [o for o in range(NOFF) if 8 * t + 4 * o < REACH or 8 * t + 4 * o + 8 > height + REACH]


def softmin_middle_kernel(total_y, ft_ref, mt_ref, n_ref, o_ref, pk_ref, dn_ref, nm_ref, f_ref, m0_ref, m4_ref):
    height = ft_ref.shape[1]
    lanes_total = ft_ref.shape[2]
    rows = height + 2 * REACH

    def build(c, carry):
        f_ref[c] = ft_ref[c].astype(jnp.float32)
        m0_ref[c, pl.ds(REACH, height), :] = mt_ref[c].astype(jnp.float32)
        m0_ref[c, pl.ds(0, REACH), :] = jnp.zeros((REACH, lanes_total), jnp.float32)
        m0_ref[c, pl.ds(REACH + height, REACH), :] = jnp.zeros((REACH, lanes_total), jnp.float32)
        m4_ref[c, pl.ds(0, rows - 8), :] = m0_ref[c, pl.ds(4, rows - 8), :]
        m4_ref[c, pl.ds(rows - 8, 8), :] = jnp.zeros((8, lanes_total), jnp.float32)
        return carry

    lax.fori_loop(0, CH, build, 0)
    tiles = height // 8
    softmin_tiles(total_y, f_ref, m0_ref, m4_ref, n_ref, o_ref, REACH // 8, tiles - REACH // 8)
    for t in edge_tiles(height):
        beyond = halo_offsets(t, height)
        inner = [o for o in range(NOFF) if o not in beyond]

        def part(j, carry, t=t, inner=inner):
            lanes = pl.ds(pl.multiple_of(j * 128, 128), 128)
            peak, den, num = offset_partial(
                total_y, f_ref, m0_ref, m4_ref, n_ref, 8 * t, inner, lanes
            )
            pk_ref[pl.ds(8 * t, 8), lanes] = peak
            dn_ref[pl.ds(8 * t, 8), lanes] = den
            nm_ref[pl.ds(8 * t, 8), lanes] = num
            return carry

        lax.fori_loop(0, lanes_total // 128, part, 0)


def softmin_edge_kernel(
    total_y, ft_ref, mt_ref, top_ref, bot_ref, n_ref, done_ref, pk_ref, dn_ref, nm_ref,
    o_ref, f_ref, m0_ref, m4_ref,
):
    height = ft_ref.shape[1]
    lanes_total = ft_ref.shape[2]
    rows = height + 2 * REACH
    span = REACH + 16

    def build(c, carry):
        f_ref[c, pl.ds(0, REACH), :] = ft_ref[c, pl.ds(0, REACH), :].astype(jnp.float32)
        f_ref[c, pl.ds(height - REACH, REACH), :] = ft_ref[c, pl.ds(height - REACH, REACH), :].astype(
            jnp.float32
        )
        m0_ref[c, pl.ds(0, REACH), :] = top_ref[c].astype(jnp.float32)
        m0_ref[c, pl.ds(REACH, 16), :] = mt_ref[c, pl.ds(0, 16), :].astype(jnp.float32)
        m0_ref[c, pl.ds(rows - span, 16), :] = mt_ref[c, pl.ds(height - 16, 16), :].astype(jnp.float32)
        m0_ref[c, pl.ds(rows - REACH, REACH), :] = bot_ref[c].astype(jnp.float32)
        m4_ref[c, pl.ds(0, span - 8), :] = m0_ref[c, pl.ds(4, span - 8), :]
        m4_ref[c, pl.ds(rows - span, span - 8), :] = m0_ref[c, pl.ds(rows - span + 4, span - 8), :]
        m4_ref[c, pl.ds(rows - 8, 8), :] = jnp.zeros((8, lanes_total), jnp.float32)
        return carry

    lax.fori_loop(0, CH, build, 0)
    for t in edge_tiles(height):
        beyond = halo_offsets(t, height)

        def part(j, carry, t=t, beyond=beyond):
            lanes = pl.ds(pl.multiple_of(j * 128, 128), 128)
            rows_t = pl.ds(8 * t, 8)
            peak, den, num = offset_partial(
                total_y, f_ref, m0_ref, m4_ref, n_ref, 8 * t, beyond, lanes
            )
            peak_in = pk_ref[rows_t, lanes]
            top_score = jnp.maximum(peak, peak_in)
            scale = jnp.exp(peak - top_score)
            scale_in = jnp.exp(peak_in - top_score)
            den = den * scale + dn_ref[rows_t, lanes] * scale_in
            num = num * scale + nm_ref[rows_t, lanes] * scale_in
            o_ref[rows_t, lanes] = num / den
            return carry

        lax.fori_loop(0, lanes_total // 128, part, 0)
    middle_rows = pl.ds(REACH, height - 2 * REACH)
    o_ref[middle_rows, :] = done_ref[middle_rows, :]


def per_device(fixed_features, moving_features, cand_offsets, cand_lengths, smooth_radii):
    height = fixed_features.shape[0]
    columns_dev = fixed_features.shape[1] // CH
    blocks = height // 4
    total_y = height * lax.axis_size("gy")
    shifts = cand_offsets[:, 0, :]
    counts = cand_lengths[:, 0]
    live = jnp.arange(shifts.shape[1], dtype=jnp.int32)[None, :] < counts[:, None]
    offset_values = 4 * jnp.arange(NOFF, dtype=jnp.int32) - REACH
    hits = (shifts[:, :, None] == offset_values[None, None, :]) & live[:, :, None]
    mult = jnp.sum(hits.astype(jnp.float32), axis=1)
    mult_rows = jnp.repeat(mult.T, 4, axis=1)

    gy_count = lax.axis_size("gy")
    fixed_c = channel_major(fixed_features)
    moving_c = channel_major(moving_features)
    top_rows = lax.ppermute(
        moving_c[:, height - REACH :], "gy", [(i, i + 1) for i in range(gy_count - 1)]
    )
    bottom_rows = lax.ppermute(
        moving_c[:, :REACH], "gy", [(i + 1, i) for i in range(gy_count - 1)]
    )

    rows = height + 2 * REACH
    tiles = height // 8
    reach_tiles = REACH // 8
    scratch = [
        pltpu.VMEM((CH, height, columns_dev), jnp.float32),
        pltpu.VMEM((CH, rows, columns_dev), jnp.float32),
        pltpu.VMEM((CH, rows, columns_dev), jnp.float32),
    ]
    params = pltpu.CompilerParams(vmem_limit_bytes=60 * 1024 * 1024)
    out_shape = jax.ShapeDtypeStruct((height, columns_dev), jnp.float32)
    n_lanes = jnp.broadcast_to(mult_rows[:, :, None], (NOFF, height, 128))
    middle, peak_part, den_part, num_part = pl.pallas_call(
        lambda *refs: softmin_middle_kernel(total_y, *refs),
        out_shape=(out_shape, out_shape, out_shape, out_shape),
        scratch_shapes=scratch,
        compiler_params=params,
    )(fixed_c, moving_c, n_lanes)
    disp_init = pl.pallas_call(
        lambda *refs: softmin_edge_kernel(total_y, *refs),
        out_shape=out_shape,
        scratch_shapes=scratch,
        compiler_params=params,
    )(
        fixed_c,
        moving_c,
        top_rows,
        bottom_rows,
        n_lanes,
        middle,
        peak_part,
        den_part,
        num_part,
    )

    ext = exchange_halo(disp_init, HALO_Y, HALO_Z, SEND_Y, SEND_Z)
    rows_ext, lanes_ext = ext.shape
    row_global = lax.axis_index("gy") * height - HALO_Y + lax.broadcasted_iota(
        jnp.int32, (rows_ext, lanes_ext), 0
    )
    lane_global = lax.axis_index("gz") * columns_dev - HALO_Z + lax.broadcasted_iota(
        jnp.int32, (rows_ext, lanes_ext), 1
    )
    inside = (
        (row_global >= 0)
        & (row_global < total_y)
        & (lane_global >= 0)
        & (lane_global < columns_dev * lax.axis_size("gz"))
    )
    grid_mask = inside.astype(jnp.float32)
    final_ext = pl.pallas_call(
        adam_kernel,
        out_shape=jax.ShapeDtypeStruct((height, columns_dev), jnp.float32),
        in_specs=[
            pl.BlockSpec(memory_space=pltpu.SMEM),
            pl.BlockSpec(memory_space=pltpu.VMEM),
            pl.BlockSpec(memory_space=pltpu.VMEM),
        ],
        compiler_params=pltpu.CompilerParams(vmem_limit_bytes=32 * 1024 * 1024),
    )(smooth_radii.astype(jnp.int32), ext, grid_mask)
    return (disp_init, final_ext)


def solution(mesh):
    in_specs = (P("gy", "gz"), P("gy", "gz"), P("gy", "gz", None), P("gy", "gz"), P())
    out_specs = (P("gy", "gz"), P("gy", "gz"))
    return jax.shard_map(
        per_device, mesh=mesh, in_specs=in_specs, out_specs=out_specs, check_vma=False
    )
```

```python
import jax
import jax.numpy as jnp
from jax import lax
from jax.experimental import pallas as pl
from jax.experimental.pallas import tpu as pltpu
from jax.sharding import PartitionSpec as P

CH = 16
XS = 8
REACH = 32
RMAX = 4
ITERS = 3
NOFF = 2 * (REACH // 4) + 1


softmin_temp = 2.0
smooth_weight = 2.0
adam_rate = 0.2
beta_first = 0.9
beta_second = 0.999
adam_floor = 0.05


def with_halo(cells, sides, width):
    for axis, dim in sides:
        count = lax.axis_size(axis)
        ends = count - 1
        head = lax.slice_in_dim(cells, 0, width, axis=dim)
        tail = lax.slice_in_dim(cells, cells.shape[dim] - width, cells.shape[dim], axis=dim)
        cells = jnp.concatenate(
            [
                lax.ppermute(tail, axis, [(i, (i + 1) % count) for i in range(ends)]),
                cells,
                lax.ppermute(head, axis, [((i + 1) % count, i) for i in range(ends)]),
            ],
            axis=dim,
        )
    return cells


def box_weights(radius):
    spread = jnp.arange(-RMAX, RMAX + 1)
    inside = jnp.abs(spread) <= radius
    return jnp.where(inside, 1.0, 0.0).astype(jnp.float32) / (2 * radius + 1).astype(jnp.float32)


def smooth_inner(padded, radius, margin):
    weights = box_weights(radius)
    height = padded.shape[0] - 2 * margin
    layers = padded.shape[1] - 2 * margin
    depth_cells = padded.shape[2]
    along_y = jnp.zeros((height, padded.shape[1], depth_cells), jnp.float32)
    for offset in range(-RMAX, RMAX + 1):
        along_y = (
            along_y + weights[RMAX + offset] * padded[margin + offset : margin + offset + height]
        )
    along_z = jnp.zeros((height, layers, depth_cells), jnp.float32)
    for offset in range(-RMAX, RMAX + 1):
        along_z = (
            along_z
            + weights[RMAX + offset] * along_y[:, margin + offset : margin + offset + layers]
        )
    x_padded = jnp.pad(along_z, ((0, 0), (0, 0), (RMAX, RMAX)))
    along_x = jnp.zeros((height, layers, depth_cells), jnp.float32)
    for offset in range(-RMAX, RMAX + 1):
        along_x = (
            along_x
            + weights[RMAX + offset] * x_padded[:, :, RMAX + offset : RMAX + offset + depth_cells]
        )
    return along_x


def adam_update(field, target_field, smoothed, first_moment, second_moment, iteration):
    gradient = field - target_field + smooth_weight * (field - smoothed)
    first_moment = beta_first * first_moment + (1.0 - beta_first) * gradient
    second_moment = beta_second * second_moment + (1.0 - beta_second) * gradient * gradient
    first_hat = first_moment / (1.0 - beta_first ** (iteration + 1))
    second_hat = second_moment / (1.0 - beta_second ** (iteration + 1))
    field = field - adam_rate * first_hat / (jnp.sqrt(second_hat) + adam_floor)
    return (field, first_moment, second_moment)


HALO_Y = 8
HALO_Z = 8 * XS
SEND_Y = 8
SEND_Z = 8 * XS


def exchange_halo(cells, wy, wz, send_y, send_z):
    ny = lax.axis_size("gy")
    nz = lax.axis_size("gz")
    top = lax.ppermute(cells[-send_y:], "gy", [(i, i + 1) for i in range(ny - 1)])
    bottom = lax.ppermute(cells[:send_y], "gy", [(i + 1, i) for i in range(ny - 1)])
    cells = jnp.concatenate([top, cells, bottom], axis=0)
    left = lax.ppermute(cells[:, -send_z:], "gz", [(i, i + 1) for i in range(nz - 1)])
    right = lax.ppermute(cells[:, :send_z], "gz", [(i + 1, i) for i in range(nz - 1)])
    cells = jnp.concatenate([left, cells, right], axis=1)
    return jnp.pad(cells, ((wy - send_y, wy - send_y), (wz - send_z, wz - send_z)))


def shifted(a, offset, axis):
    if offset == 0:
        return a
    return pltpu.roll(a, (-offset) % a.shape[axis], axis)


def box_smooth(u, radius, lane_x):
    scale = 1.0 / float(2 * radius + 1)
    along_y = u
    for o in range(1, radius + 1):
        along_y = along_y + shifted(u, -o, 0) + shifted(u, o, 0)
    along_y = along_y * scale
    along_z = along_y
    for o in range(1, radius + 1):
        along_z = along_z + shifted(along_y, -XS * o, 1) + shifted(along_y, XS * o, 1)
    along_z = along_z * scale
    along_x = along_z
    for o in range(1, radius + 1):
        along_x = (
            along_x
            + jnp.where(lane_x >= o, shifted(along_z, -o, 1), 0.0)
            + jnp.where(lane_x < XS - o, shifted(along_z, o, 1), 0.0)
        )
    return along_x * scale


def adam_kernel(radii_ref, d_ref, mask_ref, o_ref):
    target = d_ref[...]
    inside = mask_ref[...] > 0.0
    lane_x = lax.broadcasted_iota(jnp.int32, target.shape, 1) % XS
    field = jnp.where(inside, target, 0.0)
    first_moment = jnp.zeros_like(target)
    second_moment = jnp.zeros_like(target)
    for iteration in range(ITERS):
        radius = radii_ref[iteration]
        smoothed = lax.switch(
            jnp.clip(radius - 1, 0, RMAX - 1),
            [lambda u, r=r: box_smooth(u, r, lane_x) for r in range(1, RMAX + 1)],
            field,
        )
        field, first_moment, second_moment = adam_update(
            field, target, smoothed, first_moment, second_moment, iteration
        )
        field = jnp.where(inside, field, 0.0)
    height = o_ref.shape[0]
    width = o_ref.shape[1]
    o_ref[...] = field[HALO_Y : HALO_Y + height, HALO_Z : HALO_Z + width]


def transpose_kernel(x_ref, o_ref, s_ref):
    chunk = 128 * CH
    for j in range(x_ref.shape[1] // chunk):
        s_ref[...] = x_ref[:, pl.ds(chunk * j, chunk)].astype(jnp.float32).T
        for c in range(CH):
            cols = s_ref[pl.ds(c, 128, stride=CH), :]
            o_ref[c, :, pl.ds(128 * j, 128)] = cols.T.astype(o_ref.dtype)


def channel_major(x):
    rows, lanes = x.shape
    return pl.pallas_call(
        transpose_kernel,
        out_shape=jax.ShapeDtypeStruct((CH, rows, lanes // CH), x.dtype),
        scratch_shapes=[pltpu.VMEM((128 * CH, rows), jnp.float32)],
    )(x)


def block_counts(n_ref, t, offsets):
    upper = lax.broadcasted_iota(jnp.int32, (8, 128), 0) < 4
    return [jnp.where(upper, n_ref[2 * t, o], n_ref[2 * t + 1, o]) for o in offsets]


def softmin_tiles(total_y, f_ref, m0_ref, m4_ref, n_ref, o_ref, first, last):
    lanes_total = f_ref.shape[2]

    def body(t, carry):
        r0 = pl.multiple_of(t * 8, 8)
        counts = block_counts(n_ref, t, range(NOFF))
        for j in range(lanes_total // 128):
            peak, den, num = offset_partial(
                total_y, f_ref, m0_ref, m4_ref, counts, r0, range(NOFF), pl.ds(128 * j, 128)
            )
            o_ref[pl.ds(r0, 8), pl.ds(128 * j, 128)] = num / den
        return carry

    lax.fori_loop(first, last, body, 0)


def offset_partial(total_y, f_ref, m0_ref, m4_ref, counts, r0, offsets, lanes):
    fixed = [f_ref[c, pl.ds(r0, 8), lanes] for c in range(CH)]
    scores = []
    for o, n_o in zip(offsets, counts):
        shift = 4 * o
        if shift % 8 == 0:
            src, base = m0_ref, shift
        else:
            src, base = m4_ref, shift - 4
        acc = None
        for c in range(CH):
            d = fixed[c] - src[c, pl.ds(r0 + base, 8), lanes]
            acc = d * d if acc is None else acc + d * d
        scores.append(jnp.where(n_o > 0.0, -acc / softmin_temp, -jnp.inf))
    peak = scores[0]
    for s in scores[1:]:
        peak = jnp.maximum(peak, s)
    base_score = jnp.where(peak == -jnp.inf, 0.0, peak)
    den = None
    num = None
    for o, s, n_o in zip(offsets, scores, counts):
        w = n_o * jnp.exp(s - base_score)
        shift_norm = 2.0 * float(4 * o - REACH) / total_y
        den = w if den is None else den + w
        num = w * shift_norm if num is None else num + w * shift_norm
    return peak, den, num


def edge_tiles(height):
    reach_tiles = REACH // 8
    return list(range(reach_tiles)) + list(range(height // 8 - reach_tiles, height // 8))


def edge_row(t, height):
    return 8 * t if 8 * t < REACH else 8 * t - (height - 2 * REACH)


def halo_offsets(t, height):
    return [o for o in range(NOFF) if 8 * t + 4 * o < REACH or 8 * t + 4 * o + 8 > height + REACH]


def softmin_middle_kernel(total_y, n_ref, ft_ref, mt_ref, o_ref, pk_ref, dn_ref, nm_ref, f_ref, m0_ref, m4_ref):
    height = ft_ref.shape[1]
    lanes_total = ft_ref.shape[2]
    rows = height + 2 * REACH

    def build(c, carry):
        f_ref[c] = ft_ref[c].astype(jnp.float32)
        m0_ref[c, pl.ds(REACH, height), :] = mt_ref[c].astype(jnp.float32)
        m0_ref[c, pl.ds(0, REACH), :] = jnp.zeros((REACH, lanes_total), jnp.float32)
        m0_ref[c, pl.ds(REACH + height, REACH), :] = jnp.zeros((REACH, lanes_total), jnp.float32)
        m4_ref[c, pl.ds(0, rows - 8), :] = m0_ref[c, pl.ds(4, rows - 8), :]
        m4_ref[c, pl.ds(rows - 8, 8), :] = jnp.zeros((8, lanes_total), jnp.float32)
        return carry

    lax.fori_loop(0, CH, build, 0)
    tiles = height // 8
    softmin_tiles(total_y, f_ref, m0_ref, m4_ref, n_ref, o_ref, REACH // 8, tiles - REACH // 8)
    for t in edge_tiles(height):
        beyond = halo_offsets(t, height)
        inner = [o for o in range(NOFF) if o not in beyond]
        row = edge_row(t, height)

        def part(j, carry, t=t, inner=inner, row=row):
            lanes = pl.ds(pl.multiple_of(j * 128, 128), 128)
            counts = block_counts(n_ref, t, inner)
            peak, den, num = offset_partial(
                total_y, f_ref, m0_ref, m4_ref, counts, 8 * t, inner, lanes
            )
            pk_ref[pl.ds(row, 8), lanes] = peak
            dn_ref[pl.ds(row, 8), lanes] = den
            nm_ref[pl.ds(row, 8), lanes] = num
            return carry

        lax.fori_loop(0, lanes_total // 128, part, 0)


def softmin_edge_kernel(
    total_y, n_ref, fe_ref, me_ref, top_ref, bot_ref, pk_ref, dn_ref, nm_ref, _,
    o_hbm, f_ref, m0_ref, m4_ref, res_ref, sem,
):
    height = o_hbm.shape[0]
    lanes_total = fe_ref.shape[2]
    rows = height + 2 * REACH
    span = REACH + 16

    def build(c, carry):
        f_ref[c, pl.ds(0, REACH), :] = fe_ref[c, pl.ds(0, REACH), :].astype(jnp.float32)
        f_ref[c, pl.ds(height - REACH, REACH), :] = fe_ref[c, pl.ds(REACH, REACH), :].astype(
            jnp.float32
        )
        m0_ref[c, pl.ds(0, REACH), :] = top_ref[c].astype(jnp.float32)
        m0_ref[c, pl.ds(REACH, 16), :] = me_ref[c, pl.ds(0, 16), :].astype(jnp.float32)
        m0_ref[c, pl.ds(rows - span, 16), :] = me_ref[c, pl.ds(16, 16), :].astype(jnp.float32)
        m0_ref[c, pl.ds(rows - REACH, REACH), :] = bot_ref[c].astype(jnp.float32)
        m4_ref[c, pl.ds(0, span - 8), :] = m0_ref[c, pl.ds(4, span - 8), :]
        m4_ref[c, pl.ds(rows - span, span - 8), :] = m0_ref[c, pl.ds(rows - span + 4, span - 8), :]
        m4_ref[c, pl.ds(rows - 8, 8), :] = jnp.zeros((8, lanes_total), jnp.float32)
        return carry

    lax.fori_loop(0, CH, build, 0)
    for t in edge_tiles(height):
        beyond = halo_offsets(t, height)
        row = edge_row(t, height)

        def part(j, carry, t=t, beyond=beyond, row=row):
            lanes = pl.ds(pl.multiple_of(j * 128, 128), 128)
            rows_t = pl.ds(row, 8)
            counts = block_counts(n_ref, t, beyond)
            peak, den, num = offset_partial(
                total_y, f_ref, m0_ref, m4_ref, counts, 8 * t, beyond, lanes
            )
            peak_in = pk_ref[rows_t, lanes]
            top_score = jnp.maximum(peak, peak_in)
            scale = jnp.exp(peak - top_score)
            scale_in = jnp.exp(peak_in - top_score)
            den = den * scale + dn_ref[rows_t, lanes] * scale_in
            num = num * scale + nm_ref[rows_t, lanes] * scale_in
            res_ref[rows_t, lanes] = num / den
            return carry

        lax.fori_loop(0, lanes_total // 128, part, 0)
    head = pltpu.make_async_copy(
        res_ref.at[pl.ds(0, REACH)], o_hbm.at[pl.ds(0, REACH)], sem.at[0]
    )
    tail = pltpu.make_async_copy(
        res_ref.at[pl.ds(REACH, REACH)], o_hbm.at[pl.ds(height - REACH, REACH)], sem.at[1]
    )
    head.start()
    tail.start()
    head.wait()
    tail.wait()


def per_device(fixed_features, moving_features, cand_offsets, cand_lengths, smooth_radii):
    height = fixed_features.shape[0]
    columns_dev = fixed_features.shape[1] // CH
    blocks = height // 4
    total_y = height * lax.axis_size("gy")
    shifts = cand_offsets[:, 0, :]
    counts = cand_lengths[:, 0]
    live = jnp.arange(shifts.shape[1], dtype=jnp.int32)[None, :] < counts[:, None]
    offset_values = 4 * jnp.arange(NOFF, dtype=jnp.int32) - REACH
    hits = (shifts[:, :, None] == offset_values[None, None, :]) & live[:, :, None]
    mult = jnp.sum(hits.astype(jnp.float32), axis=1)

    gy_count = lax.axis_size("gy")
    fixed_c = channel_major(fixed_features)
    moving_c = channel_major(moving_features)
    top_rows = lax.ppermute(
        moving_c[:, height - REACH :], "gy", [(i, i + 1) for i in range(gy_count - 1)]
    )
    bottom_rows = lax.ppermute(
        moving_c[:, :REACH], "gy", [(i + 1, i) for i in range(gy_count - 1)]
    )

    rows = height + 2 * REACH
    tiles = height // 8
    reach_tiles = REACH // 8
    scratch = [
        pltpu.VMEM((CH, height, columns_dev), jnp.float32),
        pltpu.VMEM((CH, rows, columns_dev), jnp.float32),
        pltpu.VMEM((CH, rows, columns_dev), jnp.float32),
    ]
    params = pltpu.CompilerParams(vmem_limit_bytes=60 * 1024 * 1024)
    out_shape = jax.ShapeDtypeStruct((height, columns_dev), jnp.float32)
    smem = pl.BlockSpec(memory_space=pltpu.SMEM)
    vmem = pl.BlockSpec(memory_space=pltpu.VMEM)
    edge_shape = jax.ShapeDtypeStruct((2 * REACH, columns_dev), jnp.float32)
    middle, peak_part, den_part, num_part = pl.pallas_call(
        lambda *refs: softmin_middle_kernel(total_y, *refs),
        out_shape=(out_shape, edge_shape, edge_shape, edge_shape),
        in_specs=[smem, vmem, vmem],
        scratch_shapes=scratch,
        compiler_params=params,
    )(mult, fixed_c, moving_c)
    fixed_edge = jnp.concatenate([fixed_c[:, :REACH], fixed_c[:, height - REACH :]], axis=1)
    moving_edge = jnp.concatenate([moving_c[:, :16], moving_c[:, height - 16 :]], axis=1)
    disp_init = pl.pallas_call(
        lambda *refs: softmin_edge_kernel(total_y, *refs),
        out_shape=out_shape,
        in_specs=[smem] + [vmem] * 7 + [pl.BlockSpec(memory_space=pl.ANY)],
        out_specs=pl.BlockSpec(memory_space=pl.ANY),
        scratch_shapes=scratch
        + [pltpu.VMEM((2 * REACH, columns_dev), jnp.float32), pltpu.SemaphoreType.DMA((2,))],
        compiler_params=params,
        input_output_aliases={8: 0},
    )(mult, fixed_edge, moving_edge, top_rows, bottom_rows, peak_part, den_part, num_part, middle)

    ext = exchange_halo(disp_init, HALO_Y, HALO_Z, SEND_Y, SEND_Z)
    rows_ext, lanes_ext = ext.shape
    row_global = lax.axis_index("gy") * height - HALO_Y + lax.broadcasted_iota(
        jnp.int32, (rows_ext, lanes_ext), 0
    )
    lane_global = lax.axis_index("gz") * columns_dev - HALO_Z + lax.broadcasted_iota(
        jnp.int32, (rows_ext, lanes_ext), 1
    )
    inside = (
        (row_global >= 0)
        & (row_global < total_y)
        & (lane_global >= 0)
        & (lane_global < columns_dev * lax.axis_size("gz"))
    )
    grid_mask = inside.astype(jnp.float32)
    final_ext = pl.pallas_call(
        adam_kernel,
        out_shape=jax.ShapeDtypeStruct((height, columns_dev), jnp.float32),
        in_specs=[
            pl.BlockSpec(memory_space=pltpu.SMEM),
            pl.BlockSpec(memory_space=pltpu.VMEM),
            pl.BlockSpec(memory_space=pltpu.VMEM),
        ],
        compiler_params=pltpu.CompilerParams(vmem_limit_bytes=32 * 1024 * 1024),
    )(smooth_radii.astype(jnp.int32), ext, grid_mask)
    return (disp_init, final_ext)


def solution(mesh):
    in_specs = (P("gy", "gz"), P("gy", "gz"), P("gy", "gz", None), P("gy", "gz"), P())
    out_specs = (P("gy", "gz"), P("gy", "gz"))
    return jax.shard_map(
        per_device, mesh=mesh, in_specs=in_specs, out_specs=out_specs, check_vma=False
    )
```

```python
import jax
import jax.numpy as jnp
from jax import lax
from jax.experimental import pallas as pl
from jax.experimental.pallas import tpu as pltpu
from jax.sharding import PartitionSpec as P

CH = 16
XS = 8
REACH = 32
RMAX = 4
ITERS = 3
NOFF = 2 * (REACH // 4) + 1


softmin_temp = 2.0
smooth_weight = 2.0
adam_rate = 0.2
beta_first = 0.9
beta_second = 0.999
adam_floor = 0.05


def with_halo(cells, sides, width):
    for axis, dim in sides:
        count = lax.axis_size(axis)
        ends = count - 1
        head = lax.slice_in_dim(cells, 0, width, axis=dim)
        tail = lax.slice_in_dim(cells, cells.shape[dim] - width, cells.shape[dim], axis=dim)
        cells = jnp.concatenate(
            [
                lax.ppermute(tail, axis, [(i, (i + 1) % count) for i in range(ends)]),
                cells,
                lax.ppermute(head, axis, [((i + 1) % count, i) for i in range(ends)]),
            ],
            axis=dim,
        )
    return cells


def box_weights(radius):
    spread = jnp.arange(-RMAX, RMAX + 1)
    inside = jnp.abs(spread) <= radius
    return jnp.where(inside, 1.0, 0.0).astype(jnp.float32) / (2 * radius + 1).astype(jnp.float32)


def smooth_inner(padded, radius, margin):
    weights = box_weights(radius)
    height = padded.shape[0] - 2 * margin
    layers = padded.shape[1] - 2 * margin
    depth_cells = padded.shape[2]
    along_y = jnp.zeros((height, padded.shape[1], depth_cells), jnp.float32)
    for offset in range(-RMAX, RMAX + 1):
        along_y = (
            along_y + weights[RMAX + offset] * padded[margin + offset : margin + offset + height]
        )
    along_z = jnp.zeros((height, layers, depth_cells), jnp.float32)
    for offset in range(-RMAX, RMAX + 1):
        along_z = (
            along_z
            + weights[RMAX + offset] * along_y[:, margin + offset : margin + offset + layers]
        )
    x_padded = jnp.pad(along_z, ((0, 0), (0, 0), (RMAX, RMAX)))
    along_x = jnp.zeros((height, layers, depth_cells), jnp.float32)
    for offset in range(-RMAX, RMAX + 1):
        along_x = (
            along_x
            + weights[RMAX + offset] * x_padded[:, :, RMAX + offset : RMAX + offset + depth_cells]
        )
    return along_x


def adam_update(field, target_field, smoothed, first_moment, second_moment, iteration):
    gradient = field - target_field + smooth_weight * (field - smoothed)
    first_moment = beta_first * first_moment + (1.0 - beta_first) * gradient
    second_moment = beta_second * second_moment + (1.0 - beta_second) * gradient * gradient
    first_hat = first_moment / (1.0 - beta_first ** (iteration + 1))
    second_hat = second_moment / (1.0 - beta_second ** (iteration + 1))
    field = field - adam_rate * first_hat / (jnp.sqrt(second_hat) + adam_floor)
    return (field, first_moment, second_moment)


HALO_Y = 8
HALO_Z = 8 * XS
SEND_Y = 8
SEND_Z = 8 * XS


def exchange_halo(cells, wy, wz, send_y, send_z):
    ny = lax.axis_size("gy")
    nz = lax.axis_size("gz")
    top = lax.ppermute(cells[-send_y:], "gy", [(i, i + 1) for i in range(ny - 1)])
    bottom = lax.ppermute(cells[:send_y], "gy", [(i + 1, i) for i in range(ny - 1)])
    cells = jnp.concatenate([top, cells, bottom], axis=0)
    left = lax.ppermute(cells[:, -send_z:], "gz", [(i, i + 1) for i in range(nz - 1)])
    right = lax.ppermute(cells[:, :send_z], "gz", [(i + 1, i) for i in range(nz - 1)])
    cells = jnp.concatenate([left, cells, right], axis=1)
    return jnp.pad(cells, ((wy - send_y, wy - send_y), (wz - send_z, wz - send_z)))


def shifted(a, offset, axis):
    if offset == 0:
        return a
    return pltpu.roll(a, (-offset) % a.shape[axis], axis)


def box_smooth(u, radius, lane_x):
    scale = 1.0 / float(2 * radius + 1)
    along_y = u
    for o in range(1, radius + 1):
        along_y = along_y + shifted(u, -o, 0) + shifted(u, o, 0)
    along_y = along_y * scale
    along_z = along_y
    for o in range(1, radius + 1):
        along_z = along_z + shifted(along_y, -XS * o, 1) + shifted(along_y, XS * o, 1)
    along_z = along_z * scale
    along_x = along_z
    for o in range(1, radius + 1):
        along_x = (
            along_x
            + jnp.where(lane_x >= o, shifted(along_z, -o, 1), 0.0)
            + jnp.where(lane_x < XS - o, shifted(along_z, o, 1), 0.0)
        )
    return along_x * scale


def adam_kernel(radii_ref, d_ref, mask_ref, o_ref):
    target = d_ref[...]
    inside = mask_ref[...] > 0.0
    lane_x = lax.broadcasted_iota(jnp.int32, target.shape, 1) % XS
    field = jnp.where(inside, target, 0.0)
    first_moment = jnp.zeros_like(target)
    second_moment = jnp.zeros_like(target)
    for iteration in range(ITERS):
        radius = radii_ref[iteration]
        smoothed = lax.switch(
            jnp.clip(radius - 1, 0, RMAX - 1),
            [lambda u, r=r: box_smooth(u, r, lane_x) for r in range(1, RMAX + 1)],
            field,
        )
        field, first_moment, second_moment = adam_update(
            field, target, smoothed, first_moment, second_moment, iteration
        )
        field = jnp.where(inside, field, 0.0)
    height = o_ref.shape[0]
    width = o_ref.shape[1]
    o_ref[...] = field[HALO_Y : HALO_Y + height, HALO_Z : HALO_Z + width]


def transpose_kernel(x_ref, *refs):
    o_ref, s_ref = refs[0], refs[-1]
    chunk = 128 * CH
    for j in range(x_ref.shape[1] // chunk):
        s_ref[...] = x_ref[:, pl.ds(chunk * j, chunk)].astype(jnp.float32).T
        for c in range(CH):
            cols = s_ref[pl.ds(c, 128, stride=CH), :]
            o_ref[c, :, pl.ds(128 * j, 128)] = cols.T.astype(o_ref.dtype)
    if len(refs) == 4:
        rows = x_ref.shape[0]
        refs[1][...] = o_ref[:, pl.ds(0, REACH), :]
        refs[2][...] = o_ref[:, pl.ds(rows - REACH, REACH), :]


def channel_major(x, with_ends=False):
    rows, lanes = x.shape
    whole = jax.ShapeDtypeStruct((CH, rows, lanes // CH), x.dtype)
    ends = jax.ShapeDtypeStruct((CH, REACH, lanes // CH), x.dtype)
    return pl.pallas_call(
        transpose_kernel,
        out_shape=(whole, ends, ends) if with_ends else whole,
        scratch_shapes=[pltpu.VMEM((128 * CH, rows), jnp.float32)],
    )(x)


def block_counts(n_ref, t, offsets):
    upper = lax.broadcasted_iota(jnp.int32, (8, 128), 0) < 4
    return [jnp.where(upper, n_ref[2 * t, o], n_ref[2 * t + 1, o]) for o in offsets]


def softmin_tiles(total_y, f_ref, m0_ref, m4_ref, n_ref, o_ref, first, last):
    lanes_total = f_ref.shape[2]

    def body(t, carry):
        r0 = pl.multiple_of(t * 8, 8)
        counts = block_counts(n_ref, t, range(NOFF))
        for j in range(lanes_total // 128):
            peak, den, num = offset_partial(
                total_y, f_ref, m0_ref, m4_ref, counts, r0, range(NOFF), pl.ds(128 * j, 128)
            )
            o_ref[pl.ds(r0, 8), pl.ds(128 * j, 128)] = num / den
        return carry

    lax.fori_loop(first, last, body, 0)


def offset_partial(total_y, f_ref, m0_ref, m4_ref, counts, r0, offsets, lanes):
    fixed = [f_ref[c, pl.ds(r0, 8), lanes] for c in range(CH)]
    scores = []
    for o, n_o in zip(offsets, counts):
        shift = 4 * o
        if shift % 8 == 0:
            src, base = m0_ref, shift
        else:
            src, base = m4_ref, shift - 4
        acc = None
        for c in range(CH):
            d = fixed[c] - src[c, pl.ds(r0 + base, 8), lanes]
            acc = d * d if acc is None else acc + d * d
        scores.append(jnp.where(n_o > 0.0, -acc / softmin_temp, -jnp.inf))
    peak = scores[0]
    for s in scores[1:]:
        peak = jnp.maximum(peak, s)
    base_score = jnp.where(peak == -jnp.inf, 0.0, peak)
    den = None
    num = None
    for o, s, n_o in zip(offsets, scores, counts):
        w = n_o * jnp.exp(s - base_score)
        shift_norm = 2.0 * float(4 * o - REACH) / total_y
        den = w if den is None else den + w
        num = w * shift_norm if num is None else num + w * shift_norm
    return peak, den, num


def edge_tiles(height):
    reach_tiles = REACH // 8
    return list(range(reach_tiles)) + list(range(height // 8 - reach_tiles, height // 8))


def edge_row(t, height):
    return 8 * t if 8 * t < REACH else 8 * t - (height - 2 * REACH)


def halo_offsets(t, height):
    return [o for o in range(NOFF) if 8 * t + 4 * o < REACH or 8 * t + 4 * o + 8 > height + REACH]


def softmin_middle_kernel(total_y, n_ref, ft_ref, mt_ref, o_ref, pk_ref, dn_ref, nm_ref, f_ref, m0_ref, m4_ref):
    height = ft_ref.shape[1]
    lanes_total = ft_ref.shape[2]
    rows = height + 2 * REACH

    def build(c, carry):
        f_ref[c] = ft_ref[c].astype(jnp.float32)
        m0_ref[c, pl.ds(REACH, height), :] = mt_ref[c].astype(jnp.float32)
        m0_ref[c, pl.ds(0, REACH), :] = jnp.zeros((REACH, lanes_total), jnp.float32)
        m0_ref[c, pl.ds(REACH + height, REACH), :] = jnp.zeros((REACH, lanes_total), jnp.float32)
        m4_ref[c, pl.ds(0, rows - 8), :] = m0_ref[c, pl.ds(4, rows - 8), :]
        m4_ref[c, pl.ds(rows - 8, 8), :] = jnp.zeros((8, lanes_total), jnp.float32)
        return carry

    lax.fori_loop(0, CH, build, 0)
    tiles = height // 8
    softmin_tiles(total_y, f_ref, m0_ref, m4_ref, n_ref, o_ref, REACH // 8, tiles - REACH // 8)
    for t in edge_tiles(height):
        beyond = halo_offsets(t, height)
        inner = [o for o in range(NOFF) if o not in beyond]
        row = edge_row(t, height)

        def part(j, carry, t=t, inner=inner, row=row):
            lanes = pl.ds(pl.multiple_of(j * 128, 128), 128)
            counts = block_counts(n_ref, t, inner)
            peak, den, num = offset_partial(
                total_y, f_ref, m0_ref, m4_ref, counts, 8 * t, inner, lanes
            )
            pk_ref[pl.ds(row, 8), lanes] = peak
            dn_ref[pl.ds(row, 8), lanes] = den
            nm_ref[pl.ds(row, 8), lanes] = num
            return carry

        lax.fori_loop(0, lanes_total // 128, part, 0)


def softmin_edge_kernel(
    total_y, n_ref, fc_hbm, mc_hbm, top_ref, bot_ref, pk_ref, dn_ref, nm_ref, _,
    o_hbm, f_ref, m0_ref, m4_ref, res_ref, fe_ref, me_ref, sem,
):
    height = o_hbm.shape[0]
    lanes_total = fe_ref.shape[2]
    rows = height + 2 * REACH
    span = REACH + 16
    copies = [
        pltpu.make_async_copy(
            fc_hbm.at[:, pl.ds(0, REACH), :], fe_ref.at[:, pl.ds(0, REACH), :], sem.at[2]
        ),
        pltpu.make_async_copy(
            fc_hbm.at[:, pl.ds(height - REACH, REACH), :], fe_ref.at[:, pl.ds(REACH, REACH), :], sem.at[3]
        ),
        pltpu.make_async_copy(mc_hbm.at[:, pl.ds(0, 16), :], me_ref.at[:, pl.ds(0, 16), :], sem.at[4]),
        pltpu.make_async_copy(
            mc_hbm.at[:, pl.ds(height - 16, 16), :], me_ref.at[:, pl.ds(16, 16), :], sem.at[5]
        ),
    ]
    for cp in copies:
        cp.start()
    for cp in copies:
        cp.wait()

    def build(c, carry):
        f_ref[c, pl.ds(0, REACH), :] = fe_ref[c, pl.ds(0, REACH), :].astype(jnp.float32)
        f_ref[c, pl.ds(height - REACH, REACH), :] = fe_ref[c, pl.ds(REACH, REACH), :].astype(
            jnp.float32
        )
        m0_ref[c, pl.ds(0, REACH), :] = top_ref[c].astype(jnp.float32)
        m0_ref[c, pl.ds(REACH, 16), :] = me_ref[c, pl.ds(0, 16), :].astype(jnp.float32)
        m0_ref[c, pl.ds(rows - span, 16), :] = me_ref[c, pl.ds(16, 16), :].astype(jnp.float32)
        m0_ref[c, pl.ds(rows - REACH, REACH), :] = bot_ref[c].astype(jnp.float32)
        m4_ref[c, pl.ds(0, span - 8), :] = m0_ref[c, pl.ds(4, span - 8), :]
        m4_ref[c, pl.ds(rows - span, span - 8), :] = m0_ref[c, pl.ds(rows - span + 4, span - 8), :]
        m4_ref[c, pl.ds(rows - 8, 8), :] = jnp.zeros((8, lanes_total), jnp.float32)
        return carry

    lax.fori_loop(0, CH, build, 0)
    for t in edge_tiles(height):
        beyond = halo_offsets(t, height)
        row = edge_row(t, height)

        def part(j, carry, t=t, beyond=beyond, row=row):
            lanes = pl.ds(pl.multiple_of(j * 128, 128), 128)
            rows_t = pl.ds(row, 8)
            counts = block_counts(n_ref, t, beyond)
            peak, den, num = offset_partial(
                total_y, f_ref, m0_ref, m4_ref, counts, 8 * t, beyond, lanes
            )
            peak_in = pk_ref[rows_t, lanes]
            top_score = jnp.maximum(peak, peak_in)
            scale = jnp.exp(peak - top_score)
            scale_in = jnp.exp(peak_in - top_score)
            den = den * scale + dn_ref[rows_t, lanes] * scale_in
            num = num * scale + nm_ref[rows_t, lanes] * scale_in
            res_ref[rows_t, lanes] = num / den
            return carry

        lax.fori_loop(0, lanes_total // 128, part, 0)
    head = pltpu.make_async_copy(
        res_ref.at[pl.ds(0, REACH)], o_hbm.at[pl.ds(0, REACH)], sem.at[0]
    )
    tail = pltpu.make_async_copy(
        res_ref.at[pl.ds(REACH, REACH)], o_hbm.at[pl.ds(height - REACH, REACH)], sem.at[1]
    )
    head.start()
    tail.start()
    head.wait()
    tail.wait()


def per_device(fixed_features, moving_features, cand_offsets, cand_lengths, smooth_radii):
    height = fixed_features.shape[0]
    columns_dev = fixed_features.shape[1] // CH
    blocks = height // 4
    total_y = height * lax.axis_size("gy")
    shifts = cand_offsets[:, 0, :]
    counts = cand_lengths[:, 0]
    live = jnp.arange(shifts.shape[1], dtype=jnp.int32)[None, :] < counts[:, None]
    offset_values = 4 * jnp.arange(NOFF, dtype=jnp.int32) - REACH
    hits = (shifts[:, :, None] == offset_values[None, None, :]) & live[:, :, None]
    mult = jnp.sum(hits.astype(jnp.float32), axis=1)

    gy_count = lax.axis_size("gy")
    fixed_c = channel_major(fixed_features)
    moving_c, moving_head, moving_tail = channel_major(moving_features, with_ends=True)
    top_rows = lax.ppermute(moving_tail, "gy", [(i, i + 1) for i in range(gy_count - 1)])
    bottom_rows = lax.ppermute(moving_head, "gy", [(i + 1, i) for i in range(gy_count - 1)])

    rows = height + 2 * REACH
    tiles = height // 8
    reach_tiles = REACH // 8
    scratch = [
        pltpu.VMEM((CH, height, columns_dev), jnp.float32),
        pltpu.VMEM((CH, rows, columns_dev), jnp.float32),
        pltpu.VMEM((CH, rows, columns_dev), jnp.float32),
    ]
    params = pltpu.CompilerParams(vmem_limit_bytes=60 * 1024 * 1024)
    out_shape = jax.ShapeDtypeStruct((height, columns_dev), jnp.float32)
    smem = pl.BlockSpec(memory_space=pltpu.SMEM)
    vmem = pl.BlockSpec(memory_space=pltpu.VMEM)
    anywhere = pl.BlockSpec(memory_space=pl.ANY)
    edge_shape = jax.ShapeDtypeStruct((2 * REACH, columns_dev), jnp.float32)
    middle, peak_part, den_part, num_part = pl.pallas_call(
        lambda *refs: softmin_middle_kernel(total_y, *refs),
        out_shape=(out_shape, edge_shape, edge_shape, edge_shape),
        in_specs=[smem, vmem, vmem],
        scratch_shapes=scratch,
        compiler_params=params,
    )(mult, fixed_c, moving_c)
    disp_init = pl.pallas_call(
        lambda *refs: softmin_edge_kernel(total_y, *refs),
        out_shape=out_shape,
        in_specs=[smem, anywhere, anywhere] + [vmem] * 5 + [anywhere],
        out_specs=anywhere,
        scratch_shapes=scratch
        + [
            pltpu.VMEM((2 * REACH, columns_dev), jnp.float32),
            pltpu.VMEM((CH, 2 * REACH, columns_dev), jnp.bfloat16),
            pltpu.VMEM((CH, 32, columns_dev), jnp.bfloat16),
            pltpu.SemaphoreType.DMA((6,)),
        ],
        compiler_params=params,
        input_output_aliases={8: 0},
    )(mult, fixed_c, moving_c, top_rows, bottom_rows, peak_part, den_part, num_part, middle)

    ext = exchange_halo(disp_init, HALO_Y, HALO_Z, SEND_Y, SEND_Z)
    rows_ext, lanes_ext = ext.shape
    row_global = lax.axis_index("gy") * height - HALO_Y + lax.broadcasted_iota(
        jnp.int32, (rows_ext, lanes_ext), 0
    )
    lane_global = lax.axis_index("gz") * columns_dev - HALO_Z + lax.broadcasted_iota(
        jnp.int32, (rows_ext, lanes_ext), 1
    )
    inside = (
        (row_global >= 0)
        & (row_global < total_y)
        & (lane_global >= 0)
        & (lane_global < columns_dev * lax.axis_size("gz"))
    )
    grid_mask = inside.astype(jnp.float32)
    final_ext = pl.pallas_call(
        adam_kernel,
        out_shape=jax.ShapeDtypeStruct((height, columns_dev), jnp.float32),
        in_specs=[
            pl.BlockSpec(memory_space=pltpu.SMEM),
            pl.BlockSpec(memory_space=pltpu.VMEM),
            pl.BlockSpec(memory_space=pltpu.VMEM),
        ],
        compiler_params=pltpu.CompilerParams(vmem_limit_bytes=32 * 1024 * 1024),
    )(smooth_radii.astype(jnp.int32), ext, grid_mask)
    return (disp_init, final_ext)


def solution(mesh):
    in_specs = (P("gy", "gz"), P("gy", "gz"), P("gy", "gz", None), P("gy", "gz"), P())
    out_specs = (P("gy", "gz"), P("gy", "gz"))
    return jax.shard_map(
        per_device, mesh=mesh, in_specs=in_specs, out_specs=out_specs, check_vma=False
    )
```

```python
import jax
import jax.numpy as jnp
from jax import lax
from jax.experimental import pallas as pl
from jax.experimental.pallas import tpu as pltpu
from jax.sharding import PartitionSpec as P

CH = 16
XS = 8
REACH = 32
RMAX = 4
ITERS = 3
NOFF = 2 * (REACH // 4) + 1


softmin_temp = 2.0
smooth_weight = 2.0
adam_rate = 0.2
beta_first = 0.9
beta_second = 0.999
adam_floor = 0.05


def with_halo(cells, sides, width):
    for axis, dim in sides:
        count = lax.axis_size(axis)
        ends = count - 1
        head = lax.slice_in_dim(cells, 0, width, axis=dim)
        tail = lax.slice_in_dim(cells, cells.shape[dim] - width, cells.shape[dim], axis=dim)
        cells = jnp.concatenate(
            [
                lax.ppermute(tail, axis, [(i, (i + 1) % count) for i in range(ends)]),
                cells,
                lax.ppermute(head, axis, [((i + 1) % count, i) for i in range(ends)]),
            ],
            axis=dim,
        )
    return cells


def box_weights(radius):
    spread = jnp.arange(-RMAX, RMAX + 1)
    inside = jnp.abs(spread) <= radius
    return jnp.where(inside, 1.0, 0.0).astype(jnp.float32) / (2 * radius + 1).astype(jnp.float32)


def smooth_inner(padded, radius, margin):
    weights = box_weights(radius)
    height = padded.shape[0] - 2 * margin
    layers = padded.shape[1] - 2 * margin
    depth_cells = padded.shape[2]
    along_y = jnp.zeros((height, padded.shape[1], depth_cells), jnp.float32)
    for offset in range(-RMAX, RMAX + 1):
        along_y = (
            along_y + weights[RMAX + offset] * padded[margin + offset : margin + offset + height]
        )
    along_z = jnp.zeros((height, layers, depth_cells), jnp.float32)
    for offset in range(-RMAX, RMAX + 1):
        along_z = (
            along_z
            + weights[RMAX + offset] * along_y[:, margin + offset : margin + offset + layers]
        )
    x_padded = jnp.pad(along_z, ((0, 0), (0, 0), (RMAX, RMAX)))
    along_x = jnp.zeros((height, layers, depth_cells), jnp.float32)
    for offset in range(-RMAX, RMAX + 1):
        along_x = (
            along_x
            + weights[RMAX + offset] * x_padded[:, :, RMAX + offset : RMAX + offset + depth_cells]
        )
    return along_x


def adam_update(field, target_field, smoothed, first_moment, second_moment, iteration):
    gradient = field - target_field + smooth_weight * (field - smoothed)
    first_moment = beta_first * first_moment + (1.0 - beta_first) * gradient
    second_moment = beta_second * second_moment + (1.0 - beta_second) * gradient * gradient
    first_hat = first_moment / (1.0 - beta_first ** (iteration + 1))
    second_hat = second_moment / (1.0 - beta_second ** (iteration + 1))
    field = field - adam_rate * first_hat / (jnp.sqrt(second_hat) + adam_floor)
    return (field, first_moment, second_moment)


HALO_Y = 8
HALO_Z = 8 * XS
SEND_Y = 8
SEND_Z = 8 * XS


def exchange_halo(cells, wy, wz, send_y, send_z):
    ny = lax.axis_size("gy")
    nz = lax.axis_size("gz")
    top = lax.ppermute(cells[-send_y:], "gy", [(i, i + 1) for i in range(ny - 1)])
    bottom = lax.ppermute(cells[:send_y], "gy", [(i + 1, i) for i in range(ny - 1)])
    cells = jnp.concatenate([top, cells, bottom], axis=0)
    left = lax.ppermute(cells[:, -send_z:], "gz", [(i, i + 1) for i in range(nz - 1)])
    right = lax.ppermute(cells[:, :send_z], "gz", [(i + 1, i) for i in range(nz - 1)])
    cells = jnp.concatenate([left, cells, right], axis=1)
    return jnp.pad(cells, ((wy - send_y, wy - send_y), (wz - send_z, wz - send_z)))


def shifted(a, offset, axis):
    if offset == 0:
        return a
    return pltpu.roll(a, (-offset) % a.shape[axis], axis)


def box_smooth(u, radius, lane_x):
    scale = 1.0 / float(2 * radius + 1)
    along_y = u
    for o in range(1, radius + 1):
        along_y = along_y + shifted(u, -o, 0) + shifted(u, o, 0)
    along_y = along_y * scale
    along_z = along_y
    for o in range(1, radius + 1):
        along_z = along_z + shifted(along_y, -XS * o, 1) + shifted(along_y, XS * o, 1)
    along_z = along_z * scale
    along_x = along_z
    for o in range(1, radius + 1):
        along_x = (
            along_x
            + jnp.where(lane_x >= o, shifted(along_z, -o, 1), 0.0)
            + jnp.where(lane_x < XS - o, shifted(along_z, o, 1), 0.0)
        )
    return along_x * scale


def adam_kernel(radii_ref, pos_ref, d_ref, y_ref, z_ref, o_ref, ext_ref):
    height, width = d_ref.shape
    ext_ref[pl.ds(0, height), pl.ds(0, width)] = d_ref[...]
    ext_ref[pl.ds(height, 2 * HALO_Y), pl.ds(0, width)] = y_ref[...]
    ext_ref[:, pl.ds(width, 2 * HALO_Z)] = z_ref[...]
    target = ext_ref[...]
    rows = lax.broadcasted_iota(jnp.int32, target.shape, 0)
    lanes = lax.broadcasted_iota(jnp.int32, target.shape, 1)
    gy = pos_ref[0]
    gz = pos_ref[1]
    row_ok = (
        (rows < height)
        | ((rows < height + HALO_Y) & (gy < pos_ref[2] - 1))
        | ((rows >= height + HALO_Y) & (gy > 0))
    )
    lane_ok = (
        (lanes < width)
        | ((lanes < width + HALO_Z) & (gz < pos_ref[3] - 1))
        | ((lanes >= width + HALO_Z) & (gz > 0))
    )
    inside = row_ok & lane_ok
    lane_x = lanes % XS
    field = jnp.where(inside, target, 0.0)
    first_moment = jnp.zeros_like(target)
    second_moment = jnp.zeros_like(target)
    for iteration in range(ITERS):
        radius = radii_ref[iteration]
        smoothed = lax.switch(
            jnp.clip(radius - 1, 0, RMAX - 1),
            [lambda u, r=r: box_smooth(u, r, lane_x) for r in range(1, RMAX + 1)],
            field,
        )
        field, first_moment, second_moment = adam_update(
            field, target, smoothed, first_moment, second_moment, iteration
        )
        field = jnp.where(inside, field, 0.0)
    o_ref[...] = field[:height, :width]


def transpose_kernel(x_ref, *refs):
    o_ref, s_ref = refs[0], refs[-1]
    chunk = 128 * CH
    for j in range(x_ref.shape[1] // chunk):
        s_ref[...] = x_ref[:, pl.ds(chunk * j, chunk)].astype(jnp.float32).T
        for c in range(CH):
            cols = s_ref[pl.ds(c, 128, stride=CH), :]
            o_ref[c, :, pl.ds(128 * j, 128)] = cols.T.astype(o_ref.dtype)
    if len(refs) == 4:
        rows = x_ref.shape[0]
        refs[1][...] = o_ref[:, pl.ds(0, REACH), :]
        refs[2][...] = o_ref[:, pl.ds(rows - REACH, REACH), :]


def channel_major(x, with_ends=False):
    rows, lanes = x.shape
    whole = jax.ShapeDtypeStruct((CH, rows, lanes // CH), x.dtype)
    ends = jax.ShapeDtypeStruct((CH, REACH, lanes // CH), x.dtype)
    return pl.pallas_call(
        transpose_kernel,
        out_shape=(whole, ends, ends) if with_ends else whole,
        scratch_shapes=[pltpu.VMEM((128 * CH, rows), jnp.float32)],
    )(x)


def block_counts(n_ref, t, offsets):
    upper = lax.broadcasted_iota(jnp.int32, (8, 128), 0) < 4
    return [jnp.where(upper, n_ref[2 * t, o], n_ref[2 * t + 1, o]) for o in offsets]


def softmin_tiles(total_y, f_ref, m0_ref, m4_ref, n_ref, o_ref, first, last):
    lanes_total = f_ref.shape[2]

    def body(t, carry):
        r0 = pl.multiple_of(t * 8, 8)
        counts = block_counts(n_ref, t, range(NOFF))
        for j in range(lanes_total // 128):
            peak, den, num = offset_partial(
                total_y, f_ref, m0_ref, m4_ref, counts, r0, range(NOFF), pl.ds(128 * j, 128)
            )
            o_ref[pl.ds(r0, 8), pl.ds(128 * j, 128)] = num / den
        return carry

    lax.fori_loop(first, last, body, 0)


def offset_partial(total_y, f_ref, m0_ref, m4_ref, counts, r0, offsets, lanes):
    fixed = [f_ref[c, pl.ds(r0, 8), lanes] for c in range(CH)]
    scores = []
    for o, n_o in zip(offsets, counts):
        shift = 4 * o
        if shift % 8 == 0:
            src, base = m0_ref, shift
        else:
            src, base = m4_ref, shift - 4
        acc = None
        for c in range(CH):
            d = fixed[c] - src[c, pl.ds(r0 + base, 8), lanes]
            acc = d * d if acc is None else acc + d * d
        scores.append(jnp.where(n_o > 0.0, -acc / softmin_temp, -jnp.inf))
    peak = scores[0]
    for s in scores[1:]:
        peak = jnp.maximum(peak, s)
    base_score = jnp.where(peak == -jnp.inf, 0.0, peak)
    den = None
    num = None
    for o, s, n_o in zip(offsets, scores, counts):
        w = n_o * jnp.exp(s - base_score)
        shift_norm = 2.0 * float(4 * o - REACH) / total_y
        den = w if den is None else den + w
        num = w * shift_norm if num is None else num + w * shift_norm
    return peak, den, num


def edge_tiles(height):
    reach_tiles = REACH // 8
    return list(range(reach_tiles)) + list(range(height // 8 - reach_tiles, height // 8))


def edge_row(t, height):
    return 8 * t if 8 * t < REACH else 8 * t - (height - 2 * REACH)


def halo_offsets(t, height):
    return [o for o in range(NOFF) if 8 * t + 4 * o < REACH or 8 * t + 4 * o + 8 > height + REACH]


def softmin_middle_kernel(total_y, n_ref, ft_ref, mt_ref, o_ref, pk_ref, dn_ref, nm_ref, f_ref, m0_ref, m4_ref):
    height = ft_ref.shape[1]
    lanes_total = ft_ref.shape[2]
    rows = height + 2 * REACH

    def build(c, carry):
        f_ref[c] = ft_ref[c].astype(jnp.float32)
        m0_ref[c, pl.ds(REACH, height), :] = mt_ref[c].astype(jnp.float32)
        m0_ref[c, pl.ds(0, REACH), :] = jnp.zeros((REACH, lanes_total), jnp.float32)
        m0_ref[c, pl.ds(REACH + height, REACH), :] = jnp.zeros((REACH, lanes_total), jnp.float32)
        m4_ref[c, pl.ds(0, rows - 8), :] = m0_ref[c, pl.ds(4, rows - 8), :]
        m4_ref[c, pl.ds(rows - 8, 8), :] = jnp.zeros((8, lanes_total), jnp.float32)
        return carry

    lax.fori_loop(0, CH, build, 0)
    tiles = height // 8
    softmin_tiles(total_y, f_ref, m0_ref, m4_ref, n_ref, o_ref, REACH // 8, tiles - REACH // 8)
    for t in edge_tiles(height):
        beyond = halo_offsets(t, height)
        inner = [o for o in range(NOFF) if o not in beyond]
        row = edge_row(t, height)

        def part(j, carry, t=t, inner=inner, row=row):
            lanes = pl.ds(pl.multiple_of(j * 128, 128), 128)
            counts = block_counts(n_ref, t, inner)
            peak, den, num = offset_partial(
                total_y, f_ref, m0_ref, m4_ref, counts, 8 * t, inner, lanes
            )
            pk_ref[pl.ds(row, 8), lanes] = peak
            dn_ref[pl.ds(row, 8), lanes] = den
            nm_ref[pl.ds(row, 8), lanes] = num
            return carry

        lax.fori_loop(0, lanes_total // 128, part, 0)


def softmin_edge_kernel(
    total_y, n_ref, fc_hbm, mc_hbm, top_ref, bot_ref, pk_ref, dn_ref, nm_ref, _,
    o_hbm, f_ref, m0_ref, m4_ref, res_ref, fe_ref, me_ref, sem,
):
    height = o_hbm.shape[0]
    lanes_total = fe_ref.shape[2]
    rows = height + 2 * REACH
    span = REACH + 16
    copies = [
        pltpu.make_async_copy(
            fc_hbm.at[:, pl.ds(0, REACH), :], fe_ref.at[:, pl.ds(0, REACH), :], sem.at[2]
        ),
        pltpu.make_async_copy(
            fc_hbm.at[:, pl.ds(height - REACH, REACH), :], fe_ref.at[:, pl.ds(REACH, REACH), :], sem.at[3]
        ),
        pltpu.make_async_copy(mc_hbm.at[:, pl.ds(0, 16), :], me_ref.at[:, pl.ds(0, 16), :], sem.at[4]),
        pltpu.make_async_copy(
            mc_hbm.at[:, pl.ds(height - 16, 16), :], me_ref.at[:, pl.ds(16, 16), :], sem.at[5]
        ),
    ]
    for cp in copies:
        cp.start()
    for cp in copies:
        cp.wait()

    def build(c, carry):
        f_ref[c, pl.ds(0, REACH), :] = fe_ref[c, pl.ds(0, REACH), :].astype(jnp.float32)
        f_ref[c, pl.ds(height - REACH, REACH), :] = fe_ref[c, pl.ds(REACH, REACH), :].astype(
            jnp.float32
        )
        m0_ref[c, pl.ds(0, REACH), :] = top_ref[c].astype(jnp.float32)
        m0_ref[c, pl.ds(REACH, 16), :] = me_ref[c, pl.ds(0, 16), :].astype(jnp.float32)
        m0_ref[c, pl.ds(rows - span, 16), :] = me_ref[c, pl.ds(16, 16), :].astype(jnp.float32)
        m0_ref[c, pl.ds(rows - REACH, REACH), :] = bot_ref[c].astype(jnp.float32)
        m4_ref[c, pl.ds(0, span - 8), :] = m0_ref[c, pl.ds(4, span - 8), :]
        m4_ref[c, pl.ds(rows - span, span - 8), :] = m0_ref[c, pl.ds(rows - span + 4, span - 8), :]
        m4_ref[c, pl.ds(rows - 8, 8), :] = jnp.zeros((8, lanes_total), jnp.float32)
        return carry

    lax.fori_loop(0, CH, build, 0)
    for t in edge_tiles(height):
        beyond = halo_offsets(t, height)
        row = edge_row(t, height)

        def part(j, carry, t=t, beyond=beyond, row=row):
            lanes = pl.ds(pl.multiple_of(j * 128, 128), 128)
            rows_t = pl.ds(row, 8)
            counts = block_counts(n_ref, t, beyond)
            peak, den, num = offset_partial(
                total_y, f_ref, m0_ref, m4_ref, counts, 8 * t, beyond, lanes
            )
            peak_in = pk_ref[rows_t, lanes]
            top_score = jnp.maximum(peak, peak_in)
            scale = jnp.exp(peak - top_score)
            scale_in = jnp.exp(peak_in - top_score)
            den = den * scale + dn_ref[rows_t, lanes] * scale_in
            num = num * scale + nm_ref[rows_t, lanes] * scale_in
            res_ref[rows_t, lanes] = num / den
            return carry

        lax.fori_loop(0, lanes_total // 128, part, 0)
    head = pltpu.make_async_copy(
        res_ref.at[pl.ds(0, REACH)], o_hbm.at[pl.ds(0, REACH)], sem.at[0]
    )
    tail = pltpu.make_async_copy(
        res_ref.at[pl.ds(REACH, REACH)], o_hbm.at[pl.ds(height - REACH, REACH)], sem.at[1]
    )
    head.start()
    tail.start()
    head.wait()
    tail.wait()


def per_device(fixed_features, moving_features, cand_offsets, cand_lengths, smooth_radii):
    height = fixed_features.shape[0]
    columns_dev = fixed_features.shape[1] // CH
    blocks = height // 4
    total_y = height * lax.axis_size("gy")
    shifts = cand_offsets[:, 0, :]
    counts = cand_lengths[:, 0]
    live = jnp.arange(shifts.shape[1], dtype=jnp.int32)[None, :] < counts[:, None]
    offset_values = 4 * jnp.arange(NOFF, dtype=jnp.int32) - REACH
    hits = (shifts[:, :, None] == offset_values[None, None, :]) & live[:, :, None]
    mult = jnp.sum(hits.astype(jnp.float32), axis=1)

    gy_count = lax.axis_size("gy")
    fixed_c = channel_major(fixed_features)
    moving_c, moving_head, moving_tail = channel_major(moving_features, with_ends=True)
    top_rows = lax.ppermute(moving_tail, "gy", [(i, i + 1) for i in range(gy_count - 1)])
    bottom_rows = lax.ppermute(moving_head, "gy", [(i + 1, i) for i in range(gy_count - 1)])

    rows = height + 2 * REACH
    tiles = height // 8
    reach_tiles = REACH // 8
    scratch = [
        pltpu.VMEM((CH, height, columns_dev), jnp.float32),
        pltpu.VMEM((CH, rows, columns_dev), jnp.float32),
        pltpu.VMEM((CH, rows, columns_dev), jnp.float32),
    ]
    params = pltpu.CompilerParams(vmem_limit_bytes=60 * 1024 * 1024)
    out_shape = jax.ShapeDtypeStruct((height, columns_dev), jnp.float32)
    smem = pl.BlockSpec(memory_space=pltpu.SMEM)
    vmem = pl.BlockSpec(memory_space=pltpu.VMEM)
    anywhere = pl.BlockSpec(memory_space=pl.ANY)
    edge_shape = jax.ShapeDtypeStruct((2 * REACH, columns_dev), jnp.float32)
    middle, peak_part, den_part, num_part = pl.pallas_call(
        lambda *refs: softmin_middle_kernel(total_y, *refs),
        out_shape=(out_shape, edge_shape, edge_shape, edge_shape),
        in_specs=[smem, vmem, vmem],
        scratch_shapes=scratch,
        compiler_params=params,
    )(mult, fixed_c, moving_c)
    disp_init = pl.pallas_call(
        lambda *refs: softmin_edge_kernel(total_y, *refs),
        out_shape=out_shape,
        in_specs=[smem, anywhere, anywhere] + [vmem] * 5 + [anywhere],
        out_specs=anywhere,
        scratch_shapes=scratch
        + [
            pltpu.VMEM((2 * REACH, columns_dev), jnp.float32),
            pltpu.VMEM((CH, 2 * REACH, columns_dev), jnp.bfloat16),
            pltpu.VMEM((CH, 32, columns_dev), jnp.bfloat16),
            pltpu.SemaphoreType.DMA((6,)),
        ],
        compiler_params=params,
        input_output_aliases={8: 0},
    )(mult, fixed_c, moving_c, top_rows, bottom_rows, peak_part, den_part, num_part, middle)

    gz_count = lax.axis_size("gz")
    below = lax.ppermute(disp_init[:HALO_Y], "gy", [(i + 1, i) for i in range(gy_count - 1)])
    above = lax.ppermute(disp_init[-HALO_Y:], "gy", [(i, i + 1) for i in range(gy_count - 1)])

    def ring_columns(lo, hi):
        return jnp.concatenate([disp_init[:, lo:hi], below[:, lo:hi], above[:, lo:hi]], axis=0)

    left = lax.ppermute(
        ring_columns(columns_dev - HALO_Z, columns_dev),
        "gz",
        [(i, i + 1) for i in range(gz_count - 1)],
    )
    right = lax.ppermute(ring_columns(0, HALO_Z), "gz", [(i + 1, i) for i in range(gz_count - 1)])
    position = jnp.stack(
        [lax.axis_index("gy"), lax.axis_index("gz"), jnp.int32(gy_count), jnp.int32(gz_count)]
    ).astype(jnp.int32)
    final_ext = pl.pallas_call(
        adam_kernel,
        out_shape=jax.ShapeDtypeStruct((height, columns_dev), jnp.float32),
        in_specs=[smem, smem, vmem, vmem, vmem],
        scratch_shapes=[
            pltpu.VMEM((height + 2 * HALO_Y, columns_dev + 2 * HALO_Z), jnp.float32)
        ],
        compiler_params=pltpu.CompilerParams(vmem_limit_bytes=32 * 1024 * 1024),
    )(
        smooth_radii.astype(jnp.int32),
        position,
        disp_init,
        jnp.concatenate([below, above], axis=0),
        jnp.concatenate([right, left], axis=1),
    )
    return (disp_init, final_ext)


def solution(mesh):
    in_specs = (P("gy", "gz"), P("gy", "gz"), P("gy", "gz", None), P("gy", "gz"), P())
    out_specs = (P("gy", "gz"), P("gy", "gz"))
    return jax.shard_map(
        per_device, mesh=mesh, in_specs=in_specs, out_specs=out_specs, check_vma=False
    )
```

```python
import jax
import jax.numpy as jnp
from jax import lax
from jax.experimental import pallas as pl
from jax.experimental.pallas import tpu as pltpu
from jax.sharding import PartitionSpec as P

CH = 16
XS = 8
REACH = 32
RMAX = 4
ITERS = 3
NOFF = 2 * (REACH // 4) + 1


softmin_temp = 2.0
smooth_weight = 2.0
adam_rate = 0.2
beta_first = 0.9
beta_second = 0.999
adam_floor = 0.05


def with_halo(cells, sides, width):
    for axis, dim in sides:
        count = lax.axis_size(axis)
        ends = count - 1
        head = lax.slice_in_dim(cells, 0, width, axis=dim)
        tail = lax.slice_in_dim(cells, cells.shape[dim] - width, cells.shape[dim], axis=dim)
        cells = jnp.concatenate(
            [
                lax.ppermute(tail, axis, [(i, (i + 1) % count) for i in range(ends)]),
                cells,
                lax.ppermute(head, axis, [((i + 1) % count, i) for i in range(ends)]),
            ],
            axis=dim,
        )
    return cells


def box_weights(radius):
    spread = jnp.arange(-RMAX, RMAX + 1)
    inside = jnp.abs(spread) <= radius
    return jnp.where(inside, 1.0, 0.0).astype(jnp.float32) / (2 * radius + 1).astype(jnp.float32)


def smooth_inner(padded, radius, margin):
    weights = box_weights(radius)
    height = padded.shape[0] - 2 * margin
    layers = padded.shape[1] - 2 * margin
    depth_cells = padded.shape[2]
    along_y = jnp.zeros((height, padded.shape[1], depth_cells), jnp.float32)
    for offset in range(-RMAX, RMAX + 1):
        along_y = (
            along_y + weights[RMAX + offset] * padded[margin + offset : margin + offset + height]
        )
    along_z = jnp.zeros((height, layers, depth_cells), jnp.float32)
    for offset in range(-RMAX, RMAX + 1):
        along_z = (
            along_z
            + weights[RMAX + offset] * along_y[:, margin + offset : margin + offset + layers]
        )
    x_padded = jnp.pad(along_z, ((0, 0), (0, 0), (RMAX, RMAX)))
    along_x = jnp.zeros((height, layers, depth_cells), jnp.float32)
    for offset in range(-RMAX, RMAX + 1):
        along_x = (
            along_x
            + weights[RMAX + offset] * x_padded[:, :, RMAX + offset : RMAX + offset + depth_cells]
        )
    return along_x


def adam_update(field, target_field, smoothed, first_moment, second_moment, iteration):
    gradient = field - target_field + smooth_weight * (field - smoothed)
    first_moment = beta_first * first_moment + (1.0 - beta_first) * gradient
    second_moment = beta_second * second_moment + (1.0 - beta_second) * gradient * gradient
    first_hat = first_moment / (1.0 - beta_first ** (iteration + 1))
    second_hat = second_moment / (1.0 - beta_second ** (iteration + 1))
    field = field - adam_rate * first_hat / (jnp.sqrt(second_hat) + adam_floor)
    return (field, first_moment, second_moment)


HALO_Y = 8
HALO_Z = 8 * XS
SEND_Y = 8
SEND_Z = 8 * XS


def exchange_halo(cells, wy, wz, send_y, send_z):
    ny = lax.axis_size("gy")
    nz = lax.axis_size("gz")
    top = lax.ppermute(cells[-send_y:], "gy", [(i, i + 1) for i in range(ny - 1)])
    bottom = lax.ppermute(cells[:send_y], "gy", [(i + 1, i) for i in range(ny - 1)])
    cells = jnp.concatenate([top, cells, bottom], axis=0)
    left = lax.ppermute(cells[:, -send_z:], "gz", [(i, i + 1) for i in range(nz - 1)])
    right = lax.ppermute(cells[:, :send_z], "gz", [(i + 1, i) for i in range(nz - 1)])
    cells = jnp.concatenate([left, cells, right], axis=1)
    return jnp.pad(cells, ((wy - send_y, wy - send_y), (wz - send_z, wz - send_z)))


def shifted(a, offset, axis):
    if offset == 0:
        return a
    return pltpu.roll(a, (-offset) % a.shape[axis], axis)


def box_smooth(u, radius, lane_x):
    scale = 1.0 / float(2 * radius + 1)
    along_y = u
    for o in range(1, radius + 1):
        along_y = along_y + shifted(u, -o, 0) + shifted(u, o, 0)
    along_y = along_y * scale
    along_z = along_y
    for o in range(1, radius + 1):
        along_z = along_z + shifted(along_y, -XS * o, 1) + shifted(along_y, XS * o, 1)
    along_z = along_z * scale
    along_x = along_z
    for o in range(1, radius + 1):
        along_x = (
            along_x
            + jnp.where(lane_x >= o, shifted(along_z, -o, 1), 0.0)
            + jnp.where(lane_x < XS - o, shifted(along_z, o, 1), 0.0)
        )
    return along_x * scale


def adam_kernel(radii_ref, pos_ref, d_ref, y_ref, z_ref, o_ref, ext_ref):
    height, width = d_ref.shape
    ext_ref[pl.ds(0, height), pl.ds(0, width)] = d_ref[...]
    ext_ref[pl.ds(height, 2 * HALO_Y), pl.ds(0, width)] = y_ref[...]
    ext_ref[:, pl.ds(width, 2 * HALO_Z)] = z_ref[...]
    target = ext_ref[...]
    rows = lax.broadcasted_iota(jnp.int32, target.shape, 0)
    lanes = lax.broadcasted_iota(jnp.int32, target.shape, 1)
    gy = pos_ref[0]
    gz = pos_ref[1]
    row_ok = (
        (rows < height)
        | ((rows < height + HALO_Y) & (gy < pos_ref[2] - 1))
        | ((rows >= height + HALO_Y) & (gy > 0))
    )
    lane_ok = (
        (lanes < width)
        | ((lanes < width + HALO_Z) & (gz < pos_ref[3] - 1))
        | ((lanes >= width + HALO_Z) & (gz > 0))
    )
    inside = row_ok & lane_ok
    lane_x = lanes % XS
    field = jnp.where(inside, target, 0.0)
    first_moment = jnp.zeros_like(target)
    second_moment = jnp.zeros_like(target)
    for iteration in range(ITERS):
        radius = radii_ref[iteration]
        smoothed = lax.switch(
            jnp.clip(radius - 1, 0, RMAX - 1),
            [lambda u, r=r: box_smooth(u, r, lane_x) for r in range(1, RMAX + 1)],
            field,
        )
        field, first_moment, second_moment = adam_update(
            field, target, smoothed, first_moment, second_moment, iteration
        )
        field = jnp.where(inside, field, 0.0)
    o_ref[...] = field[:height, :width]


def transpose_kernel(x_ref, *refs):
    o_ref, s_ref = refs[0], refs[-1]
    chunk = 128 * CH
    for j in range(x_ref.shape[1] // chunk):
        s_ref[...] = x_ref[:, pl.ds(chunk * j, chunk)].astype(jnp.float32).T
        for c in range(CH):
            cols = s_ref[pl.ds(c, 128, stride=CH), :]
            o_ref[c, :, pl.ds(128 * j, 128)] = cols.T.astype(o_ref.dtype)
    if len(refs) == 4:
        rows = x_ref.shape[0]
        refs[1][...] = o_ref[:, pl.ds(0, REACH), :]
        refs[2][...] = o_ref[:, pl.ds(rows - REACH, REACH), :]


def channel_major(x, with_ends=False):
    rows, lanes = x.shape
    whole = jax.ShapeDtypeStruct((CH, rows, lanes // CH), x.dtype)
    ends = jax.ShapeDtypeStruct((CH, REACH, lanes // CH), x.dtype)
    return pl.pallas_call(
        transpose_kernel,
        out_shape=(whole, ends, ends) if with_ends else whole,
        scratch_shapes=[pltpu.VMEM((128 * CH, rows), jnp.float32)],
    )(x)


def block_counts(n_ref, t, offsets):
    upper = lax.broadcasted_iota(jnp.int32, (8, 128), 0) < 4
    return [jnp.where(upper, n_ref[2 * t, o], n_ref[2 * t + 1, o]) for o in offsets]


def softmin_tiles(total_y, f_ref, m0_ref, m4_ref, n_ref, o_ref, first, last):
    lanes_total = f_ref.shape[2]

    def body(t, carry):
        r0 = pl.multiple_of(t * 8, 8)
        counts = block_counts(n_ref, t, range(NOFF))
        for j in range(lanes_total // 128):
            peak, den, num = offset_partial(
                total_y, f_ref, m0_ref, m4_ref, counts, r0, range(NOFF), pl.ds(128 * j, 128)
            )
            o_ref[pl.ds(r0, 8), pl.ds(128 * j, 128)] = num / den
        return carry

    lax.fori_loop(first, last, body, 0)


def offset_partial(total_y, f_ref, m0_ref, m4_ref, counts, r0, offsets, lanes):
    fixed = [f_ref[c, pl.ds(r0, 8), lanes] for c in range(CH)]
    scores = []
    for o, n_o in zip(offsets, counts):
        shift = 4 * o
        if shift % 8 == 0:
            src, base = m0_ref, shift
        else:
            src, base = m4_ref, shift - 4
        acc = None
        for c in range(CH):
            d = fixed[c] - src[c, pl.ds(r0 + base, 8), lanes]
            acc = d * d if acc is None else acc + d * d
        scores.append(jnp.where(n_o > 0.0, -acc / softmin_temp, -jnp.inf))
    peak = scores[0]
    for s in scores[1:]:
        peak = jnp.maximum(peak, s)
    base_score = jnp.where(peak == -jnp.inf, 0.0, peak)
    den = None
    num = None
    for o, s, n_o in zip(offsets, scores, counts):
        w = n_o * jnp.exp(s - base_score)
        shift_norm = 2.0 * float(4 * o - REACH) / total_y
        den = w if den is None else den + w
        num = w * shift_norm if num is None else num + w * shift_norm
    return peak, den, num


def edge_tiles(height):
    reach_tiles = REACH // 8
    return list(range(reach_tiles)) + list(range(height // 8 - reach_tiles, height // 8))


def edge_row(t, height):
    return 8 * t if 8 * t < REACH else 8 * t - (height - 2 * REACH)


def halo_offsets(t, height):
    return [o for o in range(NOFF) if 8 * t + 4 * o < REACH or 8 * t + 4 * o + 8 > height + REACH]


def to_channel_major(x_ref, s_ref, store):
    chunk = 128 * CH
    for j in range(x_ref.shape[1] // chunk):
        s_ref[...] = x_ref[:, pl.ds(chunk * j, chunk)].astype(jnp.float32).T
        for c in range(CH):
            store(c, j, s_ref[pl.ds(c, 128, stride=CH), :].T)


def softmin_middle_kernel(
    total_y, n_ref, fx_ref, mt_ref, o_ref, pk_ref, dn_ref, nm_ref, fe_ref, f_ref, m0_ref, m4_ref, s_ref
):
    height = fx_ref.shape[0]
    lanes_total = mt_ref.shape[2]
    rows = height + 2 * REACH

    def store_fixed(c, j, block):
        f_ref[c, :, pl.ds(128 * j, 128)] = block

    to_channel_major(fx_ref, s_ref, store_fixed)
    fe_ref[:, pl.ds(0, REACH), :] = f_ref[:, pl.ds(0, REACH), :].astype(fe_ref.dtype)
    fe_ref[:, pl.ds(REACH, REACH), :] = f_ref[:, pl.ds(height - REACH, REACH), :].astype(fe_ref.dtype)

    def build(c, carry):
        m0_ref[c, pl.ds(REACH, height), :] = mt_ref[c].astype(jnp.float32)
        m0_ref[c, pl.ds(0, REACH), :] = jnp.zeros((REACH, lanes_total), jnp.float32)
        m0_ref[c, pl.ds(REACH + height, REACH), :] = jnp.zeros((REACH, lanes_total), jnp.float32)
        m4_ref[c, pl.ds(0, rows - 8), :] = m0_ref[c, pl.ds(4, rows - 8), :]
        m4_ref[c, pl.ds(rows - 8, 8), :] = jnp.zeros((8, lanes_total), jnp.float32)
        return carry

    lax.fori_loop(0, CH, build, 0)
    tiles = height // 8
    softmin_tiles(total_y, f_ref, m0_ref, m4_ref, n_ref, o_ref, REACH // 8, tiles - REACH // 8)
    for t in edge_tiles(height):
        beyond = halo_offsets(t, height)
        inner = [o for o in range(NOFF) if o not in beyond]
        row = edge_row(t, height)

        def part(j, carry, t=t, inner=inner, row=row):
            lanes = pl.ds(pl.multiple_of(j * 128, 128), 128)
            counts = block_counts(n_ref, t, inner)
            peak, den, num = offset_partial(
                total_y, f_ref, m0_ref, m4_ref, counts, 8 * t, inner, lanes
            )
            pk_ref[pl.ds(row, 8), lanes] = peak
            dn_ref[pl.ds(row, 8), lanes] = den
            nm_ref[pl.ds(row, 8), lanes] = num
            return carry

        lax.fori_loop(0, lanes_total // 128, part, 0)


def softmin_edge_kernel(
    total_y, n_ref, fe_ref, mc_hbm, top_ref, bot_ref, pk_ref, dn_ref, nm_ref, _,
    o_hbm, f_ref, m0_ref, m4_ref, res_ref, me_ref, s_ref, sem,
):
    height = o_hbm.shape[0]
    lanes_total = fe_ref.shape[2]
    rows = height + 2 * REACH
    span = REACH + 16
    copies = [
        pltpu.make_async_copy(mc_hbm.at[:, pl.ds(0, 16), :], me_ref.at[:, pl.ds(0, 16), :], sem.at[4]),
        pltpu.make_async_copy(
            mc_hbm.at[:, pl.ds(height - 16, 16), :], me_ref.at[:, pl.ds(16, 16), :], sem.at[5]
        ),
    ]
    for cp in copies:
        cp.start()

    def store_top(c, j, block):
        m0_ref[c, pl.ds(0, REACH), pl.ds(128 * j, 128)] = block

    def store_bottom(c, j, block):
        m0_ref[c, pl.ds(rows - REACH, REACH), pl.ds(128 * j, 128)] = block

    to_channel_major(top_ref, s_ref, store_top)
    to_channel_major(bot_ref, s_ref, store_bottom)
    for cp in copies:
        cp.wait()

    def build(c, carry):
        f_ref[c, pl.ds(0, REACH), :] = fe_ref[c, pl.ds(0, REACH), :].astype(jnp.float32)
        f_ref[c, pl.ds(height - REACH, REACH), :] = fe_ref[c, pl.ds(REACH, REACH), :].astype(
            jnp.float32
        )
        m0_ref[c, pl.ds(REACH, 16), :] = me_ref[c, pl.ds(0, 16), :].astype(jnp.float32)
        m0_ref[c, pl.ds(rows - span, 16), :] = me_ref[c, pl.ds(16, 16), :].astype(jnp.float32)
        m4_ref[c, pl.ds(0, span - 8), :] = m0_ref[c, pl.ds(4, span - 8), :]
        m4_ref[c, pl.ds(rows - span, span - 8), :] = m0_ref[c, pl.ds(rows - span + 4, span - 8), :]
        m4_ref[c, pl.ds(rows - 8, 8), :] = jnp.zeros((8, lanes_total), jnp.float32)
        return carry

    lax.fori_loop(0, CH, build, 0)
    for t in edge_tiles(height):
        beyond = halo_offsets(t, height)
        row = edge_row(t, height)

        def part(j, carry, t=t, beyond=beyond, row=row):
            lanes = pl.ds(pl.multiple_of(j * 128, 128), 128)
            rows_t = pl.ds(row, 8)
            counts = block_counts(n_ref, t, beyond)
            peak, den, num = offset_partial(
                total_y, f_ref, m0_ref, m4_ref, counts, 8 * t, beyond, lanes
            )
            peak_in = pk_ref[rows_t, lanes]
            top_score = jnp.maximum(peak, peak_in)
            scale = jnp.exp(peak - top_score)
            scale_in = jnp.exp(peak_in - top_score)
            den = den * scale + dn_ref[rows_t, lanes] * scale_in
            num = num * scale + nm_ref[rows_t, lanes] * scale_in
            res_ref[rows_t, lanes] = num / den
            return carry

        lax.fori_loop(0, lanes_total // 128, part, 0)
    head = pltpu.make_async_copy(
        res_ref.at[pl.ds(0, REACH)], o_hbm.at[pl.ds(0, REACH)], sem.at[0]
    )
    tail = pltpu.make_async_copy(
        res_ref.at[pl.ds(REACH, REACH)], o_hbm.at[pl.ds(height - REACH, REACH)], sem.at[1]
    )
    head.start()
    tail.start()
    head.wait()
    tail.wait()


def per_device(fixed_features, moving_features, cand_offsets, cand_lengths, smooth_radii):
    height = fixed_features.shape[0]
    columns_dev = fixed_features.shape[1] // CH
    blocks = height // 4
    total_y = height * lax.axis_size("gy")
    shifts = cand_offsets[:, 0, :]
    counts = cand_lengths[:, 0]
    live = jnp.arange(shifts.shape[1], dtype=jnp.int32)[None, :] < counts[:, None]
    offset_values = 4 * jnp.arange(NOFF, dtype=jnp.int32) - REACH
    hits = (shifts[:, :, None] == offset_values[None, None, :]) & live[:, :, None]
    mult = jnp.sum(hits.astype(jnp.float32), axis=1)

    gy_count = lax.axis_size("gy")
    top_rows = lax.ppermute(
        moving_features[height - REACH :], "gy", [(i, i + 1) for i in range(gy_count - 1)]
    )
    bottom_rows = lax.ppermute(
        moving_features[:REACH], "gy", [(i + 1, i) for i in range(gy_count - 1)]
    )
    moving_c = channel_major(moving_features)

    rows = height + 2 * REACH
    tiles = height // 8
    reach_tiles = REACH // 8
    scratch = [
        pltpu.VMEM((CH, height, columns_dev), jnp.float32),
        pltpu.VMEM((CH, rows, columns_dev), jnp.float32),
        pltpu.VMEM((CH, rows, columns_dev), jnp.float32),
    ]
    params = pltpu.CompilerParams(vmem_limit_bytes=60 * 1024 * 1024)
    out_shape = jax.ShapeDtypeStruct((height, columns_dev), jnp.float32)
    smem = pl.BlockSpec(memory_space=pltpu.SMEM)
    vmem = pl.BlockSpec(memory_space=pltpu.VMEM)
    anywhere = pl.BlockSpec(memory_space=pl.ANY)
    edge_shape = jax.ShapeDtypeStruct((2 * REACH, columns_dev), jnp.float32)
    fixed_edge_shape = jax.ShapeDtypeStruct((CH, 2 * REACH, columns_dev), fixed_features.dtype)
    middle, peak_part, den_part, num_part, fixed_edge = pl.pallas_call(
        lambda *refs: softmin_middle_kernel(total_y, *refs),
        out_shape=(out_shape, edge_shape, edge_shape, edge_shape, fixed_edge_shape),
        in_specs=[smem, vmem, vmem],
        scratch_shapes=scratch + [pltpu.VMEM((128 * CH, height), jnp.float32)],
        compiler_params=params,
    )(mult, fixed_features, moving_c)
    disp_init = pl.pallas_call(
        lambda *refs: softmin_edge_kernel(total_y, *refs),
        out_shape=out_shape,
        in_specs=[smem, vmem, anywhere] + [vmem] * 5 + [anywhere],
        out_specs=anywhere,
        scratch_shapes=scratch
        + [
            pltpu.VMEM((2 * REACH, columns_dev), jnp.float32),
            pltpu.VMEM((CH, 32, columns_dev), jnp.bfloat16),
            pltpu.VMEM((128 * CH, REACH), jnp.float32),
            pltpu.SemaphoreType.DMA((6,)),
        ],
        compiler_params=params,
        input_output_aliases={8: 0},
    )(mult, fixed_edge, moving_c, top_rows, bottom_rows, peak_part, den_part, num_part, middle)

    gz_count = lax.axis_size("gz")
    below = lax.ppermute(disp_init[:HALO_Y], "gy", [(i + 1, i) for i in range(gy_count - 1)])
    above = lax.ppermute(disp_init[-HALO_Y:], "gy", [(i, i + 1) for i in range(gy_count - 1)])

    def ring_columns(lo, hi):
        return jnp.concatenate([disp_init[:, lo:hi], below[:, lo:hi], above[:, lo:hi]], axis=0)

    left = lax.ppermute(
        ring_columns(columns_dev - HALO_Z, columns_dev),
        "gz",
        [(i, i + 1) for i in range(gz_count - 1)],
    )
    right = lax.ppermute(ring_columns(0, HALO_Z), "gz", [(i + 1, i) for i in range(gz_count - 1)])
    position = jnp.stack(
        [lax.axis_index("gy"), lax.axis_index("gz"), jnp.int32(gy_count), jnp.int32(gz_count)]
    ).astype(jnp.int32)
    final_ext = pl.pallas_call(
        adam_kernel,
        out_shape=jax.ShapeDtypeStruct((height, columns_dev), jnp.float32),
        in_specs=[smem, smem, vmem, vmem, vmem],
        scratch_shapes=[
            pltpu.VMEM((height + 2 * HALO_Y, columns_dev + 2 * HALO_Z), jnp.float32)
        ],
        compiler_params=pltpu.CompilerParams(vmem_limit_bytes=32 * 1024 * 1024),
    )(
        smooth_radii.astype(jnp.int32),
        position,
        disp_init,
        jnp.concatenate([below, above], axis=0),
        jnp.concatenate([right, left], axis=1),
    )
    return (disp_init, final_ext)


def solution(mesh):
    in_specs = (P("gy", "gz"), P("gy", "gz"), P("gy", "gz", None), P("gy", "gz"), P())
    out_specs = (P("gy", "gz"), P("gy", "gz"))
    return jax.shard_map(
        per_device, mesh=mesh, in_specs=in_specs, out_specs=out_specs, check_vma=False
    )
```

```python
import jax
import jax.numpy as jnp
from jax import lax
from jax.experimental import pallas as pl
from jax.experimental.pallas import tpu as pltpu
from jax.sharding import PartitionSpec as P

CH = 16
XS = 8
REACH = 32
RMAX = 4
ITERS = 3
NOFF = 2 * (REACH // 4) + 1


softmin_temp = 2.0
smooth_weight = 2.0
adam_rate = 0.2
beta_first = 0.9
beta_second = 0.999
adam_floor = 0.05


def with_halo(cells, sides, width):
    for axis, dim in sides:
        count = lax.axis_size(axis)
        ends = count - 1
        head = lax.slice_in_dim(cells, 0, width, axis=dim)
        tail = lax.slice_in_dim(cells, cells.shape[dim] - width, cells.shape[dim], axis=dim)
        cells = jnp.concatenate(
            [
                lax.ppermute(tail, axis, [(i, (i + 1) % count) for i in range(ends)]),
                cells,
                lax.ppermute(head, axis, [((i + 1) % count, i) for i in range(ends)]),
            ],
            axis=dim,
        )
    return cells


def box_weights(radius):
    spread = jnp.arange(-RMAX, RMAX + 1)
    inside = jnp.abs(spread) <= radius
    return jnp.where(inside, 1.0, 0.0).astype(jnp.float32) / (2 * radius + 1).astype(jnp.float32)


def smooth_inner(padded, radius, margin):
    weights = box_weights(radius)
    height = padded.shape[0] - 2 * margin
    layers = padded.shape[1] - 2 * margin
    depth_cells = padded.shape[2]
    along_y = jnp.zeros((height, padded.shape[1], depth_cells), jnp.float32)
    for offset in range(-RMAX, RMAX + 1):
        along_y = (
            along_y + weights[RMAX + offset] * padded[margin + offset : margin + offset + height]
        )
    along_z = jnp.zeros((height, layers, depth_cells), jnp.float32)
    for offset in range(-RMAX, RMAX + 1):
        along_z = (
            along_z
            + weights[RMAX + offset] * along_y[:, margin + offset : margin + offset + layers]
        )
    x_padded = jnp.pad(along_z, ((0, 0), (0, 0), (RMAX, RMAX)))
    along_x = jnp.zeros((height, layers, depth_cells), jnp.float32)
    for offset in range(-RMAX, RMAX + 1):
        along_x = (
            along_x
            + weights[RMAX + offset] * x_padded[:, :, RMAX + offset : RMAX + offset + depth_cells]
        )
    return along_x


def adam_update(field, target_field, smoothed, first_moment, second_moment, iteration):
    gradient = field - target_field + smooth_weight * (field - smoothed)
    first_moment = beta_first * first_moment + (1.0 - beta_first) * gradient
    second_moment = beta_second * second_moment + (1.0 - beta_second) * gradient * gradient
    first_hat = first_moment / (1.0 - beta_first ** (iteration + 1))
    second_hat = second_moment / (1.0 - beta_second ** (iteration + 1))
    field = field - adam_rate * first_hat / (jnp.sqrt(second_hat) + adam_floor)
    return (field, first_moment, second_moment)


HALO_Y = 8
HALO_Z = 8 * XS
SEND_Y = 8
SEND_Z = 8 * XS


def exchange_halo(cells, wy, wz, send_y, send_z):
    ny = lax.axis_size("gy")
    nz = lax.axis_size("gz")
    top = lax.ppermute(cells[-send_y:], "gy", [(i, i + 1) for i in range(ny - 1)])
    bottom = lax.ppermute(cells[:send_y], "gy", [(i + 1, i) for i in range(ny - 1)])
    cells = jnp.concatenate([top, cells, bottom], axis=0)
    left = lax.ppermute(cells[:, -send_z:], "gz", [(i, i + 1) for i in range(nz - 1)])
    right = lax.ppermute(cells[:, :send_z], "gz", [(i + 1, i) for i in range(nz - 1)])
    cells = jnp.concatenate([left, cells, right], axis=1)
    return jnp.pad(cells, ((wy - send_y, wy - send_y), (wz - send_z, wz - send_z)))


def shifted(a, offset, axis):
    if offset == 0:
        return a
    return pltpu.roll(a, (-offset) % a.shape[axis], axis)


def box_smooth(u, radius, lane_x):
    scale = 1.0 / float(2 * radius + 1)
    along_y = u
    for o in range(1, radius + 1):
        along_y = along_y + shifted(u, -o, 0) + shifted(u, o, 0)
    along_y = along_y * scale
    along_z = along_y
    for o in range(1, radius + 1):
        along_z = along_z + shifted(along_y, -XS * o, 1) + shifted(along_y, XS * o, 1)
    along_z = along_z * scale
    along_x = along_z
    for o in range(1, radius + 1):
        along_x = (
            along_x
            + jnp.where(lane_x >= o, shifted(along_z, -o, 1), 0.0)
            + jnp.where(lane_x < XS - o, shifted(along_z, o, 1), 0.0)
        )
    return along_x * scale


def adam_kernel(radii_ref, pos_ref, d_ref, y_ref, z_ref, o_ref, ext_ref):
    height, width = d_ref.shape
    ext_ref[pl.ds(0, height), pl.ds(0, width)] = d_ref[...]
    ext_ref[pl.ds(height, 2 * HALO_Y), pl.ds(0, width)] = y_ref[...]
    ext_ref[:, pl.ds(width, 2 * HALO_Z)] = z_ref[...]
    target = ext_ref[...]
    rows = lax.broadcasted_iota(jnp.int32, target.shape, 0)
    lanes = lax.broadcasted_iota(jnp.int32, target.shape, 1)
    gy = pos_ref[0]
    gz = pos_ref[1]
    row_ok = (
        (rows < height)
        | ((rows < height + HALO_Y) & (gy < pos_ref[2] - 1))
        | ((rows >= height + HALO_Y) & (gy > 0))
    )
    lane_ok = (
        (lanes < width)
        | ((lanes < width + HALO_Z) & (gz < pos_ref[3] - 1))
        | ((lanes >= width + HALO_Z) & (gz > 0))
    )
    inside = row_ok & lane_ok
    lane_x = lanes % XS
    field = jnp.where(inside, target, 0.0)
    first_moment = jnp.zeros_like(target)
    second_moment = jnp.zeros_like(target)
    for iteration in range(ITERS):
        radius = radii_ref[iteration]
        smoothed = lax.switch(
            jnp.clip(radius - 1, 0, RMAX - 1),
            [lambda u, r=r: box_smooth(u, r, lane_x) for r in range(1, RMAX + 1)],
            field,
        )
        field, first_moment, second_moment = adam_update(
            field, target, smoothed, first_moment, second_moment, iteration
        )
        field = jnp.where(inside, field, 0.0)
    o_ref[...] = field[:height, :width]


def transpose_kernel(x_ref, *refs):
    o_ref, s_ref = refs[0], refs[-1]
    chunk = 128 * CH
    for j in range(x_ref.shape[1] // chunk):
        s_ref[...] = x_ref[:, pl.ds(chunk * j, chunk)].astype(jnp.float32).T
        for c in range(CH):
            cols = s_ref[pl.ds(c, 128, stride=CH), :]
            o_ref[c, :, pl.ds(128 * j, 128)] = cols.T.astype(o_ref.dtype)
    if len(refs) == 4:
        rows = x_ref.shape[0]
        refs[1][...] = o_ref[:, pl.ds(0, REACH), :]
        refs[2][...] = o_ref[:, pl.ds(rows - REACH, REACH), :]


def channel_major(x, with_ends=False):
    rows, lanes = x.shape
    whole = jax.ShapeDtypeStruct((CH, rows, lanes // CH), x.dtype)
    ends = jax.ShapeDtypeStruct((CH, REACH, lanes // CH), x.dtype)
    return pl.pallas_call(
        transpose_kernel,
        out_shape=(whole, ends, ends) if with_ends else whole,
        scratch_shapes=[pltpu.VMEM((128 * CH, rows), jnp.float32)],
    )(x)


def block_counts(n_ref, t, offsets):
    upper = lax.broadcasted_iota(jnp.int32, (8, 128), 0) < 4
    return [jnp.where(upper, n_ref[2 * t, o], n_ref[2 * t + 1, o]) for o in offsets]


def softmin_tiles(total_y, f_ref, m0_ref, m4_ref, n_ref, o_ref, first, last):
    lanes_total = f_ref.shape[2]

    def body(t, carry):
        r0 = pl.multiple_of(t * 8, 8)
        counts = block_counts(n_ref, t, range(NOFF))
        for j in range(lanes_total // 128):
            peak, den, num = offset_partial(
                total_y, f_ref, m0_ref, m4_ref, counts, r0, range(NOFF), pl.ds(128 * j, 128)
            )
            o_ref[pl.ds(r0, 8), pl.ds(128 * j, 128)] = num / den
        return carry

    lax.fori_loop(first, last, body, 0)


def offset_partial(total_y, f_ref, m0_ref, m4_ref, counts, r0, offsets, lanes):
    fixed = [f_ref[c, pl.ds(r0, 8), lanes] for c in range(CH)]
    scores = []
    for o, n_o in zip(offsets, counts):
        shift = 4 * o
        if shift % 8 == 0:
            src, base = m0_ref, shift
        else:
            src, base = m4_ref, shift - 4
        acc = None
        for c in range(CH):
            d = fixed[c] - src[c, pl.ds(r0 + base, 8), lanes]
            acc = d * d if acc is None else acc + d * d
        scores.append(jnp.where(n_o > 0.0, -acc / softmin_temp, -jnp.inf))
    peak = scores[0]
    for s in scores[1:]:
        peak = jnp.maximum(peak, s)
    base_score = jnp.where(peak == -jnp.inf, 0.0, peak)
    den = None
    num = None
    for o, s, n_o in zip(offsets, scores, counts):
        w = n_o * jnp.exp(s - base_score)
        shift_norm = 2.0 * float(4 * o - REACH) / total_y
        den = w if den is None else den + w
        num = w * shift_norm if num is None else num + w * shift_norm
    return peak, den, num


def edge_tiles(height):
    reach_tiles = REACH // 8
    return list(range(reach_tiles)) + list(range(height // 8 - reach_tiles, height // 8))


def edge_row(t, height):
    return 8 * t if 8 * t < REACH else 8 * t - (height - 2 * REACH)


def halo_offsets(t, height):
    return [o for o in range(NOFF) if 8 * t + 4 * o < REACH or 8 * t + 4 * o + 8 > height + REACH]


def to_channel_major(x_ref, s_ref, store):
    chunk = 128 * CH
    for j in range(x_ref.shape[1] // chunk):
        s_ref[...] = x_ref[:, pl.ds(chunk * j, chunk)].astype(jnp.float32).T
        for c in range(CH):
            store(c, j, s_ref[pl.ds(c, 128, stride=CH), :].T)


def softmin_middle_kernel(
    total_y, n_ref, fx_ref, mt_ref, o_ref, pk_ref, dn_ref, nm_ref, fe_ref, f_ref, m0_ref, m4_ref, s_ref
):
    height = fx_ref.shape[0]
    lanes_total = mt_ref.shape[2]
    rows = height + 2 * REACH

    def store_fixed(c, j, block):
        f_ref[c, :, pl.ds(128 * j, 128)] = block

    to_channel_major(fx_ref, s_ref, store_fixed)
    fe_ref[:, pl.ds(0, REACH), :] = f_ref[:, pl.ds(0, REACH), :].astype(fe_ref.dtype)
    fe_ref[:, pl.ds(REACH, REACH), :] = f_ref[:, pl.ds(height - REACH, REACH), :].astype(fe_ref.dtype)

    def build(c, carry):
        m0_ref[c, pl.ds(REACH, height), :] = mt_ref[c].astype(jnp.float32)
        m0_ref[c, pl.ds(0, REACH), :] = jnp.zeros((REACH, lanes_total), jnp.float32)
        m0_ref[c, pl.ds(REACH + height, REACH), :] = jnp.zeros((REACH, lanes_total), jnp.float32)
        m4_ref[c, pl.ds(0, rows - 8), :] = m0_ref[c, pl.ds(4, rows - 8), :]
        m4_ref[c, pl.ds(rows - 8, 8), :] = jnp.zeros((8, lanes_total), jnp.float32)
        return carry

    lax.fori_loop(0, CH, build, 0)
    tiles = height // 8
    softmin_tiles(total_y, f_ref, m0_ref, m4_ref, n_ref, o_ref, REACH // 8, tiles - REACH // 8)
    for t in edge_tiles(height):
        beyond = halo_offsets(t, height)
        inner = [o for o in range(NOFF) if o not in beyond]
        row = edge_row(t, height)

        def part(j, carry, t=t, inner=inner, row=row):
            lanes = pl.ds(pl.multiple_of(j * 128, 128), 128)
            counts = block_counts(n_ref, t, inner)
            peak, den, num = offset_partial(
                total_y, f_ref, m0_ref, m4_ref, counts, 8 * t, inner, lanes
            )
            pk_ref[pl.ds(row, 8), lanes] = peak
            dn_ref[pl.ds(row, 8), lanes] = den
            nm_ref[pl.ds(row, 8), lanes] = num
            return carry

        lax.fori_loop(0, lanes_total // 128, part, 0)


def softmin_edge_kernel(
    total_y, n_ref, fe_ref, mc_hbm, top_ref, bot_ref, pk_ref, dn_ref, nm_ref, _,
    o_hbm, f_ref, m0_ref, m4_ref, res_ref, me_ref, sem,
):
    height = o_hbm.shape[0]
    lanes_total = fe_ref.shape[2]
    rows = height + 2 * REACH
    span = REACH + 16
    copies = [
        pltpu.make_async_copy(mc_hbm.at[:, pl.ds(0, 16), :], me_ref.at[:, pl.ds(0, 16), :], sem.at[4]),
        pltpu.make_async_copy(
            mc_hbm.at[:, pl.ds(height - 16, 16), :], me_ref.at[:, pl.ds(16, 16), :], sem.at[5]
        ),
    ]
    for cp in copies:
        cp.start()

    for cp in copies:
        cp.wait()

    def build(c, carry):
        f_ref[c, pl.ds(0, REACH), :] = fe_ref[c, pl.ds(0, REACH), :].astype(jnp.float32)
        f_ref[c, pl.ds(height - REACH, REACH), :] = fe_ref[c, pl.ds(REACH, REACH), :].astype(
            jnp.float32
        )
        m0_ref[c, pl.ds(0, REACH), :] = top_ref[c].astype(jnp.float32)
        m0_ref[c, pl.ds(rows - REACH, REACH), :] = bot_ref[c].astype(jnp.float32)
        m0_ref[c, pl.ds(REACH, 16), :] = me_ref[c, pl.ds(0, 16), :].astype(jnp.float32)
        m0_ref[c, pl.ds(rows - span, 16), :] = me_ref[c, pl.ds(16, 16), :].astype(jnp.float32)
        m4_ref[c, pl.ds(0, span - 8), :] = m0_ref[c, pl.ds(4, span - 8), :]
        m4_ref[c, pl.ds(rows - span, span - 8), :] = m0_ref[c, pl.ds(rows - span + 4, span - 8), :]
        m4_ref[c, pl.ds(rows - 8, 8), :] = jnp.zeros((8, lanes_total), jnp.float32)
        return carry

    lax.fori_loop(0, CH, build, 0)
    for t in edge_tiles(height):
        beyond = halo_offsets(t, height)
        row = edge_row(t, height)

        def part(j, carry, t=t, beyond=beyond, row=row):
            lanes = pl.ds(pl.multiple_of(j * 128, 128), 128)
            rows_t = pl.ds(row, 8)
            counts = block_counts(n_ref, t, beyond)
            peak, den, num = offset_partial(
                total_y, f_ref, m0_ref, m4_ref, counts, 8 * t, beyond, lanes
            )
            peak_in = pk_ref[rows_t, lanes]
            top_score = jnp.maximum(peak, peak_in)
            scale = jnp.exp(peak - top_score)
            scale_in = jnp.exp(peak_in - top_score)
            den = den * scale + dn_ref[rows_t, lanes] * scale_in
            num = num * scale + nm_ref[rows_t, lanes] * scale_in
            res_ref[rows_t, lanes] = num / den
            return carry

        lax.fori_loop(0, lanes_total // 128, part, 0)
    head = pltpu.make_async_copy(
        res_ref.at[pl.ds(0, REACH)], o_hbm.at[pl.ds(0, REACH)], sem.at[0]
    )
    tail = pltpu.make_async_copy(
        res_ref.at[pl.ds(REACH, REACH)], o_hbm.at[pl.ds(height - REACH, REACH)], sem.at[1]
    )
    head.start()
    tail.start()
    head.wait()
    tail.wait()


def per_device(fixed_features, moving_features, cand_offsets, cand_lengths, smooth_radii):
    height = fixed_features.shape[0]
    columns_dev = fixed_features.shape[1] // CH
    blocks = height // 4
    total_y = height * lax.axis_size("gy")
    shifts = cand_offsets[:, 0, :]
    counts = cand_lengths[:, 0]
    live = jnp.arange(shifts.shape[1], dtype=jnp.int32)[None, :] < counts[:, None]
    offset_values = 4 * jnp.arange(NOFF, dtype=jnp.int32) - REACH
    hits = (shifts[:, :, None] == offset_values[None, None, :]) & live[:, :, None]
    mult = jnp.sum(hits.astype(jnp.float32), axis=1)

    gy_count = lax.axis_size("gy")
    moving_c, moving_head, moving_tail = channel_major(moving_features, with_ends=True)
    top_rows = lax.ppermute(moving_tail, "gy", [(i, i + 1) for i in range(gy_count - 1)])
    bottom_rows = lax.ppermute(moving_head, "gy", [(i + 1, i) for i in range(gy_count - 1)])

    rows = height + 2 * REACH
    tiles = height // 8
    reach_tiles = REACH // 8
    scratch = [
        pltpu.VMEM((CH, height, columns_dev), jnp.float32),
        pltpu.VMEM((CH, rows, columns_dev), jnp.float32),
        pltpu.VMEM((CH, rows, columns_dev), jnp.float32),
    ]
    params = pltpu.CompilerParams(vmem_limit_bytes=60 * 1024 * 1024)
    out_shape = jax.ShapeDtypeStruct((height, columns_dev), jnp.float32)
    smem = pl.BlockSpec(memory_space=pltpu.SMEM)
    vmem = pl.BlockSpec(memory_space=pltpu.VMEM)
    anywhere = pl.BlockSpec(memory_space=pl.ANY)
    edge_shape = jax.ShapeDtypeStruct((2 * REACH, columns_dev), jnp.float32)
    fixed_edge_shape = jax.ShapeDtypeStruct((CH, 2 * REACH, columns_dev), fixed_features.dtype)
    middle, peak_part, den_part, num_part, fixed_edge = pl.pallas_call(
        lambda *refs: softmin_middle_kernel(total_y, *refs),
        out_shape=(out_shape, edge_shape, edge_shape, edge_shape, fixed_edge_shape),
        in_specs=[smem, vmem, vmem],
        scratch_shapes=scratch + [pltpu.VMEM((128 * CH, height), jnp.float32)],
        compiler_params=params,
    )(mult, fixed_features, moving_c)
    disp_init = pl.pallas_call(
        lambda *refs: softmin_edge_kernel(total_y, *refs),
        out_shape=out_shape,
        in_specs=[smem, vmem, anywhere] + [vmem] * 5 + [anywhere],
        out_specs=anywhere,
        scratch_shapes=scratch
        + [
            pltpu.VMEM((2 * REACH, columns_dev), jnp.float32),
            pltpu.VMEM((CH, 32, columns_dev), jnp.bfloat16),
            pltpu.SemaphoreType.DMA((6,)),
        ],
        compiler_params=params,
        input_output_aliases={8: 0},
    )(mult, fixed_edge, moving_c, top_rows, bottom_rows, peak_part, den_part, num_part, middle)

    gz_count = lax.axis_size("gz")
    below = lax.ppermute(disp_init[:HALO_Y], "gy", [(i + 1, i) for i in range(gy_count - 1)])
    above = lax.ppermute(disp_init[-HALO_Y:], "gy", [(i, i + 1) for i in range(gy_count - 1)])

    def ring_columns(lo, hi):
        return jnp.concatenate([disp_init[:, lo:hi], below[:, lo:hi], above[:, lo:hi]], axis=0)

    left = lax.ppermute(
        ring_columns(columns_dev - HALO_Z, columns_dev),
        "gz",
        [(i, i + 1) for i in range(gz_count - 1)],
    )
    right = lax.ppermute(ring_columns(0, HALO_Z), "gz", [(i + 1, i) for i in range(gz_count - 1)])
    position = jnp.stack(
        [lax.axis_index("gy"), lax.axis_index("gz"), jnp.int32(gy_count), jnp.int32(gz_count)]
    ).astype(jnp.int32)
    final_ext = pl.pallas_call(
        adam_kernel,
        out_shape=jax.ShapeDtypeStruct((height, columns_dev), jnp.float32),
        in_specs=[smem, smem, vmem, vmem, vmem],
        scratch_shapes=[
            pltpu.VMEM((height + 2 * HALO_Y, columns_dev + 2 * HALO_Z), jnp.float32)
        ],
        compiler_params=pltpu.CompilerParams(vmem_limit_bytes=32 * 1024 * 1024),
    )(
        smooth_radii.astype(jnp.int32),
        position,
        disp_init,
        jnp.concatenate([below, above], axis=0),
        jnp.concatenate([right, left], axis=1),
    )
    return (disp_init, final_ext)


def solution(mesh):
    in_specs = (P("gy", "gz"), P("gy", "gz"), P("gy", "gz", None), P("gy", "gz"), P())
    out_specs = (P("gy", "gz"), P("gy", "gz"))
    return jax.shard_map(
        per_device, mesh=mesh, in_specs=in_specs, out_specs=out_specs, check_vma=False
    )
```

```python
import jax
import jax.numpy as jnp
from jax import lax
from jax.experimental import pallas as pl
from jax.experimental.pallas import tpu as pltpu
from jax.sharding import PartitionSpec as P

CH = 16
XS = 8
REACH = 32
RMAX = 4
ITERS = 3
NOFF = 2 * (REACH // 4) + 1


softmin_temp = 2.0
smooth_weight = 2.0
adam_rate = 0.2
beta_first = 0.9
beta_second = 0.999
adam_floor = 0.05


def with_halo(cells, sides, width):
    for axis, dim in sides:
        count = lax.axis_size(axis)
        ends = count - 1
        head = lax.slice_in_dim(cells, 0, width, axis=dim)
        tail = lax.slice_in_dim(cells, cells.shape[dim] - width, cells.shape[dim], axis=dim)
        cells = jnp.concatenate(
            [
                lax.ppermute(tail, axis, [(i, (i + 1) % count) for i in range(ends)]),
                cells,
                lax.ppermute(head, axis, [((i + 1) % count, i) for i in range(ends)]),
            ],
            axis=dim,
        )
    return cells


def box_weights(radius):
    spread = jnp.arange(-RMAX, RMAX + 1)
    inside = jnp.abs(spread) <= radius
    return jnp.where(inside, 1.0, 0.0).astype(jnp.float32) / (2 * radius + 1).astype(jnp.float32)


def smooth_inner(padded, radius, margin):
    weights = box_weights(radius)
    height = padded.shape[0] - 2 * margin
    layers = padded.shape[1] - 2 * margin
    depth_cells = padded.shape[2]
    along_y = jnp.zeros((height, padded.shape[1], depth_cells), jnp.float32)
    for offset in range(-RMAX, RMAX + 1):
        along_y = (
            along_y + weights[RMAX + offset] * padded[margin + offset : margin + offset + height]
        )
    along_z = jnp.zeros((height, layers, depth_cells), jnp.float32)
    for offset in range(-RMAX, RMAX + 1):
        along_z = (
            along_z
            + weights[RMAX + offset] * along_y[:, margin + offset : margin + offset + layers]
        )
    x_padded = jnp.pad(along_z, ((0, 0), (0, 0), (RMAX, RMAX)))
    along_x = jnp.zeros((height, layers, depth_cells), jnp.float32)
    for offset in range(-RMAX, RMAX + 1):
        along_x = (
            along_x
            + weights[RMAX + offset] * x_padded[:, :, RMAX + offset : RMAX + offset + depth_cells]
        )
    return along_x


def adam_update(field, target_field, smoothed, first_moment, second_moment, iteration):
    gradient = field - target_field + smooth_weight * (field - smoothed)
    first_moment = beta_first * first_moment + (1.0 - beta_first) * gradient
    second_moment = beta_second * second_moment + (1.0 - beta_second) * gradient * gradient
    first_hat = first_moment / (1.0 - beta_first ** (iteration + 1))
    second_hat = second_moment / (1.0 - beta_second ** (iteration + 1))
    field = field - adam_rate * first_hat / (jnp.sqrt(second_hat) + adam_floor)
    return (field, first_moment, second_moment)


HALO_Y = 8
HALO_Z = 8 * XS
SEND_Y = 8
SEND_Z = 8 * XS


def exchange_halo(cells, wy, wz, send_y, send_z):
    ny = lax.axis_size("gy")
    nz = lax.axis_size("gz")
    top = lax.ppermute(cells[-send_y:], "gy", [(i, i + 1) for i in range(ny - 1)])
    bottom = lax.ppermute(cells[:send_y], "gy", [(i + 1, i) for i in range(ny - 1)])
    cells = jnp.concatenate([top, cells, bottom], axis=0)
    left = lax.ppermute(cells[:, -send_z:], "gz", [(i, i + 1) for i in range(nz - 1)])
    right = lax.ppermute(cells[:, :send_z], "gz", [(i + 1, i) for i in range(nz - 1)])
    cells = jnp.concatenate([left, cells, right], axis=1)
    return jnp.pad(cells, ((wy - send_y, wy - send_y), (wz - send_z, wz - send_z)))


def shifted(a, offset, axis):
    if offset == 0:
        return a
    return pltpu.roll(a, (-offset) % a.shape[axis], axis)


def box_smooth(u, radius, lane_x):
    scale = 1.0 / float(2 * radius + 1)
    along_y = u
    for o in range(1, radius + 1):
        along_y = along_y + shifted(u, -o, 0) + shifted(u, o, 0)
    along_y = along_y * scale
    along_z = along_y
    for o in range(1, radius + 1):
        along_z = along_z + shifted(along_y, -XS * o, 1) + shifted(along_y, XS * o, 1)
    along_z = along_z * scale
    along_x = along_z
    for o in range(1, radius + 1):
        along_x = (
            along_x
            + jnp.where(lane_x >= o, shifted(along_z, -o, 1), 0.0)
            + jnp.where(lane_x < XS - o, shifted(along_z, o, 1), 0.0)
        )
    return along_x * scale


def adam_kernel(radii_ref, d_ref, mask_ref, o_ref):
    target = d_ref[...]
    inside = mask_ref[...] > 0.0
    lane_x = lax.broadcasted_iota(jnp.int32, target.shape, 1) % XS
    field = jnp.where(inside, target, 0.0)
    first_moment = jnp.zeros_like(target)
    second_moment = jnp.zeros_like(target)
    for iteration in range(ITERS):
        radius = radii_ref[iteration]
        smoothed = lax.switch(
            jnp.clip(radius - 1, 0, RMAX - 1),
            [lambda u, r=r: box_smooth(u, r, lane_x) for r in range(1, RMAX + 1)],
            field,
        )
        field, first_moment, second_moment = adam_update(
            field, target, smoothed, first_moment, second_moment, iteration
        )
        field = jnp.where(inside, field, 0.0)
    height = o_ref.shape[0]
    width = o_ref.shape[1]
    o_ref[...] = field[HALO_Y : HALO_Y + height, HALO_Z : HALO_Z + width]


def transpose_kernel(x_ref, *refs):
    o_ref, s_ref = refs[0], refs[-1]
    chunk = 128 * CH
    for j in range(x_ref.shape[1] // chunk):
        s_ref[...] = x_ref[:, pl.ds(chunk * j, chunk)].astype(jnp.float32).T
        for c in range(CH):
            cols = s_ref[pl.ds(c, 128, stride=CH), :]
            o_ref[c, :, pl.ds(128 * j, 128)] = cols.T.astype(o_ref.dtype)
    if len(refs) == 4:
        rows = x_ref.shape[0]
        refs[1][...] = o_ref[:, pl.ds(0, REACH), :]
        refs[2][...] = o_ref[:, pl.ds(rows - REACH, REACH), :]


def channel_major(x, with_ends=False):
    rows, lanes = x.shape
    whole = jax.ShapeDtypeStruct((CH, rows, lanes // CH), x.dtype)
    ends = jax.ShapeDtypeStruct((CH, REACH, lanes // CH), x.dtype)
    return pl.pallas_call(
        transpose_kernel,
        out_shape=(whole, ends, ends) if with_ends else whole,
        scratch_shapes=[pltpu.VMEM((128 * CH, rows), jnp.float32)],
    )(x)


def block_counts(n_ref, t, offsets):
    upper = lax.broadcasted_iota(jnp.int32, (8, 128), 0) < 4
    return [jnp.where(upper, n_ref[2 * t, o], n_ref[2 * t + 1, o]) for o in offsets]


def softmin_tiles(total_y, f_ref, m0_ref, m4_ref, n_ref, o_ref, first, last):
    lanes_total = f_ref.shape[2]

    def body(t, carry):
        r0 = pl.multiple_of(t * 8, 8)
        counts = block_counts(n_ref, t, range(NOFF))
        for j in range(lanes_total // 128):
            peak, den, num = offset_partial(
                total_y, f_ref, m0_ref, m4_ref, counts, r0, range(NOFF), pl.ds(128 * j, 128)
            )
            o_ref[pl.ds(r0, 8), pl.ds(128 * j, 128)] = num / den
        return carry

    lax.fori_loop(first, last, body, 0)


def offset_partial(total_y, f_ref, m0_ref, m4_ref, counts, r0, offsets, lanes):
    fixed = [f_ref[c, pl.ds(r0, 8), lanes] for c in range(CH)]
    scores = []
    for o, n_o in zip(offsets, counts):
        shift = 4 * o
        if shift % 8 == 0:
            src, base = m0_ref, shift
        else:
            src, base = m4_ref, shift - 4
        acc = None
        for c in range(CH):
            d = fixed[c] - src[c, pl.ds(r0 + base, 8), lanes]
            acc = d * d if acc is None else acc + d * d
        scores.append(jnp.where(n_o > 0.0, -acc / softmin_temp, -jnp.inf))
    peak = scores[0]
    for s in scores[1:]:
        peak = jnp.maximum(peak, s)
    base_score = jnp.where(peak == -jnp.inf, 0.0, peak)
    den = None
    num = None
    for o, s, n_o in zip(offsets, scores, counts):
        w = n_o * jnp.exp(s - base_score)
        shift_norm = 2.0 * float(4 * o - REACH) / total_y
        den = w if den is None else den + w
        num = w * shift_norm if num is None else num + w * shift_norm
    return peak, den, num


def edge_tiles(height):
    reach_tiles = REACH // 8
    return list(range(reach_tiles)) + list(range(height // 8 - reach_tiles, height // 8))


def edge_row(t, height):
    return 8 * t if 8 * t < REACH else 8 * t - (height - 2 * REACH)


def halo_offsets(t, height):
    return [o for o in range(NOFF) if 8 * t + 4 * o < REACH or 8 * t + 4 * o + 8 > height + REACH]


def to_channel_major(x_ref, s_ref, store):
    chunk = 128 * CH
    for j in range(x_ref.shape[1] // chunk):
        s_ref[...] = x_ref[:, pl.ds(chunk * j, chunk)].astype(jnp.float32).T
        for c in range(CH):
            store(c, j, s_ref[pl.ds(c, 128, stride=CH), :].T)


def halo_rows_kernel(x_hbm, head_ref, tail_ref, slab_ref, s_ref, sem):
    rows = x_hbm.shape[0]
    copies = [
        pltpu.make_async_copy(x_hbm.at[pl.ds(0, REACH)], slab_ref.at[pl.ds(0, REACH)], sem.at[0]),
        pltpu.make_async_copy(
            x_hbm.at[pl.ds(rows - REACH, REACH)], slab_ref.at[pl.ds(REACH, REACH)], sem.at[1]
        ),
    ]
    for cp in copies:
        cp.start()
    for cp in copies:
        cp.wait()

    def store(c, j, block):
        head_ref[c, :, pl.ds(128 * j, 128)] = block[:REACH].astype(head_ref.dtype)
        tail_ref[c, :, pl.ds(128 * j, 128)] = block[REACH:].astype(tail_ref.dtype)

    to_channel_major(slab_ref, s_ref, store)


def softmin_middle_kernel(
    total_y, n_ref, fx_ref, mt_ref, o_ref, pk_ref, dn_ref, nm_ref, fe_ref, f_ref, m0_ref, m4_ref, s_ref
):
    height = fx_ref.shape[0]
    lanes_total = mt_ref.shape[2]
    rows = height + 2 * REACH

    def store_fixed(c, j, block):
        f_ref[c, :, pl.ds(128 * j, 128)] = block

    to_channel_major(fx_ref, s_ref, store_fixed)
    fe_ref[:, pl.ds(0, REACH), :] = f_ref[:, pl.ds(0, REACH), :].astype(fe_ref.dtype)
    fe_ref[:, pl.ds(REACH, REACH), :] = f_ref[:, pl.ds(height - REACH, REACH), :].astype(fe_ref.dtype)

    def build(c, carry):
        m0_ref[c, pl.ds(REACH, height), :] = mt_ref[c].astype(jnp.float32)
        m0_ref[c, pl.ds(0, REACH), :] = jnp.zeros((REACH, lanes_total), jnp.float32)
        m0_ref[c, pl.ds(REACH + height, REACH), :] = jnp.zeros((REACH, lanes_total), jnp.float32)
        m4_ref[c, pl.ds(0, rows - 8), :] = m0_ref[c, pl.ds(4, rows - 8), :]
        m4_ref[c, pl.ds(rows - 8, 8), :] = jnp.zeros((8, lanes_total), jnp.float32)
        return carry

    lax.fori_loop(0, CH, build, 0)
    tiles = height // 8
    softmin_tiles(total_y, f_ref, m0_ref, m4_ref, n_ref, o_ref, REACH // 8, tiles - REACH // 8)
    for t in edge_tiles(height):
        beyond = halo_offsets(t, height)
        inner = [o for o in range(NOFF) if o not in beyond]
        row = edge_row(t, height)

        def part(j, carry, t=t, inner=inner, row=row):
            lanes = pl.ds(pl.multiple_of(j * 128, 128), 128)
            counts = block_counts(n_ref, t, inner)
            peak, den, num = offset_partial(
                total_y, f_ref, m0_ref, m4_ref, counts, 8 * t, inner, lanes
            )
            pk_ref[pl.ds(row, 8), lanes] = peak
            dn_ref[pl.ds(row, 8), lanes] = den
            nm_ref[pl.ds(row, 8), lanes] = num
            return carry

        lax.fori_loop(0, lanes_total // 128, part, 0)


def softmin_edge_kernel(
    total_y, n_ref, fe_ref, mc_hbm, top_ref, bot_ref, pk_ref, dn_ref, nm_ref, _,
    o_hbm, f_ref, m0_ref, m4_ref, res_ref, me_ref, sem,
):
    height = o_hbm.shape[0]
    lanes_total = fe_ref.shape[2]
    rows = height + 2 * REACH
    span = REACH + 16
    copies = [
        pltpu.make_async_copy(mc_hbm.at[:, pl.ds(0, 16), :], me_ref.at[:, pl.ds(0, 16), :], sem.at[4]),
        pltpu.make_async_copy(
            mc_hbm.at[:, pl.ds(height - 16, 16), :], me_ref.at[:, pl.ds(16, 16), :], sem.at[5]
        ),
    ]
    for cp in copies:
        cp.start()

    for cp in copies:
        cp.wait()

    def build(c, carry):
        f_ref[c, pl.ds(0, REACH), :] = fe_ref[c, pl.ds(0, REACH), :].astype(jnp.float32)
        f_ref[c, pl.ds(height - REACH, REACH), :] = fe_ref[c, pl.ds(REACH, REACH), :].astype(
            jnp.float32
        )
        m0_ref[c, pl.ds(0, REACH), :] = top_ref[c].astype(jnp.float32)
        m0_ref[c, pl.ds(rows - REACH, REACH), :] = bot_ref[c].astype(jnp.float32)
        m0_ref[c, pl.ds(REACH, 16), :] = me_ref[c, pl.ds(0, 16), :].astype(jnp.float32)
        m0_ref[c, pl.ds(rows - span, 16), :] = me_ref[c, pl.ds(16, 16), :].astype(jnp.float32)
        m4_ref[c, pl.ds(0, span - 8), :] = m0_ref[c, pl.ds(4, span - 8), :]
        m4_ref[c, pl.ds(rows - span, span - 8), :] = m0_ref[c, pl.ds(rows - span + 4, span - 8), :]
        m4_ref[c, pl.ds(rows - 8, 8), :] = jnp.zeros((8, lanes_total), jnp.float32)
        return carry

    lax.fori_loop(0, CH, build, 0)
    for t in edge_tiles(height):
        beyond = halo_offsets(t, height)
        row = edge_row(t, height)

        def part(j, carry, t=t, beyond=beyond, row=row):
            lanes = pl.ds(pl.multiple_of(j * 128, 128), 128)
            rows_t = pl.ds(row, 8)
            counts = block_counts(n_ref, t, beyond)
            peak, den, num = offset_partial(
                total_y, f_ref, m0_ref, m4_ref, counts, 8 * t, beyond, lanes
            )
            peak_in = pk_ref[rows_t, lanes]
            top_score = jnp.maximum(peak, peak_in)
            scale = jnp.exp(peak - top_score)
            scale_in = jnp.exp(peak_in - top_score)
            den = den * scale + dn_ref[rows_t, lanes] * scale_in
            num = num * scale + nm_ref[rows_t, lanes] * scale_in
            res_ref[rows_t, lanes] = num / den
            return carry

        lax.fori_loop(0, lanes_total // 128, part, 0)
    head = pltpu.make_async_copy(
        res_ref.at[pl.ds(0, REACH)], o_hbm.at[pl.ds(0, REACH)], sem.at[0]
    )
    tail = pltpu.make_async_copy(
        res_ref.at[pl.ds(REACH, REACH)], o_hbm.at[pl.ds(height - REACH, REACH)], sem.at[1]
    )
    head.start()
    tail.start()
    head.wait()
    tail.wait()


def per_device(fixed_features, moving_features, cand_offsets, cand_lengths, smooth_radii):
    height = fixed_features.shape[0]
    columns_dev = fixed_features.shape[1] // CH
    blocks = height // 4
    total_y = height * lax.axis_size("gy")
    shifts = cand_offsets[:, 0, :]
    counts = cand_lengths[:, 0]
    live = jnp.arange(shifts.shape[1], dtype=jnp.int32)[None, :] < counts[:, None]
    offset_values = 4 * jnp.arange(NOFF, dtype=jnp.int32) - REACH
    hits = (shifts[:, :, None] == offset_values[None, None, :]) & live[:, :, None]
    mult = jnp.sum(hits.astype(jnp.float32), axis=1)

    gy_count = lax.axis_size("gy")
    columns_all = moving_features.shape[1]
    ends = jax.ShapeDtypeStruct((CH, REACH, columns_all // CH), moving_features.dtype)
    moving_head, moving_tail = pl.pallas_call(
        halo_rows_kernel,
        out_shape=(ends, ends),
        in_specs=[pl.BlockSpec(memory_space=pl.ANY)],
        scratch_shapes=[
            pltpu.VMEM((2 * REACH, columns_all), moving_features.dtype),
            pltpu.VMEM((128 * CH, 2 * REACH), jnp.float32),
            pltpu.SemaphoreType.DMA((2,)),
        ],
    )(moving_features)
    top_rows = lax.ppermute(moving_tail, "gy", [(i, i + 1) for i in range(gy_count - 1)])
    bottom_rows = lax.ppermute(moving_head, "gy", [(i + 1, i) for i in range(gy_count - 1)])
    moving_c = channel_major(moving_features)

    rows = height + 2 * REACH
    tiles = height // 8
    reach_tiles = REACH // 8
    scratch = [
        pltpu.VMEM((CH, height, columns_dev), jnp.float32),
        pltpu.VMEM((CH, rows, columns_dev), jnp.float32),
        pltpu.VMEM((CH, rows, columns_dev), jnp.float32),
    ]
    params = pltpu.CompilerParams(vmem_limit_bytes=60 * 1024 * 1024)
    out_shape = jax.ShapeDtypeStruct((height, columns_dev), jnp.float32)
    smem = pl.BlockSpec(memory_space=pltpu.SMEM)
    vmem = pl.BlockSpec(memory_space=pltpu.VMEM)
    anywhere = pl.BlockSpec(memory_space=pl.ANY)
    edge_shape = jax.ShapeDtypeStruct((2 * REACH, columns_dev), jnp.float32)
    fixed_edge_shape = jax.ShapeDtypeStruct((CH, 2 * REACH, columns_dev), fixed_features.dtype)
    middle, peak_part, den_part, num_part, fixed_edge = pl.pallas_call(
        lambda *refs: softmin_middle_kernel(total_y, *refs),
        out_shape=(out_shape, edge_shape, edge_shape, edge_shape, fixed_edge_shape),
        in_specs=[smem, vmem, vmem],
        scratch_shapes=scratch + [pltpu.VMEM((128 * CH, height), jnp.float32)],
        compiler_params=params,
    )(mult, fixed_features, moving_c)
    disp_init = pl.pallas_call(
        lambda *refs: softmin_edge_kernel(total_y, *refs),
        out_shape=out_shape,
        in_specs=[smem, vmem, anywhere] + [vmem] * 5 + [anywhere],
        out_specs=anywhere,
        scratch_shapes=scratch
        + [
            pltpu.VMEM((2 * REACH, columns_dev), jnp.float32),
            pltpu.VMEM((CH, 32, columns_dev), jnp.bfloat16),
            pltpu.SemaphoreType.DMA((6,)),
        ],
        compiler_params=params,
        input_output_aliases={8: 0},
    )(mult, fixed_edge, moving_c, top_rows, bottom_rows, peak_part, den_part, num_part, middle)

    ext = exchange_halo(disp_init, HALO_Y, HALO_Z, SEND_Y, SEND_Z)
    rows_ext, lanes_ext = ext.shape
    row_global = lax.axis_index("gy") * height - HALO_Y + lax.broadcasted_iota(
        jnp.int32, (rows_ext, lanes_ext), 0
    )
    lane_global = lax.axis_index("gz") * columns_dev - HALO_Z + lax.broadcasted_iota(
        jnp.int32, (rows_ext, lanes_ext), 1
    )
    inside = (
        (row_global >= 0)
        & (row_global < total_y)
        & (lane_global >= 0)
        & (lane_global < columns_dev * lax.axis_size("gz"))
    )
    grid_mask = inside.astype(jnp.float32)
    final_ext = pl.pallas_call(
        adam_kernel,
        out_shape=jax.ShapeDtypeStruct((height, columns_dev), jnp.float32),
        in_specs=[
            pl.BlockSpec(memory_space=pltpu.SMEM),
            pl.BlockSpec(memory_space=pltpu.VMEM),
            pl.BlockSpec(memory_space=pltpu.VMEM),
        ],
        compiler_params=pltpu.CompilerParams(vmem_limit_bytes=32 * 1024 * 1024),
    )(smooth_radii.astype(jnp.int32), ext, grid_mask)
    return (disp_init, final_ext)


def solution(mesh):
    in_specs = (P("gy", "gz"), P("gy", "gz"), P("gy", "gz", None), P("gy", "gz"), P())
    out_specs = (P("gy", "gz"), P("gy", "gz"))
    return jax.shard_map(
        per_device, mesh=mesh, in_specs=in_specs, out_specs=out_specs, check_vma=False
    )
```

```python
import jax
import jax.numpy as jnp
from jax import lax
from jax.experimental import pallas as pl
from jax.experimental.pallas import tpu as pltpu
from jax.sharding import PartitionSpec as P

CH = 16
XS = 8
REACH = 32
RMAX = 4
ITERS = 3
NOFF = 2 * (REACH // 4) + 1


softmin_temp = 2.0
smooth_weight = 2.0
adam_rate = 0.2
beta_first = 0.9
beta_second = 0.999
adam_floor = 0.05


def with_halo(cells, sides, width):
    for axis, dim in sides:
        count = lax.axis_size(axis)
        ends = count - 1
        head = lax.slice_in_dim(cells, 0, width, axis=dim)
        tail = lax.slice_in_dim(cells, cells.shape[dim] - width, cells.shape[dim], axis=dim)
        cells = jnp.concatenate(
            [
                lax.ppermute(tail, axis, [(i, (i + 1) % count) for i in range(ends)]),
                cells,
                lax.ppermute(head, axis, [((i + 1) % count, i) for i in range(ends)]),
            ],
            axis=dim,
        )
    return cells


def box_weights(radius):
    spread = jnp.arange(-RMAX, RMAX + 1)
    inside = jnp.abs(spread) <= radius
    return jnp.where(inside, 1.0, 0.0).astype(jnp.float32) / (2 * radius + 1).astype(jnp.float32)


def smooth_inner(padded, radius, margin):
    weights = box_weights(radius)
    height = padded.shape[0] - 2 * margin
    layers = padded.shape[1] - 2 * margin
    depth_cells = padded.shape[2]
    along_y = jnp.zeros((height, padded.shape[1], depth_cells), jnp.float32)
    for offset in range(-RMAX, RMAX + 1):
        along_y = (
            along_y + weights[RMAX + offset] * padded[margin + offset : margin + offset + height]
        )
    along_z = jnp.zeros((height, layers, depth_cells), jnp.float32)
    for offset in range(-RMAX, RMAX + 1):
        along_z = (
            along_z
            + weights[RMAX + offset] * along_y[:, margin + offset : margin + offset + layers]
        )
    x_padded = jnp.pad(along_z, ((0, 0), (0, 0), (RMAX, RMAX)))
    along_x = jnp.zeros((height, layers, depth_cells), jnp.float32)
    for offset in range(-RMAX, RMAX + 1):
        along_x = (
            along_x
            + weights[RMAX + offset] * x_padded[:, :, RMAX + offset : RMAX + offset + depth_cells]
        )
    return along_x


def adam_update(field, target_field, smoothed, first_moment, second_moment, iteration):
    gradient = field - target_field + smooth_weight * (field - smoothed)
    first_moment = beta_first * first_moment + (1.0 - beta_first) * gradient
    second_moment = beta_second * second_moment + (1.0 - beta_second) * gradient * gradient
    first_hat = first_moment / (1.0 - beta_first ** (iteration + 1))
    second_hat = second_moment / (1.0 - beta_second ** (iteration + 1))
    field = field - adam_rate * first_hat / (jnp.sqrt(second_hat) + adam_floor)
    return (field, first_moment, second_moment)


HALO_Y = 8
HALO_Z = 8 * XS
SEND_Y = 8
SEND_Z = 8 * XS


def exchange_halo(cells, wy, wz, send_y, send_z):
    ny = lax.axis_size("gy")
    nz = lax.axis_size("gz")
    top = lax.ppermute(cells[-send_y:], "gy", [(i, i + 1) for i in range(ny - 1)])
    bottom = lax.ppermute(cells[:send_y], "gy", [(i + 1, i) for i in range(ny - 1)])
    cells = jnp.concatenate([top, cells, bottom], axis=0)
    left = lax.ppermute(cells[:, -send_z:], "gz", [(i, i + 1) for i in range(nz - 1)])
    right = lax.ppermute(cells[:, :send_z], "gz", [(i + 1, i) for i in range(nz - 1)])
    cells = jnp.concatenate([left, cells, right], axis=1)
    return jnp.pad(cells, ((wy - send_y, wy - send_y), (wz - send_z, wz - send_z)))


def shifted(a, offset, axis):
    if offset == 0:
        return a
    return pltpu.roll(a, (-offset) % a.shape[axis], axis)


def box_smooth(u, radius, lane_x):
    scale = 1.0 / float(2 * radius + 1)
    along_y = u
    for o in range(1, radius + 1):
        along_y = along_y + shifted(u, -o, 0) + shifted(u, o, 0)
    along_y = along_y * scale
    along_z = along_y
    for o in range(1, radius + 1):
        along_z = along_z + shifted(along_y, -XS * o, 1) + shifted(along_y, XS * o, 1)
    along_z = along_z * scale
    along_x = along_z
    for o in range(1, radius + 1):
        along_x = (
            along_x
            + jnp.where(lane_x >= o, shifted(along_z, -o, 1), 0.0)
            + jnp.where(lane_x < XS - o, shifted(along_z, o, 1), 0.0)
        )
    return along_x * scale


def adam_kernel(radii_ref, d_ref, mask_ref, o_ref):
    target = d_ref[...]
    inside = mask_ref[...] > 0.0
    lane_x = lax.broadcasted_iota(jnp.int32, target.shape, 1) % XS
    field = jnp.where(inside, target, 0.0)
    first_moment = jnp.zeros_like(target)
    second_moment = jnp.zeros_like(target)
    for iteration in range(ITERS):
        radius = radii_ref[iteration]
        smoothed = lax.switch(
            jnp.clip(radius - 1, 0, RMAX - 1),
            [lambda u, r=r: box_smooth(u, r, lane_x) for r in range(1, RMAX + 1)],
            field,
        )
        field, first_moment, second_moment = adam_update(
            field, target, smoothed, first_moment, second_moment, iteration
        )
        field = jnp.where(inside, field, 0.0)
    height = o_ref.shape[0]
    width = o_ref.shape[1]
    o_ref[...] = field[HALO_Y : HALO_Y + height, HALO_Z : HALO_Z + width]


def transpose_kernel(x_ref, *refs):
    o_ref, s_ref = refs[0], refs[-1]
    chunk = 128 * CH
    for j in range(x_ref.shape[1] // chunk):
        s_ref[...] = x_ref[:, pl.ds(chunk * j, chunk)].astype(jnp.float32).T
        for c in range(CH):
            cols = s_ref[pl.ds(c, 128, stride=CH), :]
            o_ref[c, :, pl.ds(128 * j, 128)] = cols.T.astype(o_ref.dtype)
    if len(refs) == 4:
        rows = x_ref.shape[0]
        refs[1][...] = o_ref[:, pl.ds(0, REACH), :]
        refs[2][...] = o_ref[:, pl.ds(rows - REACH, REACH), :]


def channel_major(x, with_ends=False):
    rows, lanes = x.shape
    whole = jax.ShapeDtypeStruct((CH, rows, lanes // CH), x.dtype)
    ends = jax.ShapeDtypeStruct((CH, REACH, lanes // CH), x.dtype)
    return pl.pallas_call(
        transpose_kernel,
        out_shape=(whole, ends, ends) if with_ends else whole,
        scratch_shapes=[pltpu.VMEM((128 * CH, rows), jnp.float32)],
    )(x)


def block_counts(n_ref, t, offsets):
    upper = lax.broadcasted_iota(jnp.int32, (8, 128), 0) < 4
    return [jnp.where(upper, n_ref[2 * t, o], n_ref[2 * t + 1, o]) for o in offsets]


def softmin_tiles(total_y, f_ref, m0_ref, m4_ref, n_ref, o_ref, first, last):
    lanes_total = f_ref.shape[2]

    def body(t, carry):
        r0 = pl.multiple_of(t * 8, 8)
        counts = block_counts(n_ref, t, range(NOFF))
        for j in range(lanes_total // 128):
            peak, den, num = offset_partial(
                total_y, f_ref, m0_ref, m4_ref, counts, r0, range(NOFF), pl.ds(128 * j, 128)
            )
            o_ref[pl.ds(r0, 8), pl.ds(128 * j, 128)] = num / den
        return carry

    lax.fori_loop(first, last, body, 0)


def offset_partial(total_y, f_ref, m0_ref, m4_ref, counts, r0, offsets, lanes):
    fixed = [f_ref[c, pl.ds(r0, 8), lanes] for c in range(CH)]
    scores = []
    for o, n_o in zip(offsets, counts):
        shift = 4 * o
        if shift % 8 == 0:
            src, base = m0_ref, shift
        else:
            src, base = m4_ref, shift - 4
        acc = None
        for c in range(CH):
            d = fixed[c] - src[c, pl.ds(r0 + base, 8), lanes]
            acc = d * d if acc is None else acc + d * d
        scores.append(jnp.where(n_o > 0.0, -acc / softmin_temp, -jnp.inf))
    peak = scores[0]
    for s in scores[1:]:
        peak = jnp.maximum(peak, s)
    base_score = jnp.where(peak == -jnp.inf, 0.0, peak)
    den = None
    num = None
    for o, s, n_o in zip(offsets, scores, counts):
        w = n_o * jnp.exp(s - base_score)
        shift_norm = 2.0 * float(4 * o - REACH) / total_y
        den = w if den is None else den + w
        num = w * shift_norm if num is None else num + w * shift_norm
    return peak, den, num


def edge_tiles(height):
    reach_tiles = REACH // 8
    return list(range(reach_tiles)) + list(range(height // 8 - reach_tiles, height // 8))


def edge_row(t, height):
    return 8 * t if 8 * t < REACH else 8 * t - (height - 2 * REACH)


def halo_offsets(t, height):
    return [o for o in range(NOFF) if 8 * t + 4 * o < REACH or 8 * t + 4 * o + 8 > height + REACH]


def softmin_middle_kernel(total_y, n_ref, ft_ref, mt_ref, o_ref, pk_ref, dn_ref, nm_ref, f_ref, m0_ref, m4_ref):
    height = ft_ref.shape[1]
    lanes_total = ft_ref.shape[2]
    rows = height + 2 * REACH

    def build(c, carry):
        f_ref[c] = ft_ref[c].astype(jnp.float32)
        m0_ref[c, pl.ds(REACH, height), :] = mt_ref[c].astype(jnp.float32)
        m0_ref[c, pl.ds(0, REACH), :] = jnp.zeros((REACH, lanes_total), jnp.float32)
        m0_ref[c, pl.ds(REACH + height, REACH), :] = jnp.zeros((REACH, lanes_total), jnp.float32)
        m4_ref[c, pl.ds(0, rows - 8), :] = m0_ref[c, pl.ds(4, rows - 8), :]
        m4_ref[c, pl.ds(rows - 8, 8), :] = jnp.zeros((8, lanes_total), jnp.float32)
        return carry

    lax.fori_loop(0, CH, build, 0)
    tiles = height // 8
    softmin_tiles(total_y, f_ref, m0_ref, m4_ref, n_ref, o_ref, REACH // 8, tiles - REACH // 8)
    for t in edge_tiles(height):
        beyond = halo_offsets(t, height)
        inner = [o for o in range(NOFF) if o not in beyond]
        row = edge_row(t, height)

        def part(j, carry, t=t, inner=inner, row=row):
            lanes = pl.ds(pl.multiple_of(j * 128, 128), 128)
            counts = block_counts(n_ref, t, inner)
            peak, den, num = offset_partial(
                total_y, f_ref, m0_ref, m4_ref, counts, 8 * t, inner, lanes
            )
            pk_ref[pl.ds(row, 8), lanes] = peak
            dn_ref[pl.ds(row, 8), lanes] = den
            nm_ref[pl.ds(row, 8), lanes] = num
            return carry

        lax.fori_loop(0, lanes_total // 128, part, 0)


def softmin_edge_kernel(
    total_y, n_ref, fc_hbm, mc_hbm, top_hbm, bot_hbm, pk_ref, dn_ref, nm_ref, _,
    o_hbm, f_ref, m0_ref, m4_ref, res_ref, fe_ref, me_ref, top_ref, bot_ref, sem,
):
    height = o_hbm.shape[0]
    lanes_total = fe_ref.shape[2]
    rows = height + 2 * REACH
    span = REACH + 16
    halo_copies = [
        pltpu.make_async_copy(top_hbm, top_ref, sem.at[6]),
        pltpu.make_async_copy(bot_hbm, bot_ref, sem.at[7]),
    ]
    fixed_copies = [
        pltpu.make_async_copy(
            fc_hbm.at[:, pl.ds(0, REACH), :], fe_ref.at[:, pl.ds(0, REACH), :], sem.at[2]
        ),
        pltpu.make_async_copy(
            fc_hbm.at[:, pl.ds(height - REACH, REACH), :], fe_ref.at[:, pl.ds(REACH, REACH), :], sem.at[3]
        ),
    ]
    moving_copies = [
        pltpu.make_async_copy(mc_hbm.at[:, pl.ds(0, 16), :], me_ref.at[:, pl.ds(0, 16), :], sem.at[4]),
        pltpu.make_async_copy(
            mc_hbm.at[:, pl.ds(height - 16, 16), :], me_ref.at[:, pl.ds(16, 16), :], sem.at[5]
        ),
    ]
    for cp in halo_copies + fixed_copies + moving_copies:
        cp.start()
    for cp in halo_copies:
        cp.wait()

    def build_halo(c, carry):
        m0_ref[c, pl.ds(0, REACH), :] = top_ref[c].astype(jnp.float32)
        m0_ref[c, pl.ds(rows - REACH, REACH), :] = bot_ref[c].astype(jnp.float32)
        return carry

    lax.fori_loop(0, CH, build_halo, 0)
    for cp in fixed_copies:
        cp.wait()

    def build_fixed(c, carry):
        f_ref[c, pl.ds(0, REACH), :] = fe_ref[c, pl.ds(0, REACH), :].astype(jnp.float32)
        f_ref[c, pl.ds(height - REACH, REACH), :] = fe_ref[c, pl.ds(REACH, REACH), :].astype(
            jnp.float32
        )
        return carry

    lax.fori_loop(0, CH, build_fixed, 0)
    for cp in moving_copies:
        cp.wait()

    def build(c, carry):
        m0_ref[c, pl.ds(REACH, 16), :] = me_ref[c, pl.ds(0, 16), :].astype(jnp.float32)
        m0_ref[c, pl.ds(rows - span, 16), :] = me_ref[c, pl.ds(16, 16), :].astype(jnp.float32)
        m4_ref[c, pl.ds(0, span - 8), :] = m0_ref[c, pl.ds(4, span - 8), :]
        m4_ref[c, pl.ds(rows - span, span - 8), :] = m0_ref[c, pl.ds(rows - span + 4, span - 8), :]
        m4_ref[c, pl.ds(rows - 8, 8), :] = jnp.zeros((8, lanes_total), jnp.float32)
        return carry

    lax.fori_loop(0, CH, build, 0)
    for t in edge_tiles(height):
        beyond = halo_offsets(t, height)
        row = edge_row(t, height)

        def part(j, carry, t=t, beyond=beyond, row=row):
            lanes = pl.ds(pl.multiple_of(j * 128, 128), 128)
            rows_t = pl.ds(row, 8)
            counts = block_counts(n_ref, t, beyond)
            peak, den, num = offset_partial(
                total_y, f_ref, m0_ref, m4_ref, counts, 8 * t, beyond, lanes
            )
            peak_in = pk_ref[rows_t, lanes]
            top_score = jnp.maximum(peak, peak_in)
            scale = jnp.exp(peak - top_score)
            scale_in = jnp.exp(peak_in - top_score)
            den = den * scale + dn_ref[rows_t, lanes] * scale_in
            num = num * scale + nm_ref[rows_t, lanes] * scale_in
            res_ref[rows_t, lanes] = num / den
            return carry

        lax.fori_loop(0, lanes_total // 128, part, 0)
    head = pltpu.make_async_copy(
        res_ref.at[pl.ds(0, REACH)], o_hbm.at[pl.ds(0, REACH)], sem.at[0]
    )
    tail = pltpu.make_async_copy(
        res_ref.at[pl.ds(REACH, REACH)], o_hbm.at[pl.ds(height - REACH, REACH)], sem.at[1]
    )
    head.start()
    tail.start()
    head.wait()
    tail.wait()


def per_device(fixed_features, moving_features, cand_offsets, cand_lengths, smooth_radii):
    height = fixed_features.shape[0]
    columns_dev = fixed_features.shape[1] // CH
    blocks = height // 4
    total_y = height * lax.axis_size("gy")
    shifts = cand_offsets[:, 0, :]
    counts = cand_lengths[:, 0]
    live = jnp.arange(shifts.shape[1], dtype=jnp.int32)[None, :] < counts[:, None]
    offset_values = 4 * jnp.arange(NOFF, dtype=jnp.int32) - REACH
    hits = (shifts[:, :, None] == offset_values[None, None, :]) & live[:, :, None]
    mult = jnp.sum(hits.astype(jnp.float32), axis=1)

    gy_count = lax.axis_size("gy")
    fixed_c = channel_major(fixed_features)
    moving_c, moving_head, moving_tail = channel_major(moving_features, with_ends=True)
    top_rows = lax.ppermute(moving_tail, "gy", [(i, i + 1) for i in range(gy_count - 1)])
    bottom_rows = lax.ppermute(moving_head, "gy", [(i + 1, i) for i in range(gy_count - 1)])

    rows = height + 2 * REACH
    tiles = height // 8
    reach_tiles = REACH // 8
    scratch = [
        pltpu.VMEM((CH, height, columns_dev), jnp.float32),
        pltpu.VMEM((CH, rows, columns_dev), jnp.float32),
        pltpu.VMEM((CH, rows, columns_dev), jnp.float32),
    ]
    params = pltpu.CompilerParams(vmem_limit_bytes=60 * 1024 * 1024)
    out_shape = jax.ShapeDtypeStruct((height, columns_dev), jnp.float32)
    smem = pl.BlockSpec(memory_space=pltpu.SMEM)
    vmem = pl.BlockSpec(memory_space=pltpu.VMEM)
    anywhere = pl.BlockSpec(memory_space=pl.ANY)
    edge_shape = jax.ShapeDtypeStruct((2 * REACH, columns_dev), jnp.float32)
    middle, peak_part, den_part, num_part = pl.pallas_call(
        lambda *refs: softmin_middle_kernel(total_y, *refs),
        out_shape=(out_shape, edge_shape, edge_shape, edge_shape),
        in_specs=[smem, vmem, vmem],
        scratch_shapes=scratch,
        compiler_params=params,
    )(mult, fixed_c, moving_c)
    disp_init = pl.pallas_call(
        lambda *refs: softmin_edge_kernel(total_y, *refs),
        out_shape=out_shape,
        in_specs=[smem] + [anywhere] * 4 + [vmem] * 3 + [anywhere],
        out_specs=anywhere,
        scratch_shapes=scratch
        + [
            pltpu.VMEM((2 * REACH, columns_dev), jnp.float32),
            pltpu.VMEM((CH, 2 * REACH, columns_dev), jnp.bfloat16),
            pltpu.VMEM((CH, 32, columns_dev), jnp.bfloat16),
            pltpu.VMEM((CH, REACH, columns_dev), jnp.bfloat16),
            pltpu.VMEM((CH, REACH, columns_dev), jnp.bfloat16),
            pltpu.SemaphoreType.DMA((8,)),
        ],
        compiler_params=params,
        input_output_aliases={8: 0},
    )(mult, fixed_c, moving_c, top_rows, bottom_rows, peak_part, den_part, num_part, middle)

    ext = exchange_halo(disp_init, HALO_Y, HALO_Z, SEND_Y, SEND_Z)
    rows_ext, lanes_ext = ext.shape
    row_global = lax.axis_index("gy") * height - HALO_Y + lax.broadcasted_iota(
        jnp.int32, (rows_ext, lanes_ext), 0
    )
    lane_global = lax.axis_index("gz") * columns_dev - HALO_Z + lax.broadcasted_iota(
        jnp.int32, (rows_ext, lanes_ext), 1
    )
    inside = (
        (row_global >= 0)
        & (row_global < total_y)
        & (lane_global >= 0)
        & (lane_global < columns_dev * lax.axis_size("gz"))
    )
    grid_mask = inside.astype(jnp.float32)
    final_ext = pl.pallas_call(
        adam_kernel,
        out_shape=jax.ShapeDtypeStruct((height, columns_dev), jnp.float32),
        in_specs=[
            pl.BlockSpec(memory_space=pltpu.SMEM),
            pl.BlockSpec(memory_space=pltpu.VMEM),
            pl.BlockSpec(memory_space=pltpu.VMEM),
        ],
        compiler_params=pltpu.CompilerParams(vmem_limit_bytes=32 * 1024 * 1024),
    )(smooth_radii.astype(jnp.int32), ext, grid_mask)
    return (disp_init, final_ext)


def solution(mesh):
    in_specs = (P("gy", "gz"), P("gy", "gz"), P("gy", "gz", None), P("gy", "gz"), P())
    out_specs = (P("gy", "gz"), P("gy", "gz"))
    return jax.shard_map(
        per_device, mesh=mesh, in_specs=in_specs, out_specs=out_specs, check_vma=False
    )
```

```python
import jax
import jax.numpy as jnp
from jax import lax
from jax.experimental import pallas as pl
from jax.experimental.pallas import tpu as pltpu
from jax.sharding import PartitionSpec as P

CH = 16
XS = 8
REACH = 32
RMAX = 4
ITERS = 3
NOFF = 2 * (REACH // 4) + 1


softmin_temp = 2.0
smooth_weight = 2.0
adam_rate = 0.2
beta_first = 0.9
beta_second = 0.999
adam_floor = 0.05


def with_halo(cells, sides, width):
    for axis, dim in sides:
        count = lax.axis_size(axis)
        ends = count - 1
        head = lax.slice_in_dim(cells, 0, width, axis=dim)
        tail = lax.slice_in_dim(cells, cells.shape[dim] - width, cells.shape[dim], axis=dim)
        cells = jnp.concatenate(
            [
                lax.ppermute(tail, axis, [(i, (i + 1) % count) for i in range(ends)]),
                cells,
                lax.ppermute(head, axis, [((i + 1) % count, i) for i in range(ends)]),
            ],
            axis=dim,
        )
    return cells


def box_weights(radius):
    spread = jnp.arange(-RMAX, RMAX + 1)
    inside = jnp.abs(spread) <= radius
    return jnp.where(inside, 1.0, 0.0).astype(jnp.float32) / (2 * radius + 1).astype(jnp.float32)


def smooth_inner(padded, radius, margin):
    weights = box_weights(radius)
    height = padded.shape[0] - 2 * margin
    layers = padded.shape[1] - 2 * margin
    depth_cells = padded.shape[2]
    along_y = jnp.zeros((height, padded.shape[1], depth_cells), jnp.float32)
    for offset in range(-RMAX, RMAX + 1):
        along_y = (
            along_y + weights[RMAX + offset] * padded[margin + offset : margin + offset + height]
        )
    along_z = jnp.zeros((height, layers, depth_cells), jnp.float32)
    for offset in range(-RMAX, RMAX + 1):
        along_z = (
            along_z
            + weights[RMAX + offset] * along_y[:, margin + offset : margin + offset + layers]
        )
    x_padded = jnp.pad(along_z, ((0, 0), (0, 0), (RMAX, RMAX)))
    along_x = jnp.zeros((height, layers, depth_cells), jnp.float32)
    for offset in range(-RMAX, RMAX + 1):
        along_x = (
            along_x
            + weights[RMAX + offset] * x_padded[:, :, RMAX + offset : RMAX + offset + depth_cells]
        )
    return along_x


def adam_update(field, target_field, smoothed, first_moment, second_moment, iteration):
    gradient = field - target_field + smooth_weight * (field - smoothed)
    first_moment = beta_first * first_moment + (1.0 - beta_first) * gradient
    second_moment = beta_second * second_moment + (1.0 - beta_second) * gradient * gradient
    first_hat = first_moment / (1.0 - beta_first ** (iteration + 1))
    second_hat = second_moment / (1.0 - beta_second ** (iteration + 1))
    field = field - adam_rate * first_hat / (jnp.sqrt(second_hat) + adam_floor)
    return (field, first_moment, second_moment)


HALO_Y = 8
HALO_Z = 8 * XS
SEND_Y = 8
SEND_Z = 8 * XS


def exchange_halo(cells, head, tail, wy, wz, send_y, send_z):
    ny = lax.axis_size("gy")
    nz = lax.axis_size("gz")
    top = lax.ppermute(tail, "gy", [(i, i + 1) for i in range(ny - 1)])
    bottom = lax.ppermute(head, "gy", [(i + 1, i) for i in range(ny - 1)])
    cells = jnp.concatenate([top, cells, bottom], axis=0)
    left = lax.ppermute(cells[:, -send_z:], "gz", [(i, i + 1) for i in range(nz - 1)])
    right = lax.ppermute(cells[:, :send_z], "gz", [(i + 1, i) for i in range(nz - 1)])
    cells = jnp.concatenate([left, cells, right], axis=1)
    return jnp.pad(cells, ((wy - send_y, wy - send_y), (wz - send_z, wz - send_z)))


def shifted(a, offset, axis):
    if offset == 0:
        return a
    return pltpu.roll(a, (-offset) % a.shape[axis], axis)


def box_smooth(u, radius, lane_x):
    scale = 1.0 / float(2 * radius + 1)
    along_y = u
    for o in range(1, radius + 1):
        along_y = along_y + shifted(u, -o, 0) + shifted(u, o, 0)
    along_y = along_y * scale
    along_z = along_y
    for o in range(1, radius + 1):
        along_z = along_z + shifted(along_y, -XS * o, 1) + shifted(along_y, XS * o, 1)
    along_z = along_z * scale
    along_x = along_z
    for o in range(1, radius + 1):
        along_x = (
            along_x
            + jnp.where(lane_x >= o, shifted(along_z, -o, 1), 0.0)
            + jnp.where(lane_x < XS - o, shifted(along_z, o, 1), 0.0)
        )
    return along_x * scale


def adam_kernel(radii_ref, d_ref, mask_ref, o_ref):
    target = d_ref[...]
    inside = mask_ref[...] > 0.0
    lane_x = lax.broadcasted_iota(jnp.int32, target.shape, 1) % XS
    field = jnp.where(inside, target, 0.0)
    first_moment = jnp.zeros_like(target)
    second_moment = jnp.zeros_like(target)
    for iteration in range(ITERS):
        radius = radii_ref[iteration]
        smoothed = lax.switch(
            jnp.clip(radius - 1, 0, RMAX - 1),
            [lambda u, r=r: box_smooth(u, r, lane_x) for r in range(1, RMAX + 1)],
            field,
        )
        field, first_moment, second_moment = adam_update(
            field, target, smoothed, first_moment, second_moment, iteration
        )
        field = jnp.where(inside, field, 0.0)
    height = o_ref.shape[0]
    width = o_ref.shape[1]
    o_ref[...] = field[HALO_Y : HALO_Y + height, HALO_Z : HALO_Z + width]


def transpose_kernel(x_ref, *refs):
    o_ref, s_ref = refs[0], refs[-1]
    chunk = 128 * CH
    for j in range(x_ref.shape[1] // chunk):
        s_ref[...] = x_ref[:, pl.ds(chunk * j, chunk)].astype(jnp.float32).T
        for c in range(CH):
            cols = s_ref[pl.ds(c, 128, stride=CH), :]
            o_ref[c, :, pl.ds(128 * j, 128)] = cols.T.astype(o_ref.dtype)
    if len(refs) == 4:
        rows = x_ref.shape[0]
        refs[1][...] = o_ref[:, pl.ds(0, REACH), :]
        refs[2][...] = o_ref[:, pl.ds(rows - REACH, REACH), :]


def channel_major(x, with_ends=False):
    rows, lanes = x.shape
    whole = jax.ShapeDtypeStruct((CH, rows, lanes // CH), x.dtype)
    ends = jax.ShapeDtypeStruct((CH, REACH, lanes // CH), x.dtype)
    return pl.pallas_call(
        transpose_kernel,
        out_shape=(whole, ends, ends) if with_ends else whole,
        scratch_shapes=[pltpu.VMEM((128 * CH, rows), jnp.float32)],
    )(x)


def block_counts(n_ref, t, offsets):
    upper = lax.broadcasted_iota(jnp.int32, (8, 128), 0) < 4
    return [jnp.where(upper, n_ref[2 * t, o], n_ref[2 * t + 1, o]) for o in offsets]


def softmin_tiles(total_y, f_ref, m0_ref, m4_ref, n_ref, o_ref, first, last):
    lanes_total = f_ref.shape[2]

    def body(t, carry):
        r0 = pl.multiple_of(t * 8, 8)
        counts = block_counts(n_ref, t, range(NOFF))
        for j in range(lanes_total // 128):
            peak, den, num = offset_partial(
                total_y, f_ref, m0_ref, m4_ref, counts, r0, range(NOFF), pl.ds(128 * j, 128)
            )
            o_ref[pl.ds(r0, 8), pl.ds(128 * j, 128)] = num / den
        return carry

    lax.fori_loop(first, last, body, 0)


def offset_partial(total_y, f_ref, m0_ref, m4_ref, counts, r0, offsets, lanes):
    fixed = [f_ref[c, pl.ds(r0, 8), lanes] for c in range(CH)]
    scores = []
    for o, n_o in zip(offsets, counts):
        shift = 4 * o
        if shift % 8 == 0:
            src, base = m0_ref, shift
        else:
            src, base = m4_ref, shift - 4
        acc = None
        for c in range(CH):
            d = fixed[c] - src[c, pl.ds(r0 + base, 8), lanes]
            acc = d * d if acc is None else acc + d * d
        scores.append(jnp.where(n_o > 0.0, -acc / softmin_temp, -jnp.inf))
    peak = scores[0]
    for s in scores[1:]:
        peak = jnp.maximum(peak, s)
    base_score = jnp.where(peak == -jnp.inf, 0.0, peak)
    den = None
    num = None
    for o, s, n_o in zip(offsets, scores, counts):
        w = n_o * jnp.exp(s - base_score)
        shift_norm = 2.0 * float(4 * o - REACH) / total_y
        den = w if den is None else den + w
        num = w * shift_norm if num is None else num + w * shift_norm
    return peak, den, num


def edge_tiles(height):
    reach_tiles = REACH // 8
    return list(range(reach_tiles)) + list(range(height // 8 - reach_tiles, height // 8))


def edge_row(t, height):
    return 8 * t if 8 * t < REACH else 8 * t - (height - 2 * REACH)


def halo_offsets(t, height):
    return [o for o in range(NOFF) if 8 * t + 4 * o < REACH or 8 * t + 4 * o + 8 > height + REACH]


def softmin_middle_kernel(total_y, n_ref, ft_ref, mt_ref, o_ref, pk_ref, dn_ref, nm_ref, f_ref, m0_ref, m4_ref):
    height = ft_ref.shape[1]
    lanes_total = ft_ref.shape[2]
    rows = height + 2 * REACH

    def build(c, carry):
        f_ref[c] = ft_ref[c].astype(jnp.float32)
        m0_ref[c, pl.ds(REACH, height), :] = mt_ref[c].astype(jnp.float32)
        m0_ref[c, pl.ds(0, REACH), :] = jnp.zeros((REACH, lanes_total), jnp.float32)
        m0_ref[c, pl.ds(REACH + height, REACH), :] = jnp.zeros((REACH, lanes_total), jnp.float32)
        m4_ref[c, pl.ds(0, rows - 8), :] = m0_ref[c, pl.ds(4, rows - 8), :]
        m4_ref[c, pl.ds(rows - 8, 8), :] = jnp.zeros((8, lanes_total), jnp.float32)
        return carry

    lax.fori_loop(0, CH, build, 0)
    tiles = height // 8
    softmin_tiles(total_y, f_ref, m0_ref, m4_ref, n_ref, o_ref, REACH // 8, tiles - REACH // 8)
    for t in edge_tiles(height):
        beyond = halo_offsets(t, height)
        inner = [o for o in range(NOFF) if o not in beyond]
        row = edge_row(t, height)

        def part(j, carry, t=t, inner=inner, row=row):
            lanes = pl.ds(pl.multiple_of(j * 128, 128), 128)
            counts = block_counts(n_ref, t, inner)
            peak, den, num = offset_partial(
                total_y, f_ref, m0_ref, m4_ref, counts, 8 * t, inner, lanes
            )
            pk_ref[pl.ds(row, 8), lanes] = peak
            dn_ref[pl.ds(row, 8), lanes] = den
            nm_ref[pl.ds(row, 8), lanes] = num
            return carry

        lax.fori_loop(0, lanes_total // 128, part, 0)


def softmin_edge_kernel(
    total_y, n_ref, fc_hbm, mc_hbm, top_hbm, bot_hbm, pk_ref, dn_ref, nm_ref, _,
    o_hbm, head_ref, tail_ref, f_ref, m0_ref, m4_ref, res_ref, fe_ref, me_ref, top_ref, bot_ref, sem,
):
    height = o_hbm.shape[0]
    lanes_total = fe_ref.shape[2]
    rows = height + 2 * REACH
    span = REACH + 16
    halo_copies = [
        pltpu.make_async_copy(top_hbm, top_ref, sem.at[6]),
        pltpu.make_async_copy(bot_hbm, bot_ref, sem.at[7]),
    ]
    fixed_copies = [
        pltpu.make_async_copy(
            fc_hbm.at[:, pl.ds(0, REACH), :], fe_ref.at[:, pl.ds(0, REACH), :], sem.at[2]
        ),
        pltpu.make_async_copy(
            fc_hbm.at[:, pl.ds(height - REACH, REACH), :], fe_ref.at[:, pl.ds(REACH, REACH), :], sem.at[3]
        ),
    ]
    moving_copies = [
        pltpu.make_async_copy(mc_hbm.at[:, pl.ds(0, 16), :], me_ref.at[:, pl.ds(0, 16), :], sem.at[4]),
        pltpu.make_async_copy(
            mc_hbm.at[:, pl.ds(height - 16, 16), :], me_ref.at[:, pl.ds(16, 16), :], sem.at[5]
        ),
    ]
    for cp in halo_copies + fixed_copies + moving_copies:
        cp.start()
    for cp in halo_copies:
        cp.wait()

    def build_halo(c, carry):
        m0_ref[c, pl.ds(0, REACH), :] = top_ref[c].astype(jnp.float32)
        m0_ref[c, pl.ds(rows - REACH, REACH), :] = bot_ref[c].astype(jnp.float32)
        return carry

    lax.fori_loop(0, CH, build_halo, 0)
    for cp in fixed_copies:
        cp.wait()

    def build_fixed(c, carry):
        f_ref[c, pl.ds(0, REACH), :] = fe_ref[c, pl.ds(0, REACH), :].astype(jnp.float32)
        f_ref[c, pl.ds(height - REACH, REACH), :] = fe_ref[c, pl.ds(REACH, REACH), :].astype(
            jnp.float32
        )
        return carry

    lax.fori_loop(0, CH, build_fixed, 0)
    for cp in moving_copies:
        cp.wait()

    def build(c, carry):
        m0_ref[c, pl.ds(REACH, 16), :] = me_ref[c, pl.ds(0, 16), :].astype(jnp.float32)
        m0_ref[c, pl.ds(rows - span, 16), :] = me_ref[c, pl.ds(16, 16), :].astype(jnp.float32)
        m4_ref[c, pl.ds(0, span - 8), :] = m0_ref[c, pl.ds(4, span - 8), :]
        m4_ref[c, pl.ds(rows - span, span - 8), :] = m0_ref[c, pl.ds(rows - span + 4, span - 8), :]
        m4_ref[c, pl.ds(rows - 8, 8), :] = jnp.zeros((8, lanes_total), jnp.float32)
        return carry

    lax.fori_loop(0, CH, build, 0)
    for t in edge_tiles(height):
        beyond = halo_offsets(t, height)
        row = edge_row(t, height)

        def part(j, carry, t=t, beyond=beyond, row=row):
            lanes = pl.ds(pl.multiple_of(j * 128, 128), 128)
            rows_t = pl.ds(row, 8)
            counts = block_counts(n_ref, t, beyond)
            peak, den, num = offset_partial(
                total_y, f_ref, m0_ref, m4_ref, counts, 8 * t, beyond, lanes
            )
            peak_in = pk_ref[rows_t, lanes]
            top_score = jnp.maximum(peak, peak_in)
            scale = jnp.exp(peak - top_score)
            scale_in = jnp.exp(peak_in - top_score)
            den = den * scale + dn_ref[rows_t, lanes] * scale_in
            num = num * scale + nm_ref[rows_t, lanes] * scale_in
            res_ref[rows_t, lanes] = num / den
            return carry

        lax.fori_loop(0, lanes_total // 128, part, 0)
    head = pltpu.make_async_copy(
        res_ref.at[pl.ds(0, REACH)], o_hbm.at[pl.ds(0, REACH)], sem.at[0]
    )
    tail = pltpu.make_async_copy(
        res_ref.at[pl.ds(REACH, REACH)], o_hbm.at[pl.ds(height - REACH, REACH)], sem.at[1]
    )
    head.start()
    tail.start()
    head_ref[...] = res_ref[pl.ds(0, head_ref.shape[0]), :]
    tail_ref[...] = res_ref[pl.ds(2 * REACH - tail_ref.shape[0], tail_ref.shape[0]), :]
    head.wait()
    tail.wait()


def per_device(fixed_features, moving_features, cand_offsets, cand_lengths, smooth_radii):
    height = fixed_features.shape[0]
    columns_dev = fixed_features.shape[1] // CH
    blocks = height // 4
    total_y = height * lax.axis_size("gy")
    shifts = cand_offsets[:, 0, :]
    counts = cand_lengths[:, 0]
    live = jnp.arange(shifts.shape[1], dtype=jnp.int32)[None, :] < counts[:, None]
    offset_values = 4 * jnp.arange(NOFF, dtype=jnp.int32) - REACH
    hits = (shifts[:, :, None] == offset_values[None, None, :]) & live[:, :, None]
    mult = jnp.sum(hits.astype(jnp.float32), axis=1)

    gy_count = lax.axis_size("gy")
    fixed_c = channel_major(fixed_features)
    moving_c, moving_head, moving_tail = channel_major(moving_features, with_ends=True)
    top_rows = lax.ppermute(moving_tail, "gy", [(i, i + 1) for i in range(gy_count - 1)])
    bottom_rows = lax.ppermute(moving_head, "gy", [(i + 1, i) for i in range(gy_count - 1)])

    rows = height + 2 * REACH
    tiles = height // 8
    reach_tiles = REACH // 8
    scratch = [
        pltpu.VMEM((CH, height, columns_dev), jnp.float32),
        pltpu.VMEM((CH, rows, columns_dev), jnp.float32),
        pltpu.VMEM((CH, rows, columns_dev), jnp.float32),
    ]
    params = pltpu.CompilerParams(vmem_limit_bytes=60 * 1024 * 1024)
    out_shape = jax.ShapeDtypeStruct((height, columns_dev), jnp.float32)
    smem = pl.BlockSpec(memory_space=pltpu.SMEM)
    vmem = pl.BlockSpec(memory_space=pltpu.VMEM)
    anywhere = pl.BlockSpec(memory_space=pl.ANY)
    edge_shape = jax.ShapeDtypeStruct((2 * REACH, columns_dev), jnp.float32)
    middle, peak_part, den_part, num_part = pl.pallas_call(
        lambda *refs: softmin_middle_kernel(total_y, *refs),
        out_shape=(out_shape, edge_shape, edge_shape, edge_shape),
        in_specs=[smem, vmem, vmem],
        scratch_shapes=scratch,
        compiler_params=params,
    )(mult, fixed_c, moving_c)
    face_shape = jax.ShapeDtypeStruct((SEND_Y, columns_dev), jnp.float32)
    disp_init, disp_head, disp_tail = pl.pallas_call(
        lambda *refs: softmin_edge_kernel(total_y, *refs),
        out_shape=(out_shape, face_shape, face_shape),
        in_specs=[smem] + [anywhere] * 4 + [vmem] * 3 + [anywhere],
        out_specs=(anywhere, vmem, vmem),
        scratch_shapes=scratch
        + [
            pltpu.VMEM((2 * REACH, columns_dev), jnp.float32),
            pltpu.VMEM((CH, 2 * REACH, columns_dev), jnp.bfloat16),
            pltpu.VMEM((CH, 32, columns_dev), jnp.bfloat16),
            pltpu.VMEM((CH, REACH, columns_dev), jnp.bfloat16),
            pltpu.VMEM((CH, REACH, columns_dev), jnp.bfloat16),
            pltpu.SemaphoreType.DMA((8,)),
        ],
        compiler_params=params,
        input_output_aliases={8: 0},
    )(mult, fixed_c, moving_c, top_rows, bottom_rows, peak_part, den_part, num_part, middle)

    ext = exchange_halo(disp_init, disp_head, disp_tail, HALO_Y, HALO_Z, SEND_Y, SEND_Z)
    rows_ext, lanes_ext = ext.shape
    row_global = lax.axis_index("gy") * height - HALO_Y + lax.broadcasted_iota(
        jnp.int32, (rows_ext, lanes_ext), 0
    )
    lane_global = lax.axis_index("gz") * columns_dev - HALO_Z + lax.broadcasted_iota(
        jnp.int32, (rows_ext, lanes_ext), 1
    )
    inside = (
        (row_global >= 0)
        & (row_global < total_y)
        & (lane_global >= 0)
        & (lane_global < columns_dev * lax.axis_size("gz"))
    )
    grid_mask = inside.astype(jnp.float32)
    final_ext = pl.pallas_call(
        adam_kernel,
        out_shape=jax.ShapeDtypeStruct((height, columns_dev), jnp.float32),
        in_specs=[
            pl.BlockSpec(memory_space=pltpu.SMEM),
            pl.BlockSpec(memory_space=pltpu.VMEM),
            pl.BlockSpec(memory_space=pltpu.VMEM),
        ],
        compiler_params=pltpu.CompilerParams(vmem_limit_bytes=32 * 1024 * 1024),
    )(smooth_radii.astype(jnp.int32), ext, grid_mask)
    return (disp_init, final_ext)


def solution(mesh):
    in_specs = (P("gy", "gz"), P("gy", "gz"), P("gy", "gz", None), P("gy", "gz"), P())
    out_specs = (P("gy", "gz"), P("gy", "gz"))
    return jax.shard_map(
        per_device, mesh=mesh, in_specs=in_specs, out_specs=out_specs, check_vma=False
    )
```

```python
import jax
import jax.numpy as jnp
from jax import lax
from jax.experimental import pallas as pl
from jax.experimental.pallas import tpu as pltpu
from jax.sharding import PartitionSpec as P

CH = 16
XS = 8
REACH = 32
RMAX = 4
ITERS = 3
NOFF = 2 * (REACH // 4) + 1


softmin_temp = 2.0
smooth_weight = 2.0
adam_rate = 0.2
beta_first = 0.9
beta_second = 0.999
adam_floor = 0.05


def with_halo(cells, sides, width):
    for axis, dim in sides:
        count = lax.axis_size(axis)
        ends = count - 1
        head = lax.slice_in_dim(cells, 0, width, axis=dim)
        tail = lax.slice_in_dim(cells, cells.shape[dim] - width, cells.shape[dim], axis=dim)
        cells = jnp.concatenate(
            [
                lax.ppermute(tail, axis, [(i, (i + 1) % count) for i in range(ends)]),
                cells,
                lax.ppermute(head, axis, [((i + 1) % count, i) for i in range(ends)]),
            ],
            axis=dim,
        )
    return cells


def box_weights(radius):
    spread = jnp.arange(-RMAX, RMAX + 1)
    inside = jnp.abs(spread) <= radius
    return jnp.where(inside, 1.0, 0.0).astype(jnp.float32) / (2 * radius + 1).astype(jnp.float32)


def smooth_inner(padded, radius, margin):
    weights = box_weights(radius)
    height = padded.shape[0] - 2 * margin
    layers = padded.shape[1] - 2 * margin
    depth_cells = padded.shape[2]
    along_y = jnp.zeros((height, padded.shape[1], depth_cells), jnp.float32)
    for offset in range(-RMAX, RMAX + 1):
        along_y = (
            along_y + weights[RMAX + offset] * padded[margin + offset : margin + offset + height]
        )
    along_z = jnp.zeros((height, layers, depth_cells), jnp.float32)
    for offset in range(-RMAX, RMAX + 1):
        along_z = (
            along_z
            + weights[RMAX + offset] * along_y[:, margin + offset : margin + offset + layers]
        )
    x_padded = jnp.pad(along_z, ((0, 0), (0, 0), (RMAX, RMAX)))
    along_x = jnp.zeros((height, layers, depth_cells), jnp.float32)
    for offset in range(-RMAX, RMAX + 1):
        along_x = (
            along_x
            + weights[RMAX + offset] * x_padded[:, :, RMAX + offset : RMAX + offset + depth_cells]
        )
    return along_x


def adam_update(field, target_field, smoothed, first_moment, second_moment, iteration):
    gradient = field - target_field + smooth_weight * (field - smoothed)
    first_moment = beta_first * first_moment + (1.0 - beta_first) * gradient
    second_moment = beta_second * second_moment + (1.0 - beta_second) * gradient * gradient
    first_hat = first_moment / (1.0 - beta_first ** (iteration + 1))
    second_hat = second_moment / (1.0 - beta_second ** (iteration + 1))
    field = field - adam_rate * first_hat / (jnp.sqrt(second_hat) + adam_floor)
    return (field, first_moment, second_moment)


HALO_Y = 8
HALO_Z = 8 * XS
SEND_Y = 8
SEND_Z = 8 * XS


def exchange_halo(cells, head, tail, wy, wz, send_y, send_z):
    ny = lax.axis_size("gy")
    nz = lax.axis_size("gz")
    top = lax.ppermute(tail, "gy", [(i, i + 1) for i in range(ny - 1)])
    bottom = lax.ppermute(head, "gy", [(i + 1, i) for i in range(ny - 1)])
    cells = jnp.concatenate([top, cells, bottom], axis=0)
    left = lax.ppermute(cells[:, -send_z:], "gz", [(i, i + 1) for i in range(nz - 1)])
    right = lax.ppermute(cells[:, :send_z], "gz", [(i + 1, i) for i in range(nz - 1)])
    cells = jnp.concatenate([left, cells, right], axis=1)
    return jnp.pad(cells, ((wy - send_y, wy - send_y), (wz - send_z, wz - send_z)))


def shifted(a, offset, axis):
    if offset == 0:
        return a
    return pltpu.roll(a, (-offset) % a.shape[axis], axis)


def window_sum(u, radius, axis, step):
    if radius == 1:
        return u + shifted(u, -step, axis) + shifted(u, step, axis)
    pairs = u + shifted(u, step, axis)
    quads = pairs + shifted(pairs, 2 * step, axis)
    if radius == 2:
        return shifted(quads, -2 * step, axis) + shifted(u, 2 * step, axis)
    if radius == 3:
        return (
            shifted(quads, -3 * step, axis)
            + shifted(pairs, step, axis)
            + shifted(u, 3 * step, axis)
        )
    return shifted(quads, -4 * step, axis) + quads + shifted(u, 4 * step, axis)


def box_smooth(u, radius, lane_x):
    scale = 1.0 / float(2 * radius + 1)
    along_y = window_sum(u, radius, 0, 1) * scale
    along_z = window_sum(along_y, radius, 1, XS) * scale
    along_x = along_z
    for o in range(1, radius + 1):
        along_x = (
            along_x
            + jnp.where(lane_x >= o, shifted(along_z, -o, 1), 0.0)
            + jnp.where(lane_x < XS - o, shifted(along_z, o, 1), 0.0)
        )
    return along_x * scale


def adam_kernel(radii_ref, d_ref, mask_ref, o_ref):
    target = d_ref[...]
    inside = mask_ref[...] > 0.0
    lane_x = lax.broadcasted_iota(jnp.int32, target.shape, 1) % XS
    field = jnp.where(inside, target, 0.0)
    first_moment = jnp.zeros_like(target)
    second_moment = jnp.zeros_like(target)
    for iteration in range(ITERS):
        radius = radii_ref[iteration]
        smoothed = lax.switch(
            jnp.clip(radius - 1, 0, RMAX - 1),
            [lambda u, r=r: box_smooth(u, r, lane_x) for r in range(1, RMAX + 1)],
            field,
        )
        field, first_moment, second_moment = adam_update(
            field, target, smoothed, first_moment, second_moment, iteration
        )
        field = jnp.where(inside, field, 0.0)
    height = o_ref.shape[0]
    width = o_ref.shape[1]
    o_ref[...] = field[HALO_Y : HALO_Y + height, HALO_Z : HALO_Z + width]


def transpose_kernel(x_ref, *refs):
    o_ref, s_ref = refs[0], refs[-1]
    chunk = 128 * CH
    for j in range(x_ref.shape[1] // chunk):
        s_ref[...] = x_ref[:, pl.ds(chunk * j, chunk)].astype(jnp.float32).T
        for c in range(CH):
            cols = s_ref[pl.ds(c, 128, stride=CH), :]
            o_ref[c, :, pl.ds(128 * j, 128)] = cols.T.astype(o_ref.dtype)
    if len(refs) == 4:
        rows = x_ref.shape[0]
        refs[1][...] = o_ref[:, pl.ds(0, REACH), :]
        refs[2][...] = o_ref[:, pl.ds(rows - REACH, REACH), :]


def channel_major(x, with_ends=False):
    rows, lanes = x.shape
    whole = jax.ShapeDtypeStruct((CH, rows, lanes // CH), x.dtype)
    ends = jax.ShapeDtypeStruct((CH, REACH, lanes // CH), x.dtype)
    return pl.pallas_call(
        transpose_kernel,
        out_shape=(whole, ends, ends) if with_ends else whole,
        scratch_shapes=[pltpu.VMEM((128 * CH, rows), jnp.float32)],
    )(x)


def block_counts(n_ref, t, offsets):
    upper = lax.broadcasted_iota(jnp.int32, (8, 128), 0) < 4
    return [jnp.where(upper, n_ref[2 * t, o], n_ref[2 * t + 1, o]) for o in offsets]


def softmin_tiles(total_y, f_ref, m0_ref, m4_ref, n_ref, o_ref, first, last):
    lanes_total = f_ref.shape[2]

    def body(t, carry):
        r0 = pl.multiple_of(t * 8, 8)
        counts = block_counts(n_ref, t, range(NOFF))
        for j in range(lanes_total // 128):
            peak, den, num = offset_partial(
                total_y, f_ref, m0_ref, m4_ref, counts, r0, range(NOFF), pl.ds(128 * j, 128)
            )
            o_ref[pl.ds(r0, 8), pl.ds(128 * j, 128)] = num / den
        return carry

    lax.fori_loop(first, last, body, 0)


def offset_partial(total_y, f_ref, m0_ref, m4_ref, counts, r0, offsets, lanes):
    fixed = [f_ref[c, pl.ds(r0, 8), lanes] for c in range(CH)]
    scores = []
    for o, n_o in zip(offsets, counts):
        shift = 4 * o
        if shift % 8 == 0:
            src, base = m0_ref, shift
        else:
            src, base = m4_ref, shift - 4
        acc = None
        for c in range(CH):
            d = fixed[c] - src[c, pl.ds(r0 + base, 8), lanes]
            acc = d * d if acc is None else acc + d * d
        scores.append(jnp.where(n_o > 0.0, -acc / softmin_temp, -jnp.inf))
    peak = scores[0]
    for s in scores[1:]:
        peak = jnp.maximum(peak, s)
    base_score = jnp.where(peak == -jnp.inf, 0.0, peak)
    den = None
    num = None
    for o, s, n_o in zip(offsets, scores, counts):
        w = n_o * jnp.exp(s - base_score)
        shift_norm = 2.0 * float(4 * o - REACH) / total_y
        den = w if den is None else den + w
        num = w * shift_norm if num is None else num + w * shift_norm
    return peak, den, num


def edge_tiles(height):
    reach_tiles = REACH // 8
    return list(range(reach_tiles)) + list(range(height // 8 - reach_tiles, height // 8))


def edge_row(t, height):
    return 8 * t if 8 * t < REACH else 8 * t - (height - 2 * REACH)


def halo_offsets(t, height):
    return [o for o in range(NOFF) if 8 * t + 4 * o < REACH or 8 * t + 4 * o + 8 > height + REACH]


def softmin_middle_kernel(total_y, n_ref, ft_ref, mt_ref, o_ref, pk_ref, dn_ref, nm_ref, f_ref, m0_ref, m4_ref):
    height = ft_ref.shape[1]
    lanes_total = ft_ref.shape[2]
    rows = height + 2 * REACH

    def build(c, carry):
        f_ref[c] = ft_ref[c].astype(jnp.float32)
        m0_ref[c, pl.ds(REACH, height), :] = mt_ref[c].astype(jnp.float32)
        m0_ref[c, pl.ds(0, REACH), :] = jnp.zeros((REACH, lanes_total), jnp.float32)
        m0_ref[c, pl.ds(REACH + height, REACH), :] = jnp.zeros((REACH, lanes_total), jnp.float32)
        m4_ref[c, pl.ds(0, rows - 8), :] = m0_ref[c, pl.ds(4, rows - 8), :]
        m4_ref[c, pl.ds(rows - 8, 8), :] = jnp.zeros((8, lanes_total), jnp.float32)
        return carry

    lax.fori_loop(0, CH, build, 0)
    tiles = height // 8
    softmin_tiles(total_y, f_ref, m0_ref, m4_ref, n_ref, o_ref, REACH // 8, tiles - REACH // 8)
    for t in edge_tiles(height):
        beyond = halo_offsets(t, height)
        inner = [o for o in range(NOFF) if o not in beyond]
        row = edge_row(t, height)

        def part(j, carry, t=t, inner=inner, row=row):
            lanes = pl.ds(pl.multiple_of(j * 128, 128), 128)
            counts = block_counts(n_ref, t, inner)
            peak, den, num = offset_partial(
                total_y, f_ref, m0_ref, m4_ref, counts, 8 * t, inner, lanes
            )
            pk_ref[pl.ds(row, 8), lanes] = peak
            dn_ref[pl.ds(row, 8), lanes] = den
            nm_ref[pl.ds(row, 8), lanes] = num
            return carry

        lax.fori_loop(0, lanes_total // 128, part, 0)


def softmin_edge_kernel(
    total_y, n_ref, fc_hbm, mc_hbm, top_hbm, bot_hbm, pk_ref, dn_ref, nm_ref, _,
    o_hbm, head_ref, tail_ref, f_ref, m0_ref, m4_ref, res_ref, fe_ref, me_ref, top_ref, bot_ref, sem,
):
    height = o_hbm.shape[0]
    lanes_total = fe_ref.shape[2]
    rows = height + 2 * REACH
    span = REACH + 16
    halo_copies = [
        pltpu.make_async_copy(top_hbm, top_ref, sem.at[6]),
        pltpu.make_async_copy(bot_hbm, bot_ref, sem.at[7]),
    ]
    fixed_copies = [
        pltpu.make_async_copy(
            fc_hbm.at[:, pl.ds(0, REACH), :], fe_ref.at[:, pl.ds(0, REACH), :], sem.at[2]
        ),
        pltpu.make_async_copy(
            fc_hbm.at[:, pl.ds(height - REACH, REACH), :], fe_ref.at[:, pl.ds(REACH, REACH), :], sem.at[3]
        ),
    ]
    moving_copies = [
        pltpu.make_async_copy(mc_hbm.at[:, pl.ds(0, 16), :], me_ref.at[:, pl.ds(0, 16), :], sem.at[4]),
        pltpu.make_async_copy(
            mc_hbm.at[:, pl.ds(height - 16, 16), :], me_ref.at[:, pl.ds(16, 16), :], sem.at[5]
        ),
    ]
    for cp in halo_copies + fixed_copies + moving_copies:
        cp.start()
    for cp in halo_copies:
        cp.wait()

    def build_halo(c, carry):
        m0_ref[c, pl.ds(0, REACH), :] = top_ref[c].astype(jnp.float32)
        m0_ref[c, pl.ds(rows - REACH, REACH), :] = bot_ref[c].astype(jnp.float32)
        return carry

    lax.fori_loop(0, CH, build_halo, 0)
    for cp in fixed_copies:
        cp.wait()

    def build_fixed(c, carry):
        f_ref[c, pl.ds(0, REACH), :] = fe_ref[c, pl.ds(0, REACH), :].astype(jnp.float32)
        f_ref[c, pl.ds(height - REACH, REACH), :] = fe_ref[c, pl.ds(REACH, REACH), :].astype(
            jnp.float32
        )
        return carry

    lax.fori_loop(0, CH, build_fixed, 0)
    for cp in moving_copies:
        cp.wait()

    def build(c, carry):
        m0_ref[c, pl.ds(REACH, 16), :] = me_ref[c, pl.ds(0, 16), :].astype(jnp.float32)
        m0_ref[c, pl.ds(rows - span, 16), :] = me_ref[c, pl.ds(16, 16), :].astype(jnp.float32)
        m4_ref[c, pl.ds(0, span - 8), :] = m0_ref[c, pl.ds(4, span - 8), :]
        m4_ref[c, pl.ds(rows - span, span - 8), :] = m0_ref[c, pl.ds(rows - span + 4, span - 8), :]
        m4_ref[c, pl.ds(rows - 8, 8), :] = jnp.zeros((8, lanes_total), jnp.float32)
        return carry

    lax.fori_loop(0, CH, build, 0)
    for t in edge_tiles(height):
        beyond = halo_offsets(t, height)
        row = edge_row(t, height)

        def part(j, carry, t=t, beyond=beyond, row=row):
            lanes = pl.ds(pl.multiple_of(j * 128, 128), 128)
            rows_t = pl.ds(row, 8)
            counts = block_counts(n_ref, t, beyond)
            peak, den, num = offset_partial(
                total_y, f_ref, m0_ref, m4_ref, counts, 8 * t, beyond, lanes
            )
            peak_in = pk_ref[rows_t, lanes]
            top_score = jnp.maximum(peak, peak_in)
            scale = jnp.exp(peak - top_score)
            scale_in = jnp.exp(peak_in - top_score)
            den = den * scale + dn_ref[rows_t, lanes] * scale_in
            num = num * scale + nm_ref[rows_t, lanes] * scale_in
            res_ref[rows_t, lanes] = num / den
            return carry

        lax.fori_loop(0, lanes_total // 128, part, 0)
    head = pltpu.make_async_copy(
        res_ref.at[pl.ds(0, REACH)], o_hbm.at[pl.ds(0, REACH)], sem.at[0]
    )
    tail = pltpu.make_async_copy(
        res_ref.at[pl.ds(REACH, REACH)], o_hbm.at[pl.ds(height - REACH, REACH)], sem.at[1]
    )
    head.start()
    tail.start()
    head_ref[...] = res_ref[pl.ds(0, head_ref.shape[0]), :]
    tail_ref[...] = res_ref[pl.ds(2 * REACH - tail_ref.shape[0], tail_ref.shape[0]), :]
    head.wait()
    tail.wait()


def per_device(fixed_features, moving_features, cand_offsets, cand_lengths, smooth_radii):
    height = fixed_features.shape[0]
    columns_dev = fixed_features.shape[1] // CH
    blocks = height // 4
    total_y = height * lax.axis_size("gy")
    shifts = cand_offsets[:, 0, :]
    counts = cand_lengths[:, 0]
    live = jnp.arange(shifts.shape[1], dtype=jnp.int32)[None, :] < counts[:, None]
    offset_values = 4 * jnp.arange(NOFF, dtype=jnp.int32) - REACH
    hits = (shifts[:, :, None] == offset_values[None, None, :]) & live[:, :, None]
    mult = jnp.sum(hits.astype(jnp.float32), axis=1)

    gy_count = lax.axis_size("gy")
    fixed_c = channel_major(fixed_features)
    moving_c, moving_head, moving_tail = channel_major(moving_features, with_ends=True)
    top_rows = lax.ppermute(moving_tail, "gy", [(i, i + 1) for i in range(gy_count - 1)])
    bottom_rows = lax.ppermute(moving_head, "gy", [(i + 1, i) for i in range(gy_count - 1)])

    rows = height + 2 * REACH
    tiles = height // 8
    reach_tiles = REACH // 8
    scratch = [
        pltpu.VMEM((CH, height, columns_dev), jnp.float32),
        pltpu.VMEM((CH, rows, columns_dev), jnp.float32),
        pltpu.VMEM((CH, rows, columns_dev), jnp.float32),
    ]
    params = pltpu.CompilerParams(vmem_limit_bytes=60 * 1024 * 1024)
    out_shape = jax.ShapeDtypeStruct((height, columns_dev), jnp.float32)
    smem = pl.BlockSpec(memory_space=pltpu.SMEM)
    vmem = pl.BlockSpec(memory_space=pltpu.VMEM)
    anywhere = pl.BlockSpec(memory_space=pl.ANY)
    edge_shape = jax.ShapeDtypeStruct((2 * REACH, columns_dev), jnp.float32)
    middle, peak_part, den_part, num_part = pl.pallas_call(
        lambda *refs: softmin_middle_kernel(total_y, *refs),
        out_shape=(out_shape, edge_shape, edge_shape, edge_shape),
        in_specs=[smem, vmem, vmem],
        scratch_shapes=scratch,
        compiler_params=params,
    )(mult, fixed_c, moving_c)
    face_shape = jax.ShapeDtypeStruct((SEND_Y, columns_dev), jnp.float32)
    disp_init, disp_head, disp_tail = pl.pallas_call(
        lambda *refs: softmin_edge_kernel(total_y, *refs),
        out_shape=(out_shape, face_shape, face_shape),
        in_specs=[smem] + [anywhere] * 4 + [vmem] * 3 + [anywhere],
        out_specs=(anywhere, vmem, vmem),
        scratch_shapes=scratch
        + [
            pltpu.VMEM((2 * REACH, columns_dev), jnp.float32),
            pltpu.VMEM((CH, 2 * REACH, columns_dev), jnp.bfloat16),
            pltpu.VMEM((CH, 32, columns_dev), jnp.bfloat16),
            pltpu.VMEM((CH, REACH, columns_dev), jnp.bfloat16),
            pltpu.VMEM((CH, REACH, columns_dev), jnp.bfloat16),
            pltpu.SemaphoreType.DMA((8,)),
        ],
        compiler_params=params,
        input_output_aliases={8: 0},
    )(mult, fixed_c, moving_c, top_rows, bottom_rows, peak_part, den_part, num_part, middle)

    ext = exchange_halo(disp_init, disp_head, disp_tail, HALO_Y, HALO_Z, SEND_Y, SEND_Z)
    rows_ext, lanes_ext = ext.shape
    row_global = lax.axis_index("gy") * height - HALO_Y + lax.broadcasted_iota(
        jnp.int32, (rows_ext, lanes_ext), 0
    )
    lane_global = lax.axis_index("gz") * columns_dev - HALO_Z + lax.broadcasted_iota(
        jnp.int32, (rows_ext, lanes_ext), 1
    )
    inside = (
        (row_global >= 0)
        & (row_global < total_y)
        & (lane_global >= 0)
        & (lane_global < columns_dev * lax.axis_size("gz"))
    )
    grid_mask = inside.astype(jnp.float32)
    final_ext = pl.pallas_call(
        adam_kernel,
        out_shape=jax.ShapeDtypeStruct((height, columns_dev), jnp.float32),
        in_specs=[
            pl.BlockSpec(memory_space=pltpu.SMEM),
            pl.BlockSpec(memory_space=pltpu.VMEM),
            pl.BlockSpec(memory_space=pltpu.VMEM),
        ],
        compiler_params=pltpu.CompilerParams(vmem_limit_bytes=32 * 1024 * 1024),
    )(smooth_radii.astype(jnp.int32), ext, grid_mask)
    return (disp_init, final_ext)


def solution(mesh):
    in_specs = (P("gy", "gz"), P("gy", "gz"), P("gy", "gz", None), P("gy", "gz"), P())
    out_specs = (P("gy", "gz"), P("gy", "gz"))
    return jax.shard_map(
        per_device, mesh=mesh, in_specs=in_specs, out_specs=out_specs, check_vma=False
    )
```
